32 devices in a mesh: rows: 8 (over y, x, core), cols: 4 (over z).
Axes of the slice: x: 2, y: 2, z: 4, core: 2. Of those that a mesh axis runs over, the one named last changes fastest.
Arguments:
- fields: bfloat16 [12, 64, 128, 4096], P(None, 'rows', 'cols'), may hold values from -110 to 110
- front_cells: int32 [32, 32, 4], P(('rows', 'cols')), may hold values from -1 to 2047, as said below
Outputs:
- front_tensors: bfloat16 [32, 33, 128], P(('rows', 'cols'))
The draws below stay inside these ranges and needn't reach their ends.
Inputs may be any that keep to these rules, and one draw needn't show every extreme that they name: front_cells[s, d, n] is a cell number of device s's slab or -1 for an empty slot; the live slots of each (s, d) come first; in every draw some owner receives 4 cells from every device; a cell may go to several owners.
All inputs are finite; a program needn't handle non-finite values.
Results may differ from the reference program's by a relative error of at most 0.01.
Values may be sent and summed in bfloat16 or wider, within the bound.
No kernel may reach another device: no remote copies, remote signals or barrier semaphores. Data moves between devices by JAX's collectives and lax.ppermute only.
A program may use at most 192 MiB of HBM per device.

```python
import jax
import jax.numpy as jnp
from jax import lax

F = 12
NZ = 4096
CAP = 4
NX = 64
NY = 128
CELLS_DEV = 2048
DEVICES = 32


def draw_front_cells(key, part):
    count_key = jax.random.fold_in(key, 11)
    owner_key = jax.random.fold_in(key, 12)
    cell_key = jax.random.fold_in(key, 13)
    counts = jax.random.randint(count_key, (DEVICES, DEVICES), 0, CAP + 1)
    busiest = jax.random.randint(owner_key, (), 0, DEVICES)
    owners = jnp.arange(DEVICES)
    counts = jnp.where(owners[None, :] == busiest, CAP, counts)
    cells = jax.random.randint(cell_key, (DEVICES, DEVICES, CAP), 0, CELLS_DEV)
    slots = jnp.arange(CAP)
    return jnp.where(slots[None, None, :] < counts[:, :, None], cells, -1).astype(jnp.int32)


def block_scale(own_key, extent, split, least, high):
    gain = 1.0
    for axis_at, blocks in split:
        steps = jax.random.uniform(jax.random.fold_in(jax.random.fold_in(own_key, 6), axis_at), (blocks,), jnp.float32, least / len(split), high / len(split))
        gain = gain * jnp.repeat(jnp.exp(steps), extent[axis_at] // blocks).reshape((-1,) + (1,) * (len(extent) - 1 - axis_at))
    return gain


def setup_inputs(seed: int = 0) -> dict:
    keys = jax.random.split(jax.random.key(seed), 3)
    fields = jnp.clip(jax.random.uniform(keys[0], (F, NX, NY, NZ), jnp.float32, -110.0, 110.0) * block_scale(keys[0], (F, NX, NY, NZ), ((1, 8), (2, 4)), -0.4, 0.0), -110.0, 110.0).astype(jnp.bfloat16)
    front_cells = draw_front_cells(jax.random.fold_in(keys[2], 71), 0)
    return {"fields": fields, "front_cells": front_cells}


first_tap = -20
last_tap = 27
margin = 64
block_len = 1024
sigma_sq = 256.0 / 12.0
coarse_step = 8.0
model_coeff = 1.0 / 3.0
upper_pairs = ((0, 0), (0, 1), (0, 2), (1, 1), (1, 2), (2, 2))


def tap_weights(offsets):
    every_tap = jnp.arange(first_tap, last_tap + 1).astype(jnp.float32)
    weight_sum = jnp.sum(jnp.exp(-(every_tap - 3.5) * (every_tap - 3.5) / (2.0 * sigma_sq)))
    shifted = offsets.astype(jnp.float32) - 3.5
    inside = (offsets >= first_tap) & (offsets <= last_tap)
    gauss = jnp.where(inside, jnp.exp(-shifted * shifted / (2.0 * sigma_sq)), 0.0) / weight_sum
    slope = -coarse_step * shifted / sigma_sq * gauss
    return gauss.astype(jnp.bfloat16), slope.astype(jnp.bfloat16)


def line_matrices(length):
    fine_pos = jnp.arange(length)[:, None]
    coarse_pos = jnp.arange(length // 8)[None, :]
    offsets = jnp.mod(fine_pos - 8 * coarse_pos, length)
    offsets = jnp.where(offsets >= length // 2, offsets - length, offsets)
    return tap_weights(offsets)


def block_kernel():
    window_pos = jnp.arange(block_len + 2 * margin)[:, None]
    coarse_pos = jnp.arange(block_len // 8)[None, :]
    gauss, slope = tap_weights(window_pos - margin - 8 * coarse_pos)
    return jnp.concatenate([gauss, slope], axis=1)


def model_tensors(coarse):
    values = coarse.astype(jnp.float32)
    points = values.shape[-1]
    values = values.reshape(values.shape[0] // 3, 3, points)
    velocity = values[:3]
    species = values[3:]
    stress = [jnp.sum(velocity[first_comp] * velocity[second_comp], axis=0) for first_comp, second_comp in upper_pairs]
    species_flux = jnp.sum(species[:, None, :, :] * velocity[None, :, :, :], axis=2)
    joined = jnp.concatenate([jnp.stack(stress, axis=0), species_flux.reshape(-1, points)], axis=0)
    return (model_coeff * joined).astype(jnp.bfloat16)


def reference(fields, front_cells):
    kernel = block_kernel().astype(jnp.float32)
    highest = lax.Precision.HIGHEST

    def one_field(single):
        line_rows = single.reshape(NX * NY, NZ).astype(jnp.float32)
        padded = jnp.concatenate([line_rows[:, NZ - margin:], line_rows, line_rows[:, :margin]], axis=1)
        pieces = []
        for position in range(0, NZ, block_len):
            window = padded[:, position:position + block_len + 2 * margin]
            result = jnp.dot(window, kernel, precision=highest, preferred_element_type=jnp.float32)
            pieces.append(result.reshape(NX * NY, 2, block_len // 8))
        joined = jnp.stack(pieces, axis=2).reshape(NX, NY, 2, NZ // 8)
        return joined.astype(jnp.bfloat16)

    z_filtered = lax.map(one_field, fields)
    smooth_x, deriv_x = line_matrices(NX)
    smooth_y, deriv_y = line_matrices(NY)
    smooth_x = smooth_x.astype(jnp.float32)
    deriv_x = deriv_x.astype(jnp.float32)
    smooth_y = smooth_y.astype(jnp.float32)
    deriv_y = deriv_y.astype(jnp.float32)
    zvalue = z_filtered[:, :, :, 0].astype(jnp.float32)
    zslope = z_filtered[:, :, :, 1].astype(jnp.float32)
    value_ax = jnp.einsum("fxyc,xp->fpyc", zvalue, smooth_x, precision=highest)
    value_bx = jnp.einsum("fxyc,xp->fpyc", zvalue, deriv_x, precision=highest)
    slope_ax = jnp.einsum("fxyc,xp->fpyc", zslope, smooth_x, precision=highest)
    grad_x = jnp.einsum("fpyc,yq->fpqc", value_bx, smooth_y, precision=highest)
    grad_y = jnp.einsum("fpyc,yq->fpqc", value_ax, deriv_y, precision=highest)
    grad_z = jnp.einsum("fpyc,yq->fpqc", slope_ax, smooth_y, precision=highest)
    coarse_grads = jnp.stack([grad_x, grad_y, grad_z], axis=1).astype(jnp.bfloat16)
    devices = front_cells.shape[0]
    slots = front_cells.shape[2]
    by_source = coarse_grads.reshape(3 * F, NX // 8, NY // 8, devices, -1)
    by_source = jnp.transpose(by_source, (3, 0, 1, 2, 4)).reshape(devices, 3 * F, -1)

    def pick_cells(source_vals, source_cells):
        flat_cells = source_cells.reshape(-1).astype(jnp.int32)
        clipped = jnp.clip(flat_cells, 0, source_vals.shape[1] - 1)
        taken = jnp.take(source_vals, clipped, axis=1)
        return jnp.where(flat_cells[None, :] >= 0, taken, jnp.zeros_like(taken))

    picked = jax.vmap(pick_cells)(by_source, front_cells)
    gathered = jnp.transpose(picked, (1, 0, 2)).reshape(3 * F, -1)
    tensors = model_tensors(gathered).reshape(-1, devices, devices, slots)
    tensors = jnp.transpose(tensors, (2, 0, 1, 3))
    return tensors.reshape(devices, -1, devices * slots)
```

```python
import numpy as np
import jax
import jax.numpy as jnp
import ml_dtypes
from jax import lax
from jax.sharding import PartitionSpec as P
from jax.experimental import pallas as pl
from jax.experimental.pallas import tpu as pltpu

first_tap = -20
last_tap = 27
sigma_sq = 256.0 / 12.0
coarse_step = 8.0
model_coeff = 1.0 / 3.0
upper_pairs = ((0, 0), (0, 1), (0, 2), (1, 1), (1, 2), (2, 2))
block_len = 1024
halo = 128


def tap_weights(offsets):
    f32 = np.float32
    every_tap = np.arange(first_tap, last_tap + 1).astype(f32)
    weight_sum = np.sum(np.exp(-(every_tap - f32(3.5)) * (every_tap - f32(3.5)) / f32(2.0 * sigma_sq)), dtype=f32)
    shifted = offsets.astype(f32) - f32(3.5)
    inside = (offsets >= first_tap) & (offsets <= last_tap)
    gauss = np.where(inside, np.exp(-shifted * shifted / f32(2.0 * sigma_sq)), f32(0.0)).astype(f32) / weight_sum
    slope = (f32(-coarse_step) * shifted / f32(sigma_sq) * gauss).astype(f32)
    bf = ml_dtypes.bfloat16
    return gauss.astype(bf).astype(f32), slope.astype(bf).astype(f32)


def line_matrices(length):
    fine_pos = np.arange(length)[:, None]
    coarse_pos = np.arange(length // 8)[None, :]
    offsets = np.mod(fine_pos - 8 * coarse_pos, length)
    offsets = np.where(offsets >= length // 2, offsets - length, offsets)
    return tap_weights(offsets)


def z_tables(length):
    coarse = np.arange(length // 8)[None, :]
    main = np.arange(length)[:, None] - 8 * coarse
    prev = np.arange(halo)[:, None] - halo - 8 * coarse
    nxt = np.arange(halo)[:, None] + length - 8 * coarse
    return [tap_weights(o) for o in (main, prev, nxt)]


def filter_kernel(block_count, coarse_block, value_rows, slope_rows):
    def body(x_ref, main_ref, prev_ref, next_ref, wv_ref, ws_ref, o_ref, zv_ref, zs_ref):
        length = x_ref.shape[2]
        blen = length // block_count
        for b in range(block_count):
            main = x_ref[0, :, b * blen:(b + 1) * blen]
            start = (b * blen - halo) % length
            tail = x_ref[0, :, start:start + halo]
            start = ((b + 1) * blen) % length
            head = x_ref[0, :, start:start + halo]
            acc = jnp.dot(main, main_ref[...], preferred_element_type=jnp.float32)
            acc = acc + jnp.dot(tail, prev_ref[...], preferred_element_type=jnp.float32)
            acc = acc + jnp.dot(head, next_ref[...], preferred_element_type=jnp.float32)
            lanes = slice(b * coarse_block, (b + 1) * coarse_block)
            zv_ref[:, lanes] = acc[:, :coarse_block].astype(jnp.bfloat16)
            zs_ref[:, lanes] = acc[:, coarse_block:].astype(jnp.bfloat16)
        zv = zv_ref[...]
        zs = zs_ref[...]
        pv = jnp.dot(wv_ref[0], zv, preferred_element_type=jnp.float32)
        pv = pv + jnp.dot(wv_ref[1], zv, preferred_element_type=jnp.float32)
        ps = jnp.dot(ws_ref[0], zs, preferred_element_type=jnp.float32)
        ps = ps + jnp.dot(ws_ref[1], zs, preferred_element_type=jnp.float32)
        o_ref[0, :value_rows, :] = pv
        o_ref[0, value_rows:, :] = ps

    return body


def split_hi_lo(w):
    hi = w.astype(jnp.bfloat16)
    lo = (w - hi.astype(jnp.float32)).astype(jnp.bfloat16)
    return jnp.stack([hi, lo], axis=0)


def filtered_partials(fields3, value_w, slope_w):
    field_count, rows, length = fields3.shape
    blen = block_len if (length % block_len == 0 and length > block_len) else length
    block_count = length // blen
    coarse_block = blen // 8
    tables = z_tables(blen)
    joined = [np.concatenate([t[0], t[1]], axis=1) for t in tables]
    main, prev, nxt = [jnp.asarray(t, jnp.bfloat16) for t in joined]
    wv = split_hi_lo(value_w)
    ws = split_hi_lo(slope_w)
    value_rows = wv.shape[1]
    slope_rows = ws.shape[1]
    total_rows = value_rows + slope_rows
    coarse = length // 8
    const = lambda f: (0, 0)
    const3 = lambda f: (0, 0, 0)
    return pl.pallas_call(
        filter_kernel(block_count, coarse_block, value_rows, slope_rows),
        out_shape=jax.ShapeDtypeStruct((field_count, total_rows, coarse), jnp.float32),
        grid=(field_count,),
        in_specs=[
            pl.BlockSpec((1, rows, length), lambda f: (f, 0, 0)),
            pl.BlockSpec(main.shape, const),
            pl.BlockSpec(prev.shape, const),
            pl.BlockSpec(nxt.shape, const),
            pl.BlockSpec(wv.shape, const3),
            pl.BlockSpec(ws.shape, const3),
        ],
        out_specs=pl.BlockSpec((1, total_rows, coarse), lambda f: (f, 0, 0)),
        scratch_shapes=[pltpu.VMEM((rows, coarse), jnp.bfloat16), pltpu.VMEM((rows, coarse), jnp.bfloat16)],
    )(fields3, main, prev, nxt, wv, ws)


def model_tensors(coarse):
    values = coarse.astype(jnp.float32)
    points = values.shape[-1]
    values = values.reshape(values.shape[0] // 3, 3, points)
    velocity = values[:3]
    species = values[3:]
    stress = [
        jnp.sum(velocity[first_comp] * velocity[second_comp], axis=0)
        for first_comp, second_comp in upper_pairs
    ]
    species_flux = jnp.sum(species[:, None, :, :] * velocity[None, :, :, :], axis=2)
    joined = jnp.concatenate([jnp.stack(stress, axis=0), species_flux.reshape(-1, points)], axis=0)
    return (model_coeff * joined).astype(jnp.bfloat16)


def window(at, count, coarse):
    reach = (count + 19) // 8 + 4
    if count % 8 or reach >= coarse:
        return 0, coarse
    return at * (count // 8) - 3, reach


def make_shards(row_count, col_count):
    def shards(fields, front_cells):
        field_count, local_x, local_y, z_length = fields.shape
        devices = row_count * col_count
        full_x = local_x * row_count
        full_y = local_y * col_count
        coarse_x = full_x // 8
        coarse_y = full_y // 8
        coarse_z = z_length // 8
        slab = coarse_z // devices
        slots = front_cells.shape[2]
        row = lax.axis_index("rows")
        col = lax.axis_index("cols")
        me = row * col_count + col

        every_cell = lax.all_gather(front_cells, ("rows", "cols"), axis=0, tiled=True)

        smooth_x, deriv_x = line_matrices(full_x)
        smooth_y, deriv_y = line_matrices(full_y)
        x_base, x_count = window(row, local_x, coarse_x)
        y_base, y_count = window(col, local_y, coarse_y)

        def local_rows(table, at, count, base, width, full):
            rows = lax.dynamic_slice_in_dim(jnp.asarray(table), at * count, count)
            picks = (base + jnp.arange(width)) % full
            return jnp.take(rows, picks, axis=1)

        ax = local_rows(smooth_x, row, local_x, x_base, x_count, coarse_x)
        bx = local_rows(deriv_x, row, local_x, x_base, x_count, coarse_x)
        ay = local_rows(smooth_y, col, local_y, y_base, y_count, coarse_y)
        by = local_rows(deriv_y, col, local_y, y_base, y_count, coarse_y)
        group = x_count * y_count
        padded = -(-group // 8) * 8

        def kron(wx, wy):
            joined = (wx[:, None, :, None] * wy[None, :, None, :]).reshape(local_x * local_y, group)
            return jnp.pad(joined, ((0, 0), (0, padded - group))).T

        value_w = jnp.concatenate([kron(bx, ay), kron(ax, by)], axis=0)
        slope_w = kron(ax, ay)
        fields3 = fields.reshape(field_count, local_x * local_y, z_length)
        partials = filtered_partials(fields3, value_w, slope_w)
        partials = partials.reshape(field_count, 3, padded, coarse_z)

        by_owner = jnp.transpose(every_cell, (1, 0, 2))
        holder = lax.broadcasted_iota(jnp.int32, by_owner.shape, 1)
        clipped = jnp.clip(by_owner, 0, coarse_x * coarse_y * slab - 1)
        cell_pq = clipped // slab
        at_z = holder * slab + clipped % slab
        at_x = (cell_pq // coarse_y - x_base) % coarse_x
        at_y = (cell_pq % coarse_y - y_base) % coarse_y
        inside = (at_x < x_count) & (at_y < y_count) & (by_owner >= 0)
        at_group = jnp.where(inside, at_x * y_count + at_y, 0)
        flat = (at_group * coarse_z + at_z).reshape(-1)
        table = jnp.transpose(partials, (2, 3, 0, 1)).reshape(padded * coarse_z, field_count * 3)
        taken = jnp.take(table, flat, axis=0)
        taken = jnp.where(inside.reshape(-1, 1), taken, jnp.zeros_like(taken))
        taken = taken.reshape(devices, -1, field_count * 3)
        arrived = lax.all_to_all(taken, ("rows", "cols"), split_axis=0, concat_axis=0, tiled=True)
        summed = jnp.sum(arrived.reshape(devices, -1, field_count * 3), axis=0).T
        rounded = lax.reduce_precision(summed, exponent_bits=8, mantissa_bits=7)
        mine = lax.dynamic_index_in_dim(by_owner, me, axis=0, keepdims=False).reshape(-1)
        picked = jnp.where(mine[None, :] >= 0, rounded, jnp.zeros_like(rounded))
        return model_tensors(picked)[None]

    return shards


def solution(mesh):
    in_specs = (P(None, "rows", "cols", None), P(("rows", "cols"), None, None))
    out_specs = P(("rows", "cols"), None, None)
    shards = make_shards(mesh.shape["rows"], mesh.shape["cols"])
    return jax.shard_map(shards, mesh=mesh, in_specs=in_specs, out_specs=out_specs, check_vma=False)
```

```python
import numpy as np
import jax
import jax.numpy as jnp
import ml_dtypes
from jax import lax
from jax.sharding import PartitionSpec as P
from jax.experimental import pallas as pl
from jax.experimental.pallas import tpu as pltpu

first_tap = -20
last_tap = 27
sigma_sq = 256.0 / 12.0
coarse_step = 8.0
model_coeff = 1.0 / 3.0
upper_pairs = ((0, 0), (0, 1), (0, 2), (1, 1), (1, 2), (2, 2))
block_len = 1024
halo = 128


def tap_weights(offsets):
    f32 = np.float32
    every_tap = np.arange(first_tap, last_tap + 1).astype(f32)
    weight_sum = np.sum(np.exp(-(every_tap - f32(3.5)) * (every_tap - f32(3.5)) / f32(2.0 * sigma_sq)), dtype=f32)
    shifted = offsets.astype(f32) - f32(3.5)
    inside = (offsets >= first_tap) & (offsets <= last_tap)
    gauss = np.where(inside, np.exp(-shifted * shifted / f32(2.0 * sigma_sq)), f32(0.0)).astype(f32) / weight_sum
    slope = (f32(-coarse_step) * shifted / f32(sigma_sq) * gauss).astype(f32)
    bf = ml_dtypes.bfloat16
    return gauss.astype(bf).astype(f32), slope.astype(bf).astype(f32)


def line_matrices(length):
    fine_pos = np.arange(length)[:, None]
    coarse_pos = np.arange(length // 8)[None, :]
    offsets = np.mod(fine_pos - 8 * coarse_pos, length)
    offsets = np.where(offsets >= length // 2, offsets - length, offsets)
    return tap_weights(offsets)


def z_tables(length):
    coarse = np.arange(length // 8)[None, :]
    main = np.arange(length)[:, None] - 8 * coarse
    prev = np.arange(halo)[:, None] - halo - 8 * coarse
    nxt = np.arange(halo)[:, None] + length - 8 * coarse
    return [tap_weights(o) for o in (main, prev, nxt)]


def filter_kernel(block_count, coarse_block, value_rows, slope_rows):
    def body(x_ref, main_ref, prev_ref, next_ref, wv_ref, ws_ref, o_ref, zv_ref, zs_ref):
        length = x_ref.shape[2]
        blen = length // block_count
        for b in range(block_count):
            main = x_ref[0, :, b * blen:(b + 1) * blen]
            start = (b * blen - halo) % length
            tail = x_ref[0, :, start:start + halo]
            start = ((b + 1) * blen) % length
            head = x_ref[0, :, start:start + halo]
            acc = jnp.dot(main, main_ref[...], preferred_element_type=jnp.float32)
            acc = acc + jnp.dot(tail, prev_ref[...], preferred_element_type=jnp.float32)
            acc = acc + jnp.dot(head, next_ref[...], preferred_element_type=jnp.float32)
            lanes = slice(b * coarse_block, (b + 1) * coarse_block)
            zv_ref[:, lanes] = acc[:, :coarse_block].astype(jnp.bfloat16)
            zs_ref[:, lanes] = acc[:, coarse_block:].astype(jnp.bfloat16)
        zv = zv_ref[...]
        zs = zs_ref[...]
        pv = jnp.dot(wv_ref[0], zv, preferred_element_type=jnp.float32)
        pv = pv + jnp.dot(wv_ref[1], zv, preferred_element_type=jnp.float32)
        ps = jnp.dot(ws_ref[0], zs, preferred_element_type=jnp.float32)
        ps = ps + jnp.dot(ws_ref[1], zs, preferred_element_type=jnp.float32)
        o_ref[0, :value_rows, :] = pv
        o_ref[0, value_rows:, :] = ps

    return body


def split_hi_lo(w):
    hi = w.astype(jnp.bfloat16)
    lo = (w - hi.astype(jnp.float32)).astype(jnp.bfloat16)
    return jnp.stack([hi, lo], axis=0)


def filtered_partials(fields3, value_w, slope_w):
    field_count, rows, length = fields3.shape
    blen = block_len if (length % block_len == 0 and length > block_len) else length
    block_count = length // blen
    coarse_block = blen // 8
    tables = z_tables(blen)
    joined = [np.concatenate([t[0], t[1]], axis=1) for t in tables]
    main, prev, nxt = [jnp.asarray(t, jnp.bfloat16) for t in joined]
    wv = split_hi_lo(value_w)
    ws = split_hi_lo(slope_w)
    value_rows = wv.shape[1]
    slope_rows = ws.shape[1]
    total_rows = value_rows + slope_rows
    coarse = length // 8
    const = lambda f: (0, 0)
    const3 = lambda f: (0, 0, 0)
    return pl.pallas_call(
        filter_kernel(block_count, coarse_block, value_rows, slope_rows),
        out_shape=jax.ShapeDtypeStruct((field_count, total_rows, coarse), jnp.float32),
        grid=(field_count,),
        in_specs=[
            pl.BlockSpec((1, rows, length), lambda f: (f, 0, 0)),
            pl.BlockSpec(main.shape, const),
            pl.BlockSpec(prev.shape, const),
            pl.BlockSpec(nxt.shape, const),
            pl.BlockSpec(wv.shape, const3),
            pl.BlockSpec(ws.shape, const3),
        ],
        out_specs=pl.BlockSpec((1, total_rows, coarse), lambda f: (f, 0, 0)),
        scratch_shapes=[pltpu.VMEM((rows, coarse), jnp.bfloat16), pltpu.VMEM((rows, coarse), jnp.bfloat16)],
    )(fields3, main, prev, nxt, wv, ws)


def model_tensors(coarse):
    values = coarse.astype(jnp.float32)
    points = values.shape[-1]
    values = values.reshape(values.shape[0] // 3, 3, points)
    velocity = values[:3]
    species = values[3:]
    stress = [
        jnp.sum(velocity[first_comp] * velocity[second_comp], axis=0)
        for first_comp, second_comp in upper_pairs
    ]
    species_flux = jnp.sum(species[:, None, :, :] * velocity[None, :, :, :], axis=2)
    joined = jnp.concatenate([jnp.stack(stress, axis=0), species_flux.reshape(-1, points)], axis=0)
    return (model_coeff * joined).astype(jnp.bfloat16)


def window(at, count, coarse):
    reach = (count + 19) // 8 + 4
    if count % 8 or reach >= coarse:
        return 0, coarse
    return at * (count // 8) - 3, reach


def make_shards(row_count, col_count):
    def shards(fields, front_cells):
        field_count, local_x, local_y, z_length = fields.shape
        devices = row_count * col_count
        full_x = local_x * row_count
        full_y = local_y * col_count
        coarse_x = full_x // 8
        coarse_y = full_y // 8
        coarse_z = z_length // 8
        slab = coarse_z // devices
        slots = front_cells.shape[2]
        row = lax.axis_index("rows")
        col = lax.axis_index("cols")
        me = row * col_count + col

        copies = jnp.broadcast_to(front_cells, (devices,) + front_cells.shape[1:])
        every_cell = lax.all_to_all(copies, ("rows", "cols"), split_axis=0, concat_axis=0, tiled=True)

        smooth_x, deriv_x = line_matrices(full_x)
        smooth_y, deriv_y = line_matrices(full_y)
        x_base, x_count = window(row, local_x, coarse_x)
        y_base, y_count = window(col, local_y, coarse_y)

        def local_rows(table, at, count, base, width, full):
            rows = lax.dynamic_slice_in_dim(jnp.asarray(table), at * count, count)
            picks = (base + jnp.arange(width)) % full
            return jnp.take(rows, picks, axis=1)

        ax = local_rows(smooth_x, row, local_x, x_base, x_count, coarse_x)
        bx = local_rows(deriv_x, row, local_x, x_base, x_count, coarse_x)
        ay = local_rows(smooth_y, col, local_y, y_base, y_count, coarse_y)
        by = local_rows(deriv_y, col, local_y, y_base, y_count, coarse_y)
        group = x_count * y_count
        padded = -(-group // 8) * 8

        def kron(wx, wy):
            joined = (wx[:, None, :, None] * wy[None, :, None, :]).reshape(local_x * local_y, group)
            return jnp.pad(joined, ((0, 0), (0, padded - group))).T

        value_w = jnp.concatenate([kron(bx, ay), kron(ax, by)], axis=0)
        slope_w = kron(ax, ay)
        fields3 = fields.reshape(field_count, local_x * local_y, z_length)
        partials = filtered_partials(fields3, value_w, slope_w)
        partials = partials.reshape(field_count, 3, padded, coarse_z)

        by_owner = jnp.transpose(every_cell, (1, 0, 2))
        holder = lax.broadcasted_iota(jnp.int32, by_owner.shape, 1)
        clipped = jnp.clip(by_owner, 0, coarse_x * coarse_y * slab - 1)
        cell_pq = clipped // slab
        at_z = holder * slab + clipped % slab
        at_x = (cell_pq // coarse_y - x_base) % coarse_x
        at_y = (cell_pq % coarse_y - y_base) % coarse_y
        inside = (at_x < x_count) & (at_y < y_count) & (by_owner >= 0)
        at_group = jnp.where(inside, at_x * y_count + at_y, 0)
        flat = (at_group * coarse_z + at_z).reshape(-1)
        table = jnp.transpose(partials, (2, 3, 0, 1)).reshape(padded * coarse_z, field_count * 3)
        taken = jnp.take(table, flat, axis=0)
        taken = jnp.where(inside.reshape(-1, 1), taken, jnp.zeros_like(taken))
        taken = taken.reshape(devices, -1, field_count * 3)
        arrived = lax.all_to_all(taken, ("rows", "cols"), split_axis=0, concat_axis=0, tiled=True)
        summed = jnp.sum(arrived.reshape(devices, -1, field_count * 3), axis=0).T
        rounded = lax.reduce_precision(summed, exponent_bits=8, mantissa_bits=7)
        mine = lax.dynamic_index_in_dim(by_owner, me, axis=0, keepdims=False).reshape(-1)
        picked = jnp.where(mine[None, :] >= 0, rounded, jnp.zeros_like(rounded))
        return model_tensors(picked)[None]

    return shards


def solution(mesh):
    in_specs = (P(None, "rows", "cols", None), P(("rows", "cols"), None, None))
    out_specs = P(("rows", "cols"), None, None)
    shards = make_shards(mesh.shape["rows"], mesh.shape["cols"])
    return jax.shard_map(shards, mesh=mesh, in_specs=in_specs, out_specs=out_specs, check_vma=False)
```

```python
import numpy as np
import jax
import jax.numpy as jnp
import ml_dtypes
from jax import lax
from jax.sharding import PartitionSpec as P
from jax.experimental import pallas as pl
from jax.experimental.pallas import tpu as pltpu

first_tap = -20
last_tap = 27
sigma_sq = 256.0 / 12.0
coarse_step = 8.0
model_coeff = 1.0 / 3.0
upper_pairs = ((0, 0), (0, 1), (0, 2), (1, 1), (1, 2), (2, 2))
block_len = 1024
halo = 128


def tap_weights(offsets):
    f32 = np.float32
    every_tap = np.arange(first_tap, last_tap + 1).astype(f32)
    weight_sum = np.sum(np.exp(-(every_tap - f32(3.5)) * (every_tap - f32(3.5)) / f32(2.0 * sigma_sq)), dtype=f32)
    shifted = offsets.astype(f32) - f32(3.5)
    inside = (offsets >= first_tap) & (offsets <= last_tap)
    gauss = np.where(inside, np.exp(-shifted * shifted / f32(2.0 * sigma_sq)), f32(0.0)).astype(f32) / weight_sum
    slope = (f32(-coarse_step) * shifted / f32(sigma_sq) * gauss).astype(f32)
    bf = ml_dtypes.bfloat16
    return gauss.astype(bf).astype(f32), slope.astype(bf).astype(f32)


def line_matrices(length):
    fine_pos = np.arange(length)[:, None]
    coarse_pos = np.arange(length // 8)[None, :]
    offsets = np.mod(fine_pos - 8 * coarse_pos, length)
    offsets = np.where(offsets >= length // 2, offsets - length, offsets)
    return tap_weights(offsets)


def z_tables(length):
    coarse = np.arange(length // 8)[None, :]
    main = np.arange(length)[:, None] - 8 * coarse
    prev = np.arange(halo)[:, None] - halo - 8 * coarse
    nxt = np.arange(halo)[:, None] + length - 8 * coarse
    return [tap_weights(o) for o in (main, prev, nxt)]


def filter_kernel(block_count, coarse_block, value_rows, slope_rows):
    def body(x_ref, main_ref, prev_ref, next_ref, wv_ref, ws_ref, o_ref, zv_ref, zs_ref):
        length = x_ref.shape[2]
        blen = length // block_count
        for b in range(block_count):
            main = x_ref[0, :, b * blen:(b + 1) * blen]
            start = (b * blen - halo) % length
            tail = x_ref[0, :, start:start + halo]
            start = ((b + 1) * blen) % length
            head = x_ref[0, :, start:start + halo]
            acc = jnp.dot(main, main_ref[...], preferred_element_type=jnp.float32)
            acc = acc + jnp.dot(tail, prev_ref[...], preferred_element_type=jnp.float32)
            acc = acc + jnp.dot(head, next_ref[...], preferred_element_type=jnp.float32)
            lanes = slice(b * coarse_block, (b + 1) * coarse_block)
            zv_ref[:, lanes] = acc[:, :coarse_block].astype(jnp.bfloat16)
            zs_ref[:, lanes] = acc[:, coarse_block:].astype(jnp.bfloat16)
        zv = zv_ref[...]
        zs = zs_ref[...]
        pv = jnp.dot(wv_ref[0], zv, preferred_element_type=jnp.float32)
        pv = pv + jnp.dot(wv_ref[1], zv, preferred_element_type=jnp.float32)
        ps = jnp.dot(ws_ref[0], zs, preferred_element_type=jnp.float32)
        ps = ps + jnp.dot(ws_ref[1], zs, preferred_element_type=jnp.float32)
        o_ref[0, :value_rows, :] = pv
        o_ref[0, value_rows:, :] = ps

    return body


def split_hi_lo(w):
    hi = w.astype(jnp.bfloat16)
    lo = (w - hi.astype(jnp.float32)).astype(jnp.bfloat16)
    return jnp.stack([hi, lo], axis=0)


def filtered_partials(fields3, value_w, slope_w):
    field_count, rows, length = fields3.shape
    blen = block_len if (length % block_len == 0 and length > block_len) else length
    block_count = length // blen
    coarse_block = blen // 8
    tables = z_tables(blen)
    joined = [np.concatenate([t[0], t[1]], axis=1) for t in tables]
    main, prev, nxt = [jnp.asarray(t, jnp.bfloat16) for t in joined]
    wv = split_hi_lo(value_w)
    ws = split_hi_lo(slope_w)
    value_rows = wv.shape[1]
    slope_rows = ws.shape[1]
    total_rows = value_rows + slope_rows
    coarse = length // 8
    const = lambda f: (0, 0)
    const3 = lambda f: (0, 0, 0)
    return pl.pallas_call(
        filter_kernel(block_count, coarse_block, value_rows, slope_rows),
        out_shape=jax.ShapeDtypeStruct((field_count, total_rows, coarse), jnp.float32),
        grid=(field_count,),
        in_specs=[
            pl.BlockSpec((1, rows, length), lambda f: (f, 0, 0)),
            pl.BlockSpec(main.shape, const),
            pl.BlockSpec(prev.shape, const),
            pl.BlockSpec(nxt.shape, const),
            pl.BlockSpec(wv.shape, const3),
            pl.BlockSpec(ws.shape, const3),
        ],
        out_specs=pl.BlockSpec((1, total_rows, coarse), lambda f: (f, 0, 0)),
        scratch_shapes=[pltpu.VMEM((rows, coarse), jnp.bfloat16), pltpu.VMEM((rows, coarse), jnp.bfloat16)],
    )(fields3, main, prev, nxt, wv, ws)


def model_tensors(coarse):
    values = coarse.astype(jnp.float32)
    points = values.shape[-1]
    values = values.reshape(values.shape[0] // 3, 3, points)
    velocity = values[:3]
    species = values[3:]
    stress = [
        jnp.sum(velocity[first_comp] * velocity[second_comp], axis=0)
        for first_comp, second_comp in upper_pairs
    ]
    species_flux = jnp.sum(species[:, None, :, :] * velocity[None, :, :, :], axis=2)
    joined = jnp.concatenate([jnp.stack(stress, axis=0), species_flux.reshape(-1, points)], axis=0)
    return (model_coeff * joined).astype(jnp.bfloat16)


def window(at, count, coarse):
    reach = (count + 19) // 8 + 4
    if count % 8 or reach >= coarse:
        return 0, coarse
    return at * (count // 8) - 3, reach


def make_shards(row_count, col_count):
    def shards(fields, front_cells):
        field_count, local_x, local_y, z_length = fields.shape
        devices = row_count * col_count
        full_x = local_x * row_count
        full_y = local_y * col_count
        coarse_x = full_x // 8
        coarse_y = full_y // 8
        coarse_z = z_length // 8
        slab = coarse_z // devices
        slots = front_cells.shape[2]
        row = lax.axis_index("rows")
        col = lax.axis_index("cols")
        me = row * col_count + col

        copies = jnp.broadcast_to(front_cells, (devices,) + front_cells.shape[1:])
        every_cell = lax.all_to_all(copies, ("rows", "cols"), split_axis=0, concat_axis=0, tiled=True)

        smooth_x, deriv_x = line_matrices(full_x)
        smooth_y, deriv_y = line_matrices(full_y)
        x_base, x_count = window(row, local_x, coarse_x)
        y_base, y_count = window(col, local_y, coarse_y)

        def local_rows(table, at, count, base, width, full):
            rows = lax.dynamic_slice_in_dim(jnp.asarray(table), at * count, count)
            picks = (base + jnp.arange(width)) % full
            return jnp.take(rows, picks, axis=1)

        ax = local_rows(smooth_x, row, local_x, x_base, x_count, coarse_x)
        bx = local_rows(deriv_x, row, local_x, x_base, x_count, coarse_x)
        ay = local_rows(smooth_y, col, local_y, y_base, y_count, coarse_y)
        by = local_rows(deriv_y, col, local_y, y_base, y_count, coarse_y)
        group = x_count * y_count
        padded = -(-group // 8) * 8

        def kron(wx, wy):
            joined = (wx[:, None, :, None] * wy[None, :, None, :]).reshape(local_x * local_y, group)
            return jnp.pad(joined, ((0, 0), (0, padded - group))).T

        value_w = jnp.concatenate([kron(bx, ay), kron(ax, by)], axis=0)
        slope_w = kron(ax, ay)
        fields3 = fields.reshape(field_count, local_x * local_y, z_length)
        partials = filtered_partials(fields3, value_w, slope_w)
        partials = partials.reshape(field_count, 3, padded, coarse_z)

        by_owner = jnp.transpose(every_cell, (1, 0, 2))
        holder = lax.broadcasted_iota(jnp.int32, by_owner.shape, 1)
        clipped = jnp.clip(by_owner, 0, coarse_x * coarse_y * slab - 1)
        cell_pq = clipped // slab
        at_z = holder * slab + clipped % slab
        at_x = (cell_pq // coarse_y - x_base) % coarse_x
        at_y = (cell_pq % coarse_y - y_base) % coarse_y
        inside = (at_x < x_count) & (at_y < y_count) & (by_owner >= 0)
        at_group = jnp.where(inside, at_x * y_count + at_y, 0)
        flat = (at_group * coarse_z + at_z).reshape(-1)
        table = partials.reshape(field_count * 3, padded * coarse_z)
        taken = jnp.take(table, flat, axis=1).T
        taken = jnp.where(inside.reshape(-1, 1), taken, jnp.zeros_like(taken))
        taken = taken.reshape(devices, -1, field_count * 3)
        arrived = lax.all_to_all(taken, ("rows", "cols"), split_axis=0, concat_axis=0, tiled=True)
        summed = jnp.sum(arrived.reshape(devices, -1, field_count * 3), axis=0).T
        rounded = lax.reduce_precision(summed, exponent_bits=8, mantissa_bits=7)
        mine = lax.dynamic_index_in_dim(by_owner, me, axis=0, keepdims=False).reshape(-1)
        picked = jnp.where(mine[None, :] >= 0, rounded, jnp.zeros_like(rounded))
        return model_tensors(picked)[None]

    return shards


def solution(mesh):
    in_specs = (P(None, "rows", "cols", None), P(("rows", "cols"), None, None))
    out_specs = P(("rows", "cols"), None, None)
    shards = make_shards(mesh.shape["rows"], mesh.shape["cols"])
    return jax.shard_map(shards, mesh=mesh, in_specs=in_specs, out_specs=out_specs, check_vma=False)
```

```python
import numpy as np
import jax
import jax.numpy as jnp
import ml_dtypes
from jax import lax
from jax.sharding import PartitionSpec as P
from jax.experimental import pallas as pl
from jax.experimental.pallas import tpu as pltpu

first_tap = -20
last_tap = 27
sigma_sq = 256.0 / 12.0
coarse_step = 8.0
model_coeff = 1.0 / 3.0
upper_pairs = ((0, 0), (0, 1), (0, 2), (1, 1), (1, 2), (2, 2))
block_len = 1024
halo = 128


def tap_weights(offsets):
    f32 = np.float32
    every_tap = np.arange(first_tap, last_tap + 1).astype(f32)
    weight_sum = np.sum(np.exp(-(every_tap - f32(3.5)) * (every_tap - f32(3.5)) / f32(2.0 * sigma_sq)), dtype=f32)
    shifted = offsets.astype(f32) - f32(3.5)
    inside = (offsets >= first_tap) & (offsets <= last_tap)
    gauss = np.where(inside, np.exp(-shifted * shifted / f32(2.0 * sigma_sq)), f32(0.0)).astype(f32) / weight_sum
    slope = (f32(-coarse_step) * shifted / f32(sigma_sq) * gauss).astype(f32)
    bf = ml_dtypes.bfloat16
    return gauss.astype(bf).astype(f32), slope.astype(bf).astype(f32)


def line_matrices(length):
    fine_pos = np.arange(length)[:, None]
    coarse_pos = np.arange(length // 8)[None, :]
    offsets = np.mod(fine_pos - 8 * coarse_pos, length)
    offsets = np.where(offsets >= length // 2, offsets - length, offsets)
    return tap_weights(offsets)


def z_tables(length):
    coarse = np.arange(length // 8)[None, :]
    main = np.arange(length)[:, None] - 8 * coarse
    prev = np.arange(halo)[:, None] - halo - 8 * coarse
    nxt = np.arange(halo)[:, None] + length - 8 * coarse
    return [tap_weights(o) for o in (main, prev, nxt)]


def filter_kernel(block_count, coarse_block, value_rows, slope_rows):
    def body(x_ref, main_ref, prev_ref, next_ref, wv_ref, ws_ref, o_ref, zv_ref, zs_ref):
        length = x_ref.shape[2]
        blen = length // block_count
        for b in range(block_count):
            main = x_ref[0, :, b * blen:(b + 1) * blen]
            start = (b * blen - halo) % length
            tail = x_ref[0, :, start:start + halo]
            start = ((b + 1) * blen) % length
            head = x_ref[0, :, start:start + halo]
            acc = jnp.dot(main, main_ref[...], preferred_element_type=jnp.float32)
            acc = acc + jnp.dot(tail, prev_ref[...], preferred_element_type=jnp.float32)
            acc = acc + jnp.dot(head, next_ref[...], preferred_element_type=jnp.float32)
            lanes = slice(b * coarse_block, (b + 1) * coarse_block)
            zv_ref[:, lanes] = acc[:, :coarse_block].astype(jnp.bfloat16)
            zs_ref[:, lanes] = acc[:, coarse_block:].astype(jnp.bfloat16)
        zv = zv_ref[...]
        zs = zs_ref[...]
        pv = jnp.dot(wv_ref[0], zv, preferred_element_type=jnp.float32)
        pv = pv + jnp.dot(wv_ref[1], zv, preferred_element_type=jnp.float32)
        ps = jnp.dot(ws_ref[0], zs, preferred_element_type=jnp.float32)
        ps = ps + jnp.dot(ws_ref[1], zs, preferred_element_type=jnp.float32)
        o_ref[0, :value_rows, :] = pv
        o_ref[0, value_rows:, :] = ps

    return body


def split_hi_lo(w):
    hi = w.astype(jnp.bfloat16)
    lo = (w - hi.astype(jnp.float32)).astype(jnp.bfloat16)
    return jnp.stack([hi, lo], axis=0)


def filtered_partials(fields3, value_w, slope_w):
    field_count, rows, length = fields3.shape
    blen = block_len if (length % block_len == 0 and length > block_len) else length
    block_count = length // blen
    coarse_block = blen // 8
    tables = z_tables(blen)
    joined = [np.concatenate([t[0], t[1]], axis=1) for t in tables]
    main, prev, nxt = [jnp.asarray(t, jnp.bfloat16) for t in joined]
    wv = split_hi_lo(value_w)
    ws = split_hi_lo(slope_w)
    value_rows = wv.shape[1]
    slope_rows = ws.shape[1]
    total_rows = value_rows + slope_rows
    coarse = length // 8
    const = lambda f: (0, 0)
    const3 = lambda f: (0, 0, 0)
    return pl.pallas_call(
        filter_kernel(block_count, coarse_block, value_rows, slope_rows),
        out_shape=jax.ShapeDtypeStruct((field_count, total_rows, coarse), jnp.float32),
        grid=(field_count,),
        in_specs=[
            pl.BlockSpec((1, rows, length), lambda f: (f, 0, 0)),
            pl.BlockSpec(main.shape, const),
            pl.BlockSpec(prev.shape, const),
            pl.BlockSpec(nxt.shape, const),
            pl.BlockSpec(wv.shape, const3),
            pl.BlockSpec(ws.shape, const3),
        ],
        out_specs=pl.BlockSpec((1, total_rows, coarse), lambda f: (f, 0, 0)),
        scratch_shapes=[pltpu.VMEM((rows, coarse), jnp.bfloat16), pltpu.VMEM((rows, coarse), jnp.bfloat16)],
    )(fields3, main, prev, nxt, wv, ws)


def transpose_body(x_ref, o_ref):
    rows = x_ref.shape[0]
    width = o_ref.shape[2]
    for gi in range(x_ref.shape[1]):
        slab = x_ref[:, gi, :]
        slab = jnp.concatenate([slab, jnp.zeros((width - rows, slab.shape[1]), slab.dtype)], axis=0)
        o_ref[gi] = slab.T


def cells_by_row(x):
    rows, groups, lanes = x.shape
    step = 8
    width = -(-rows // 128) * 128
    return pl.pallas_call(
        transpose_body,
        out_shape=jax.ShapeDtypeStruct((groups, lanes, width), x.dtype),
        grid=(groups // step,),
        in_specs=[pl.BlockSpec((rows, step, lanes), lambda j: (0, j, 0))],
        out_specs=pl.BlockSpec((step, lanes, width), lambda j: (j, 0, 0)),
    )(x)


def model_tensors(coarse):
    values = coarse.astype(jnp.float32)
    points = values.shape[-1]
    values = values.reshape(values.shape[0] // 3, 3, points)
    velocity = values[:3]
    species = values[3:]
    stress = [
        jnp.sum(velocity[first_comp] * velocity[second_comp], axis=0)
        for first_comp, second_comp in upper_pairs
    ]
    species_flux = jnp.sum(species[:, None, :, :] * velocity[None, :, :, :], axis=2)
    joined = jnp.concatenate([jnp.stack(stress, axis=0), species_flux.reshape(-1, points)], axis=0)
    return (model_coeff * joined).astype(jnp.bfloat16)


def window(at, count, coarse):
    reach = (count + 19) // 8 + 4
    if count % 8 or reach >= coarse:
        return 0, coarse
    return at * (count // 8) - 3, reach


def make_shards(row_count, col_count):
    def shards(fields, front_cells):
        field_count, local_x, local_y, z_length = fields.shape
        devices = row_count * col_count
        full_x = local_x * row_count
        full_y = local_y * col_count
        coarse_x = full_x // 8
        coarse_y = full_y // 8
        coarse_z = z_length // 8
        slab = coarse_z // devices
        slots = front_cells.shape[2]
        row = lax.axis_index("rows")
        col = lax.axis_index("cols")
        me = row * col_count + col

        copies = jnp.broadcast_to(front_cells, (devices,) + front_cells.shape[1:])
        every_cell = lax.all_to_all(copies, ("rows", "cols"), split_axis=0, concat_axis=0, tiled=True)

        smooth_x, deriv_x = line_matrices(full_x)
        smooth_y, deriv_y = line_matrices(full_y)
        x_base, x_count = window(row, local_x, coarse_x)
        y_base, y_count = window(col, local_y, coarse_y)

        def local_rows(table, at, count, base, width, full):
            rows = lax.dynamic_slice_in_dim(jnp.asarray(table), at * count, count)
            picks = (base + jnp.arange(width)) % full
            return jnp.take(rows, picks, axis=1)

        ax = local_rows(smooth_x, row, local_x, x_base, x_count, coarse_x)
        bx = local_rows(deriv_x, row, local_x, x_base, x_count, coarse_x)
        ay = local_rows(smooth_y, col, local_y, y_base, y_count, coarse_y)
        by = local_rows(deriv_y, col, local_y, y_base, y_count, coarse_y)
        group = x_count * y_count
        padded = -(-group // 8) * 8

        def kron(wx, wy):
            joined = (wx[:, None, :, None] * wy[None, :, None, :]).reshape(local_x * local_y, group)
            return jnp.pad(joined, ((0, 0), (0, padded - group))).T

        value_w = jnp.concatenate([kron(bx, ay), kron(ax, by)], axis=0)
        slope_w = kron(ax, ay)
        fields3 = fields.reshape(field_count, local_x * local_y, z_length)
        partials = filtered_partials(fields3, value_w, slope_w)
        partials = partials.reshape(field_count, 3, padded, coarse_z)

        by_owner = jnp.transpose(every_cell, (1, 0, 2))
        holder = lax.broadcasted_iota(jnp.int32, by_owner.shape, 1)
        clipped = jnp.clip(by_owner, 0, coarse_x * coarse_y * slab - 1)
        cell_pq = clipped // slab
        at_z = holder * slab + clipped % slab
        at_x = (cell_pq // coarse_y - x_base) % coarse_x
        at_y = (cell_pq % coarse_y - y_base) % coarse_y
        inside = (at_x < x_count) & (at_y < y_count) & (by_owner >= 0)
        at_group = jnp.where(inside, at_x * y_count + at_y, 0)
        flat = (at_group * coarse_z + at_z).reshape(-1)
        table = cells_by_row(partials.reshape(field_count * 3, padded, coarse_z))
        taken = jnp.take(table.reshape(padded * coarse_z, -1), flat, axis=0)[:, :field_count * 3]
        taken = jnp.where(inside.reshape(-1, 1), taken, jnp.zeros_like(taken))
        taken = taken.reshape(devices, -1, field_count * 3)
        arrived = lax.all_to_all(taken, ("rows", "cols"), split_axis=0, concat_axis=0, tiled=True)
        summed = jnp.sum(arrived.reshape(devices, -1, field_count * 3), axis=0).T
        rounded = lax.reduce_precision(summed, exponent_bits=8, mantissa_bits=7)
        mine = lax.dynamic_index_in_dim(by_owner, me, axis=0, keepdims=False).reshape(-1)
        picked = jnp.where(mine[None, :] >= 0, rounded, jnp.zeros_like(rounded))
        return model_tensors(picked)[None]

    return shards


def solution(mesh):
    in_specs = (P(None, "rows", "cols", None), P(("rows", "cols"), None, None))
    out_specs = P(("rows", "cols"), None, None)
    shards = make_shards(mesh.shape["rows"], mesh.shape["cols"])
    return jax.shard_map(shards, mesh=mesh, in_specs=in_specs, out_specs=out_specs, check_vma=False)
```

```python
import numpy as np
import jax
import jax.numpy as jnp
import ml_dtypes
from jax import lax
from jax.sharding import PartitionSpec as P
from jax.experimental import pallas as pl
from jax.experimental.pallas import tpu as pltpu

first_tap = -20
last_tap = 27
sigma_sq = 256.0 / 12.0
coarse_step = 8.0
model_coeff = 1.0 / 3.0
upper_pairs = ((0, 0), (0, 1), (0, 2), (1, 1), (1, 2), (2, 2))
block_len = 1024
halo = 128


def tap_weights(offsets):
    f32 = np.float32
    every_tap = np.arange(first_tap, last_tap + 1).astype(f32)
    weight_sum = np.sum(np.exp(-(every_tap - f32(3.5)) * (every_tap - f32(3.5)) / f32(2.0 * sigma_sq)), dtype=f32)
    shifted = offsets.astype(f32) - f32(3.5)
    inside = (offsets >= first_tap) & (offsets <= last_tap)
    gauss = np.where(inside, np.exp(-shifted * shifted / f32(2.0 * sigma_sq)), f32(0.0)).astype(f32) / weight_sum
    slope = (f32(-coarse_step) * shifted / f32(sigma_sq) * gauss).astype(f32)
    bf = ml_dtypes.bfloat16
    return gauss.astype(bf).astype(f32), slope.astype(bf).astype(f32)


def line_matrices(length):
    fine_pos = np.arange(length)[:, None]
    coarse_pos = np.arange(length // 8)[None, :]
    offsets = np.mod(fine_pos - 8 * coarse_pos, length)
    offsets = np.where(offsets >= length // 2, offsets - length, offsets)
    return tap_weights(offsets)


def z_tables(length):
    coarse = np.arange(length // 8)[None, :]
    main = np.arange(length)[:, None] - 8 * coarse
    prev = np.arange(halo)[:, None] - halo - 8 * coarse
    nxt = np.arange(halo)[:, None] + length - 8 * coarse
    return [tap_weights(o) for o in (main, prev, nxt)]


def filter_kernel(block_count, coarse_block, value_rows, slope_rows):
    def body(x_ref, main_ref, prev_ref, next_ref, wv_ref, ws_ref, o_ref, zv_ref, zs_ref):
        length = x_ref.shape[2]
        blen = length // block_count
        for b in range(block_count):
            main = x_ref[0, :, b * blen:(b + 1) * blen]
            start = (b * blen - halo) % length
            tail = x_ref[0, :, start:start + halo]
            start = ((b + 1) * blen) % length
            head = x_ref[0, :, start:start + halo]
            acc = jnp.dot(main, main_ref[...], preferred_element_type=jnp.float32)
            acc = acc + jnp.dot(tail, prev_ref[...], preferred_element_type=jnp.float32)
            acc = acc + jnp.dot(head, next_ref[...], preferred_element_type=jnp.float32)
            lanes = slice(b * coarse_block, (b + 1) * coarse_block)
            zv_ref[:, lanes] = acc[:, :coarse_block].astype(jnp.bfloat16)
            zs_ref[:, lanes] = acc[:, coarse_block:].astype(jnp.bfloat16)
        zv = zv_ref[...]
        zs = zs_ref[...]
        pv = jnp.dot(wv_ref[0], zv, preferred_element_type=jnp.float32)
        pv = pv + jnp.dot(wv_ref[1], zv, preferred_element_type=jnp.float32)
        ps = jnp.dot(ws_ref[0], zs, preferred_element_type=jnp.float32)
        ps = ps + jnp.dot(ws_ref[1], zs, preferred_element_type=jnp.float32)
        o_ref[0, :value_rows, :] = pv
        o_ref[0, value_rows:, :] = ps

    return body


def split_hi_lo(w):
    hi = w.astype(jnp.bfloat16)
    lo = (w - hi.astype(jnp.float32)).astype(jnp.bfloat16)
    return jnp.stack([hi, lo], axis=0)


def filtered_partials(fields3, value_w, slope_w):
    field_count, rows, length = fields3.shape
    blen = block_len if (length % block_len == 0 and length > block_len) else length
    block_count = length // blen
    coarse_block = blen // 8
    tables = z_tables(blen)
    joined = [np.concatenate([t[0], t[1]], axis=1) for t in tables]
    main, prev, nxt = [jnp.asarray(t, jnp.bfloat16) for t in joined]
    wv = split_hi_lo(value_w)
    ws = split_hi_lo(slope_w)
    value_rows = wv.shape[1]
    slope_rows = ws.shape[1]
    total_rows = value_rows + slope_rows
    coarse = length // 8
    const = lambda f: (0, 0)
    const3 = lambda f: (0, 0, 0)
    return pl.pallas_call(
        filter_kernel(block_count, coarse_block, value_rows, slope_rows),
        out_shape=jax.ShapeDtypeStruct((field_count, total_rows, coarse), jnp.float32),
        grid=(field_count,),
        in_specs=[
            pl.BlockSpec((1, rows, length), lambda f: (f, 0, 0)),
            pl.BlockSpec(main.shape, const),
            pl.BlockSpec(prev.shape, const),
            pl.BlockSpec(nxt.shape, const),
            pl.BlockSpec(wv.shape, const3),
            pl.BlockSpec(ws.shape, const3),
        ],
        out_specs=pl.BlockSpec((1, total_rows, coarse), lambda f: (f, 0, 0)),
        scratch_shapes=[pltpu.VMEM((rows, coarse), jnp.bfloat16), pltpu.VMEM((rows, coarse), jnp.bfloat16)],
    )(fields3, main, prev, nxt, wv, ws)


def pick_kernel(group_steps, step, chunk):
    def body(idx_ref, x_ref, o_ref, tab_ref):
        j = pl.program_id(0)
        rows = x_ref.shape[0]
        lanes = x_ref.shape[2]
        width = tab_ref.shape[1]

        @pl.when(j < group_steps)
        def _():
            for gi in range(step):
                slab = x_ref[:, gi, :]
                slab = jnp.concatenate([slab, jnp.zeros((width - rows, lanes), slab.dtype)], axis=0)
                at = pl.multiple_of((j * step + gi) * lanes, lanes)
                tab_ref[pl.ds(at, lanes), :] = slab.T

        @pl.when(j == group_steps - 1)
        def _():
            tail = tab_ref.shape[0] - 8
            tab_ref[pl.ds(tail, 8), :] = jnp.zeros((8, width), tab_ref.dtype)

        @pl.when(j >= group_steps)
        def _():
            base = (j - group_steps) * chunk

            def one(e, carry):
                at = idx_ref[base + e]
                o_ref[pl.ds(e, 1), :] = tab_ref[pl.ds(at, 1), :][:, :rows]
                return carry

            lax.fori_loop(0, chunk, one, 0, unroll=8)

    return body


def pick_cells(x, flat, chunk=2048):
    rows, groups, lanes = x.shape
    step = 8
    group_steps = groups // step
    entries = flat.shape[0]
    chunk = min(chunk, entries)
    width = -(-rows // 128) * 128
    grid_spec = pltpu.PrefetchScalarGridSpec(
        num_scalar_prefetch=1,
        grid=(group_steps + entries // chunk,),
        in_specs=[pl.BlockSpec((rows, step, lanes), lambda j, idx: (0, jnp.minimum(j, group_steps - 1), 0))],
        out_specs=pl.BlockSpec((chunk, rows), lambda j, idx: (jnp.maximum(j - group_steps, 0), 0)),
        scratch_shapes=[pltpu.VMEM((groups * lanes + 8, width), x.dtype)],
    )
    return pl.pallas_call(
        pick_kernel(group_steps, step, chunk),
        out_shape=jax.ShapeDtypeStruct((entries, rows), x.dtype),
        grid_spec=grid_spec,
    )(flat, x)


def model_tensors(coarse):
    values = coarse.astype(jnp.float32)
    points = values.shape[-1]
    values = values.reshape(values.shape[0] // 3, 3, points)
    velocity = values[:3]
    species = values[3:]
    stress = [
        jnp.sum(velocity[first_comp] * velocity[second_comp], axis=0)
        for first_comp, second_comp in upper_pairs
    ]
    species_flux = jnp.sum(species[:, None, :, :] * velocity[None, :, :, :], axis=2)
    joined = jnp.concatenate([jnp.stack(stress, axis=0), species_flux.reshape(-1, points)], axis=0)
    return (model_coeff * joined).astype(jnp.bfloat16)


def window(at, count, coarse):
    reach = (count + 19) // 8 + 4
    if count % 8 or reach >= coarse:
        return 0, coarse
    return at * (count // 8) - 3, reach


def make_shards(row_count, col_count):
    def shards(fields, front_cells):
        field_count, local_x, local_y, z_length = fields.shape
        devices = row_count * col_count
        full_x = local_x * row_count
        full_y = local_y * col_count
        coarse_x = full_x // 8
        coarse_y = full_y // 8
        coarse_z = z_length // 8
        slab = coarse_z // devices
        slots = front_cells.shape[2]
        row = lax.axis_index("rows")
        col = lax.axis_index("cols")
        me = row * col_count + col

        copies = jnp.broadcast_to(front_cells, (devices,) + front_cells.shape[1:])
        every_cell = lax.all_to_all(copies, ("rows", "cols"), split_axis=0, concat_axis=0, tiled=True)

        smooth_x, deriv_x = line_matrices(full_x)
        smooth_y, deriv_y = line_matrices(full_y)
        x_base, x_count = window(row, local_x, coarse_x)
        y_base, y_count = window(col, local_y, coarse_y)

        def local_rows(table, at, count, base, width, full):
            rows = lax.dynamic_slice_in_dim(jnp.asarray(table), at * count, count)
            picks = (base + jnp.arange(width)) % full
            return jnp.take(rows, picks, axis=1)

        ax = local_rows(smooth_x, row, local_x, x_base, x_count, coarse_x)
        bx = local_rows(deriv_x, row, local_x, x_base, x_count, coarse_x)
        ay = local_rows(smooth_y, col, local_y, y_base, y_count, coarse_y)
        by = local_rows(deriv_y, col, local_y, y_base, y_count, coarse_y)
        group = x_count * y_count
        padded = -(-group // 8) * 8

        def kron(wx, wy):
            joined = (wx[:, None, :, None] * wy[None, :, None, :]).reshape(local_x * local_y, group)
            return jnp.pad(joined, ((0, 0), (0, padded - group))).T

        value_w = jnp.concatenate([kron(bx, ay), kron(ax, by)], axis=0)
        slope_w = kron(ax, ay)
        fields3 = fields.reshape(field_count, local_x * local_y, z_length)
        partials = filtered_partials(fields3, value_w, slope_w)
        partials = partials.reshape(field_count, 3, padded, coarse_z)

        by_owner = jnp.transpose(every_cell, (1, 0, 2))
        holder = lax.broadcasted_iota(jnp.int32, by_owner.shape, 1)
        clipped = jnp.clip(by_owner, 0, coarse_x * coarse_y * slab - 1)
        cell_pq = clipped // slab
        at_z = holder * slab + clipped % slab
        at_x = (cell_pq // coarse_y - x_base) % coarse_x
        at_y = (cell_pq % coarse_y - y_base) % coarse_y
        inside = (at_x < x_count) & (at_y < y_count) & (by_owner >= 0)
        flat = jnp.where(inside, (at_x * y_count + at_y) * coarse_z + at_z, padded * coarse_z)
        taken = pick_cells(partials.reshape(field_count * 3, padded, coarse_z), flat.reshape(-1))
        taken = taken.reshape(devices, -1, field_count * 3)
        arrived = lax.all_to_all(taken, ("rows", "cols"), split_axis=0, concat_axis=0, tiled=True)
        summed = jnp.sum(arrived.reshape(devices, -1, field_count * 3), axis=0).T
        rounded = lax.reduce_precision(summed, exponent_bits=8, mantissa_bits=7)
        mine = lax.dynamic_index_in_dim(by_owner, me, axis=0, keepdims=False).reshape(-1)
        picked = jnp.where(mine[None, :] >= 0, rounded, jnp.zeros_like(rounded))
        return model_tensors(picked)[None]

    return shards


def solution(mesh):
    in_specs = (P(None, "rows", "cols", None), P(("rows", "cols"), None, None))
    out_specs = P(("rows", "cols"), None, None)
    shards = make_shards(mesh.shape["rows"], mesh.shape["cols"])
    return jax.shard_map(shards, mesh=mesh, in_specs=in_specs, out_specs=out_specs, check_vma=False)
```

```python
import numpy as np
import jax
import jax.numpy as jnp
import ml_dtypes
from jax import lax
from jax.sharding import PartitionSpec as P
from jax.experimental import pallas as pl
from jax.experimental.pallas import tpu as pltpu

first_tap = -20
last_tap = 27
sigma_sq = 256.0 / 12.0
coarse_step = 8.0
model_coeff = 1.0 / 3.0
upper_pairs = ((0, 0), (0, 1), (0, 2), (1, 1), (1, 2), (2, 2))
block_len = 1024
halo = 128


def tap_weights(offsets):
    f32 = np.float32
    every_tap = np.arange(first_tap, last_tap + 1).astype(f32)
    weight_sum = np.sum(np.exp(-(every_tap - f32(3.5)) * (every_tap - f32(3.5)) / f32(2.0 * sigma_sq)), dtype=f32)
    shifted = offsets.astype(f32) - f32(3.5)
    inside = (offsets >= first_tap) & (offsets <= last_tap)
    gauss = np.where(inside, np.exp(-shifted * shifted / f32(2.0 * sigma_sq)), f32(0.0)).astype(f32) / weight_sum
    slope = (f32(-coarse_step) * shifted / f32(sigma_sq) * gauss).astype(f32)
    bf = ml_dtypes.bfloat16
    return gauss.astype(bf).astype(f32), slope.astype(bf).astype(f32)


def line_matrices(length):
    fine_pos = np.arange(length)[:, None]
    coarse_pos = np.arange(length // 8)[None, :]
    offsets = np.mod(fine_pos - 8 * coarse_pos, length)
    offsets = np.where(offsets >= length // 2, offsets - length, offsets)
    return tap_weights(offsets)


def z_tables(length):
    coarse = np.arange(length // 8)[None, :]
    main = np.arange(length)[:, None] - 8 * coarse
    prev = np.arange(halo)[:, None] - halo - 8 * coarse
    nxt = np.arange(halo)[:, None] + length - 8 * coarse
    return [tap_weights(o) for o in (main, prev, nxt)]


def filter_kernel(block_count, coarse_block, value_rows, slope_rows):
    def body(x_ref, main_ref, prev_ref, next_ref, wv_ref, ws_ref, o_ref, zv_ref, zs_ref):
        length = x_ref.shape[2]
        blen = length // block_count
        for b in range(block_count):
            main = x_ref[0, :, b * blen:(b + 1) * blen]
            start = (b * blen - halo) % length
            tail = x_ref[0, :, start:start + halo]
            start = ((b + 1) * blen) % length
            head = x_ref[0, :, start:start + halo]
            acc = jnp.dot(main, main_ref[...], preferred_element_type=jnp.float32)
            acc = acc + jnp.dot(tail, prev_ref[...], preferred_element_type=jnp.float32)
            acc = acc + jnp.dot(head, next_ref[...], preferred_element_type=jnp.float32)
            lanes = slice(b * coarse_block, (b + 1) * coarse_block)
            zv_ref[:, lanes] = acc[:, :coarse_block].astype(jnp.bfloat16)
            zs_ref[:, lanes] = acc[:, coarse_block:].astype(jnp.bfloat16)
        zv = zv_ref[...]
        zs = zs_ref[...]
        pv = jnp.dot(wv_ref[0], zv, preferred_element_type=jnp.float32)
        pv = pv + jnp.dot(wv_ref[1], zv, preferred_element_type=jnp.float32)
        ps = jnp.dot(ws_ref[0], zs, preferred_element_type=jnp.float32)
        ps = ps + jnp.dot(ws_ref[1], zs, preferred_element_type=jnp.float32)
        o_ref[0, :value_rows, :] = pv
        o_ref[0, value_rows:, :] = ps

    return body


def split_hi_lo(w):
    hi = w.astype(jnp.bfloat16)
    lo = (w - hi.astype(jnp.float32)).astype(jnp.bfloat16)
    return jnp.stack([hi, lo], axis=0)


def filtered_partials(fields3, value_w, slope_w):
    field_count, rows, length = fields3.shape
    blen = block_len if (length % block_len == 0 and length > block_len) else length
    block_count = length // blen
    coarse_block = blen // 8
    tables = z_tables(blen)
    joined = [np.concatenate([t[0], t[1]], axis=1) for t in tables]
    main, prev, nxt = [jnp.asarray(t, jnp.bfloat16) for t in joined]
    wv = split_hi_lo(value_w)
    ws = split_hi_lo(slope_w)
    value_rows = wv.shape[1]
    slope_rows = ws.shape[1]
    total_rows = value_rows + slope_rows
    coarse = length // 8
    const = lambda f: (0, 0)
    const3 = lambda f: (0, 0, 0)
    return pl.pallas_call(
        filter_kernel(block_count, coarse_block, value_rows, slope_rows),
        out_shape=jax.ShapeDtypeStruct((field_count, total_rows, coarse), jnp.float32),
        grid=(field_count,),
        in_specs=[
            pl.BlockSpec((1, rows, length), lambda f: (f, 0, 0)),
            pl.BlockSpec(main.shape, const),
            pl.BlockSpec(prev.shape, const),
            pl.BlockSpec(nxt.shape, const),
            pl.BlockSpec(wv.shape, const3),
            pl.BlockSpec(ws.shape, const3),
        ],
        out_specs=pl.BlockSpec((1, total_rows, coarse), lambda f: (f, 0, 0)),
        scratch_shapes=[pltpu.VMEM((rows, coarse), jnp.bfloat16), pltpu.VMEM((rows, coarse), jnp.bfloat16)],
    )(fields3, main, prev, nxt, wv, ws)


def pick_kernel(group_steps, step, chunk, owner_len):
    def body(idx_ref, x_ref, o_ref, tab_ref, buf_ref):
        j = pl.program_id(0)
        rows = x_ref.shape[0]
        lanes = x_ref.shape[2]
        width = tab_ref.shape[1]

        @pl.when(j < group_steps)
        def _():
            for gi in range(step):
                slab = x_ref[:, gi, :]
                slab = jnp.concatenate([slab, jnp.zeros((width - rows, lanes), slab.dtype)], axis=0)
                at = pl.multiple_of((j * step + gi) * lanes, lanes)
                tab_ref[pl.ds(at, lanes), :] = slab.T

        @pl.when(j == group_steps - 1)
        def _():
            tail = tab_ref.shape[0] - 8
            tab_ref[pl.ds(tail, 8), :] = jnp.zeros((8, width), tab_ref.dtype)

        @pl.when(j >= group_steps)
        def _():
            base = (j - group_steps) * chunk

            def one(e, carry):
                at = idx_ref[base + e]
                buf_ref[pl.ds(e, 1), :] = tab_ref[pl.ds(at, 1), :]
                return carry

            lax.fori_loop(0, chunk, one, 0, unroll=8)
            flipped = buf_ref[...].T
            for owner in range(chunk // owner_len):
                o_ref[owner] = flipped[:rows, owner * owner_len:(owner + 1) * owner_len]

    return body


def pick_cells(x, flat, owner_len, chunk=2048):
    rows, groups, lanes = x.shape
    step = 8
    group_steps = groups // step
    entries = flat.shape[0]
    chunk = min(chunk, entries)
    width = -(-rows // 128) * 128
    per_chunk = chunk // owner_len
    grid_spec = pltpu.PrefetchScalarGridSpec(
        num_scalar_prefetch=1,
        grid=(group_steps + entries // chunk,),
        in_specs=[pl.BlockSpec((rows, step, lanes), lambda j, idx: (0, jnp.minimum(j, group_steps - 1), 0))],
        out_specs=pl.BlockSpec((per_chunk, rows, owner_len), lambda j, idx: (jnp.maximum(j - group_steps, 0), 0, 0)),
        scratch_shapes=[pltpu.VMEM((groups * lanes + 8, width), x.dtype), pltpu.VMEM((chunk, width), x.dtype)],
    )
    return pl.pallas_call(
        pick_kernel(group_steps, step, chunk, owner_len),
        out_shape=jax.ShapeDtypeStruct((entries // owner_len, rows, owner_len), x.dtype),
        grid_spec=grid_spec,
    )(flat, x)


def model_tensors(coarse):
    values = coarse.astype(jnp.float32)
    points = values.shape[-1]
    values = values.reshape(values.shape[0] // 3, 3, points)
    velocity = values[:3]
    species = values[3:]
    stress = [
        jnp.sum(velocity[first_comp] * velocity[second_comp], axis=0)
        for first_comp, second_comp in upper_pairs
    ]
    species_flux = jnp.sum(species[:, None, :, :] * velocity[None, :, :, :], axis=2)
    joined = jnp.concatenate([jnp.stack(stress, axis=0), species_flux.reshape(-1, points)], axis=0)
    return (model_coeff * joined).astype(jnp.bfloat16)


def window(at, count, coarse):
    reach = (count + 19) // 8 + 4
    if count % 8 or reach >= coarse:
        return 0, coarse
    return at * (count // 8) - 3, reach


def make_shards(row_count, col_count):
    def shards(fields, front_cells):
        field_count, local_x, local_y, z_length = fields.shape
        devices = row_count * col_count
        full_x = local_x * row_count
        full_y = local_y * col_count
        coarse_x = full_x // 8
        coarse_y = full_y // 8
        coarse_z = z_length // 8
        slab = coarse_z // devices
        slots = front_cells.shape[2]
        row = lax.axis_index("rows")
        col = lax.axis_index("cols")
        me = row * col_count + col

        copies = jnp.broadcast_to(front_cells, (devices,) + front_cells.shape[1:])
        every_cell = lax.all_to_all(copies, ("rows", "cols"), split_axis=0, concat_axis=0, tiled=True)

        smooth_x, deriv_x = line_matrices(full_x)
        smooth_y, deriv_y = line_matrices(full_y)
        x_base, x_count = window(row, local_x, coarse_x)
        y_base, y_count = window(col, local_y, coarse_y)

        def local_rows(table, at, count, base, width, full):
            rows = lax.dynamic_slice_in_dim(jnp.asarray(table), at * count, count)
            picks = (base + jnp.arange(width)) % full
            return jnp.take(rows, picks, axis=1)

        ax = local_rows(smooth_x, row, local_x, x_base, x_count, coarse_x)
        bx = local_rows(deriv_x, row, local_x, x_base, x_count, coarse_x)
        ay = local_rows(smooth_y, col, local_y, y_base, y_count, coarse_y)
        by = local_rows(deriv_y, col, local_y, y_base, y_count, coarse_y)
        group = x_count * y_count
        padded = -(-group // 8) * 8

        def kron(wx, wy):
            joined = (wx[:, None, :, None] * wy[None, :, None, :]).reshape(local_x * local_y, group)
            return jnp.pad(joined, ((0, 0), (0, padded - group))).T

        value_w = jnp.concatenate([kron(bx, ay), kron(ax, by)], axis=0)
        slope_w = kron(ax, ay)
        fields3 = fields.reshape(field_count, local_x * local_y, z_length)
        partials = filtered_partials(fields3, value_w, slope_w)
        partials = partials.reshape(field_count, 3, padded, coarse_z)

        by_owner = jnp.transpose(every_cell, (1, 0, 2))
        holder = lax.broadcasted_iota(jnp.int32, by_owner.shape, 1)
        clipped = jnp.clip(by_owner, 0, coarse_x * coarse_y * slab - 1)
        cell_pq = clipped // slab
        at_z = holder * slab + clipped % slab
        at_x = (cell_pq // coarse_y - x_base) % coarse_x
        at_y = (cell_pq % coarse_y - y_base) % coarse_y
        inside = (at_x < x_count) & (at_y < y_count) & (by_owner >= 0)
        flat = jnp.where(inside, (at_x * y_count + at_y) * coarse_z + at_z, padded * coarse_z)
        owner_len = devices * slots
        taken = pick_cells(partials.reshape(field_count * 3, padded, coarse_z), flat.reshape(-1), owner_len)
        arrived = lax.all_to_all(taken, ("rows", "cols"), split_axis=0, concat_axis=0, tiled=True)
        summed = jnp.sum(arrived, axis=0)
        rounded = lax.reduce_precision(summed, exponent_bits=8, mantissa_bits=7)
        mine = lax.dynamic_index_in_dim(by_owner, me, axis=0, keepdims=False).reshape(-1)
        picked = jnp.where(mine[None, :] >= 0, rounded, jnp.zeros_like(rounded))
        return model_tensors(picked)[None]

    return shards


def solution(mesh):
    in_specs = (P(None, "rows", "cols", None), P(("rows", "cols"), None, None))
    out_specs = P(("rows", "cols"), None, None)
    shards = make_shards(mesh.shape["rows"], mesh.shape["cols"])
    return jax.shard_map(shards, mesh=mesh, in_specs=in_specs, out_specs=out_specs, check_vma=False)
```

```python
import numpy as np
import jax
import jax.numpy as jnp
import ml_dtypes
from jax import lax
from jax.sharding import PartitionSpec as P
from jax.experimental import pallas as pl
from jax.experimental.pallas import tpu as pltpu

first_tap = -20
last_tap = 27
sigma_sq = 256.0 / 12.0
coarse_step = 8.0
model_coeff = 1.0 / 3.0
upper_pairs = ((0, 0), (0, 1), (0, 2), (1, 1), (1, 2), (2, 2))
block_len = 1024
halo = 128


def tap_weights(offsets):
    f32 = np.float32
    every_tap = np.arange(first_tap, last_tap + 1).astype(f32)
    weight_sum = np.sum(np.exp(-(every_tap - f32(3.5)) * (every_tap - f32(3.5)) / f32(2.0 * sigma_sq)), dtype=f32)
    shifted = offsets.astype(f32) - f32(3.5)
    inside = (offsets >= first_tap) & (offsets <= last_tap)
    gauss = np.where(inside, np.exp(-shifted * shifted / f32(2.0 * sigma_sq)), f32(0.0)).astype(f32) / weight_sum
    slope = (f32(-coarse_step) * shifted / f32(sigma_sq) * gauss).astype(f32)
    bf = ml_dtypes.bfloat16
    return gauss.astype(bf).astype(f32), slope.astype(bf).astype(f32)


def line_matrices(length):
    fine_pos = np.arange(length)[:, None]
    coarse_pos = np.arange(length // 8)[None, :]
    offsets = np.mod(fine_pos - 8 * coarse_pos, length)
    offsets = np.where(offsets >= length // 2, offsets - length, offsets)
    return tap_weights(offsets)


def z_tables(length):
    coarse = np.arange(length // 8)[None, :]
    main = np.arange(length)[:, None] - 8 * coarse
    prev = np.arange(halo)[:, None] - halo - 8 * coarse
    nxt = np.arange(halo)[:, None] + length - 8 * coarse
    return [tap_weights(o) for o in (main, prev, nxt)]


def filter_kernel(block_count, coarse_block, value_rows, slope_rows):
    def body(x_ref, main_ref, halo_ref, w_ref, o_ref, zv_ref, zs_ref):
        length = x_ref.shape[2]
        blen = length // block_count
        for b in range(block_count):
            main = x_ref[0, :, b * blen:(b + 1) * blen]
            start = (b * blen - halo) % length
            tail = x_ref[0, :, start:start + halo]
            start = ((b + 1) * blen) % length
            head = x_ref[0, :, start:start + halo]
            edges = jnp.concatenate([tail, head], axis=1)
            acc = jnp.dot(main, main_ref[...], preferred_element_type=jnp.float32)
            acc = acc + jnp.dot(edges, halo_ref[...], preferred_element_type=jnp.float32)
            lanes = slice(b * coarse_block, (b + 1) * coarse_block)
            zv_ref[:, lanes] = acc[:, :coarse_block].astype(jnp.bfloat16)
            zs_ref[:, lanes] = acc[:, coarse_block:].astype(jnp.bfloat16)
        zv = zv_ref[...]
        zs = zs_ref[...]
        pv = jnp.dot(w_ref[0, :value_rows, :], zv, preferred_element_type=jnp.float32)
        pv = pv + jnp.dot(w_ref[1, :value_rows, :], zv, preferred_element_type=jnp.float32)
        ps = jnp.dot(w_ref[0, value_rows:, :], zs, preferred_element_type=jnp.float32)
        ps = ps + jnp.dot(w_ref[1, value_rows:, :], zs, preferred_element_type=jnp.float32)
        o_ref[0, :value_rows, :] = pv
        o_ref[0, value_rows:, :] = ps

    return body


def split_hi_lo(w):
    hi = w.astype(jnp.bfloat16)
    lo = (w - hi.astype(jnp.float32)).astype(jnp.bfloat16)
    return jnp.stack([hi, lo], axis=0)


def filtered_partials(fields3, weights):
    field_count, rows, length = fields3.shape
    blen = block_len if (length % block_len == 0 and length > block_len) else length
    block_count = length // blen
    coarse_block = blen // 8
    tables = z_tables(blen)
    joined = [np.concatenate([t[0], t[1]], axis=1) for t in tables]
    main = jnp.asarray(joined[0], jnp.bfloat16)
    halo_w = jnp.asarray(np.concatenate([joined[1], joined[2]], axis=0), jnp.bfloat16)
    w = split_hi_lo(weights)
    total_rows = w.shape[1]
    value_rows = total_rows // 3 * 2
    coarse = length // 8
    const = lambda f: (0, 0)
    return pl.pallas_call(
        filter_kernel(block_count, coarse_block, value_rows, total_rows - value_rows),
        out_shape=jax.ShapeDtypeStruct((field_count, total_rows, coarse), jnp.float32),
        grid=(field_count,),
        in_specs=[
            pl.BlockSpec((1, rows, length), lambda f: (f, 0, 0)),
            pl.BlockSpec(main.shape, const),
            pl.BlockSpec(halo_w.shape, const),
            pl.BlockSpec(w.shape, lambda f: (0, 0, 0)),
        ],
        out_specs=pl.BlockSpec((1, total_rows, coarse), lambda f: (f, 0, 0)),
        scratch_shapes=[pltpu.VMEM((rows, coarse), jnp.bfloat16), pltpu.VMEM((rows, coarse), jnp.bfloat16)],
    )(fields3, main, halo_w, w)


def window_tables(blocks, count, full):
    smooth, deriv = line_matrices(full)
    coarse = full // 8
    out = []
    for at in range(blocks):
        base, width = window(at, count, coarse)
        picks = (base + np.arange(width)) % coarse
        part = slice(at * count, (at + 1) * count)
        out.append(np.stack([smooth[part][:, picks].T, deriv[part][:, picks].T]))
    return np.stack(out)


def pick_kernel(group_steps, step, chunk, owner_len):
    def body(idx_ref, x_ref, o_ref, tab_ref, buf_ref):
        j = pl.program_id(0)
        rows = x_ref.shape[0]
        lanes = x_ref.shape[2]
        width = tab_ref.shape[1]

        @pl.when(j < group_steps)
        def _():
            for gi in range(step):
                slab = x_ref[:, gi, :]
                slab = jnp.concatenate([slab, jnp.zeros((width - rows, lanes), slab.dtype)], axis=0)
                at = pl.multiple_of((j * step + gi) * lanes, lanes)
                tab_ref[pl.ds(at, lanes), :] = slab.T

        @pl.when(j == group_steps - 1)
        def _():
            tail = tab_ref.shape[0] - 8
            tab_ref[pl.ds(tail, 8), :] = jnp.zeros((8, width), tab_ref.dtype)

        @pl.when(j >= group_steps)
        def _():
            base = (j - group_steps) * chunk

            def one(e, carry):
                at = idx_ref[base + e]
                buf_ref[pl.ds(e, 1), :] = tab_ref[pl.ds(at, 1), :]
                return carry

            lax.fori_loop(0, chunk, one, 0, unroll=8)
            flipped = buf_ref[...].T
            for owner in range(chunk // owner_len):
                o_ref[owner] = flipped[:rows, owner * owner_len:(owner + 1) * owner_len]

    return body


def pick_cells(x, flat, owner_len, chunk=2048):
    rows, groups, lanes = x.shape
    step = 8
    group_steps = groups // step
    entries = flat.shape[0]
    chunk = min(chunk, entries)
    width = -(-rows // 128) * 128
    per_chunk = chunk // owner_len
    grid_spec = pltpu.PrefetchScalarGridSpec(
        num_scalar_prefetch=1,
        grid=(group_steps + entries // chunk,),
        in_specs=[pl.BlockSpec((rows, step, lanes), lambda j, idx: (0, jnp.minimum(j, group_steps - 1), 0))],
        out_specs=pl.BlockSpec((per_chunk, rows, owner_len), lambda j, idx: (jnp.maximum(j - group_steps, 0), 0, 0)),
        scratch_shapes=[pltpu.VMEM((groups * lanes + 8, width), x.dtype), pltpu.VMEM((chunk, width), x.dtype)],
    )
    return pl.pallas_call(
        pick_kernel(group_steps, step, chunk, owner_len),
        out_shape=jax.ShapeDtypeStruct((entries // owner_len, rows, owner_len), x.dtype),
        grid_spec=grid_spec,
    )(flat, x)


def model_tensors(coarse):
    values = coarse.astype(jnp.float32)
    points = values.shape[-1]
    values = values.reshape(values.shape[0] // 3, 3, points)
    velocity = values[:3]
    species = values[3:]
    stress = [
        jnp.sum(velocity[first_comp] * velocity[second_comp], axis=0)
        for first_comp, second_comp in upper_pairs
    ]
    species_flux = jnp.sum(species[:, None, :, :] * velocity[None, :, :, :], axis=2)
    joined = jnp.concatenate([jnp.stack(stress, axis=0), species_flux.reshape(-1, points)], axis=0)
    return (model_coeff * joined).astype(jnp.bfloat16)


def window(at, count, coarse):
    reach = (count + 19) // 8 + 4
    if count % 8 or reach >= coarse:
        return 0, coarse
    return at * (count // 8) - 3, reach


def make_shards(row_count, col_count):
    def shards(fields, front_cells):
        field_count, local_x, local_y, z_length = fields.shape
        devices = row_count * col_count
        full_x = local_x * row_count
        full_y = local_y * col_count
        coarse_x = full_x // 8
        coarse_y = full_y // 8
        coarse_z = z_length // 8
        slab = coarse_z // devices
        slots = front_cells.shape[2]
        row = lax.axis_index("rows")
        col = lax.axis_index("cols")
        me = row * col_count + col

        copies = jnp.broadcast_to(front_cells, (devices,) + front_cells.shape[1:])
        every_cell = lax.all_to_all(copies, ("rows", "cols"), split_axis=0, concat_axis=0, tiled=True)

        x_base, x_count = window(row, local_x, coarse_x)
        y_base, y_count = window(col, local_y, coarse_y)
        wx = jnp.asarray(window_tables(row_count, local_x, full_x))[row]
        wy = jnp.asarray(window_tables(col_count, local_y, full_y))[col]
        group = x_count * y_count
        padded = -(-group // 8) * 8
        xs = jnp.stack([wx[1], wx[0], wx[0]])
        ys = jnp.stack([wy[0], wy[1], wy[0]])
        weights = xs[:, :, None, :, None] * ys[:, None, :, None, :]
        weights = weights.reshape(3, group, local_x * local_y)
        weights = jnp.pad(weights, ((0, 0), (0, padded - group), (0, 0))).reshape(3 * padded, -1)
        fields3 = fields.reshape(field_count, local_x * local_y, z_length)
        partials = filtered_partials(fields3, weights)

        by_owner = jnp.transpose(every_cell, (1, 0, 2))
        holder = lax.broadcasted_iota(jnp.int32, by_owner.shape, 1)
        clipped = jnp.clip(by_owner, 0, coarse_x * coarse_y * slab - 1)
        cell_pq = clipped // slab
        at_z = holder * slab + clipped % slab
        at_x = (cell_pq // coarse_y - x_base) % coarse_x
        at_y = (cell_pq % coarse_y - y_base) % coarse_y
        inside = (at_x < x_count) & (at_y < y_count) & (by_owner >= 0)
        flat = jnp.where(inside, (at_x * y_count + at_y) * coarse_z + at_z, padded * coarse_z)
        owner_len = devices * slots
        taken = pick_cells(partials.reshape(field_count * 3, padded, coarse_z), flat.reshape(-1), owner_len)
        arrived = lax.all_to_all(taken, ("rows", "cols"), split_axis=0, concat_axis=0, tiled=True)
        summed = jnp.sum(arrived, axis=0)
        rounded = lax.reduce_precision(summed, exponent_bits=8, mantissa_bits=7)
        mine = lax.dynamic_index_in_dim(by_owner, me, axis=0, keepdims=False).reshape(-1)
        picked = jnp.where(mine[None, :] >= 0, rounded, jnp.zeros_like(rounded))
        return model_tensors(picked)[None]

    return shards


def solution(mesh):
    in_specs = (P(None, "rows", "cols", None), P(("rows", "cols"), None, None))
    out_specs = P(("rows", "cols"), None, None)
    shards = make_shards(mesh.shape["rows"], mesh.shape["cols"])
    return jax.shard_map(shards, mesh=mesh, in_specs=in_specs, out_specs=out_specs, check_vma=False)
```

```python
import numpy as np
import jax
import jax.numpy as jnp
import ml_dtypes
from jax import lax
from jax.sharding import PartitionSpec as P
from jax.experimental import pallas as pl
from jax.experimental.pallas import tpu as pltpu

first_tap = -20
last_tap = 27
sigma_sq = 256.0 / 12.0
coarse_step = 8.0
model_coeff = 1.0 / 3.0
upper_pairs = ((0, 0), (0, 1), (0, 2), (1, 1), (1, 2), (2, 2))
block_len = 1024
halo = 128


def tap_weights(offsets):
    f32 = np.float32
    every_tap = np.arange(first_tap, last_tap + 1).astype(f32)
    weight_sum = np.sum(np.exp(-(every_tap - f32(3.5)) * (every_tap - f32(3.5)) / f32(2.0 * sigma_sq)), dtype=f32)
    shifted = offsets.astype(f32) - f32(3.5)
    inside = (offsets >= first_tap) & (offsets <= last_tap)
    gauss = np.where(inside, np.exp(-shifted * shifted / f32(2.0 * sigma_sq)), f32(0.0)).astype(f32) / weight_sum
    slope = (f32(-coarse_step) * shifted / f32(sigma_sq) * gauss).astype(f32)
    bf = ml_dtypes.bfloat16
    return gauss.astype(bf).astype(f32), slope.astype(bf).astype(f32)


def line_matrices(length):
    fine_pos = np.arange(length)[:, None]
    coarse_pos = np.arange(length // 8)[None, :]
    offsets = np.mod(fine_pos - 8 * coarse_pos, length)
    offsets = np.where(offsets >= length // 2, offsets - length, offsets)
    return tap_weights(offsets)


def z_tables(length):
    coarse = np.arange(length // 8)[None, :]
    main = np.arange(length)[:, None] - 8 * coarse
    prev = np.arange(halo)[:, None] - halo - 8 * coarse
    nxt = np.arange(halo)[:, None] + length - 8 * coarse
    return [tap_weights(o) for o in (main, prev, nxt)]


def filter_kernel(block_count, coarse_block, value_rows, slope_rows):
    def body(x_ref, main_ref, halo_ref, w_ref, o_ref, zv_ref, zs_ref):
        length = x_ref.shape[2]
        blen = length // block_count
        for b in range(block_count):
            main = x_ref[0, :, b * blen:(b + 1) * blen]
            start = (b * blen - halo) % length
            tail = x_ref[0, :, start:start + halo]
            start = ((b + 1) * blen) % length
            head = x_ref[0, :, start:start + halo]
            edges = jnp.concatenate([tail, head], axis=1)
            acc = jnp.dot(main, main_ref[...], preferred_element_type=jnp.float32)
            acc = acc + jnp.dot(edges, halo_ref[...], preferred_element_type=jnp.float32)
            lanes = slice(b * coarse_block, (b + 1) * coarse_block)
            zv_ref[:, lanes] = acc[:, :coarse_block].astype(jnp.bfloat16)
            zs_ref[:, lanes] = acc[:, coarse_block:].astype(jnp.bfloat16)
        zv = zv_ref[...]
        zs = zs_ref[...]
        pv = jnp.dot(w_ref[0, :value_rows, :], zv, preferred_element_type=jnp.float32)
        pv = pv + jnp.dot(w_ref[1, :value_rows, :], zv, preferred_element_type=jnp.float32)
        ps = jnp.dot(w_ref[0, value_rows:, :], zs, preferred_element_type=jnp.float32)
        ps = ps + jnp.dot(w_ref[1, value_rows:, :], zs, preferred_element_type=jnp.float32)
        o_ref[0, :value_rows, :] = pv
        o_ref[0, value_rows:, :] = ps

    return body


def split_hi_lo(w):
    hi = w.astype(jnp.bfloat16)
    lo = (w - hi.astype(jnp.float32)).astype(jnp.bfloat16)
    return jnp.stack([hi, lo], axis=0)


def filtered_partials(fields3, weights):
    field_count, rows, length = fields3.shape
    blen = block_len if (length % block_len == 0 and length > block_len) else length
    block_count = length // blen
    coarse_block = blen // 8
    tables = z_tables(blen)
    joined = [np.concatenate([t[0], t[1]], axis=1) for t in tables]
    main = jnp.asarray(joined[0], jnp.bfloat16)
    halo_w = jnp.asarray(np.concatenate([joined[1], joined[2]], axis=0), jnp.bfloat16)
    w = split_hi_lo(weights)
    total_rows = w.shape[1]
    value_rows = total_rows // 3 * 2
    coarse = length // 8
    const = lambda f: (0, 0)
    return pl.pallas_call(
        filter_kernel(block_count, coarse_block, value_rows, total_rows - value_rows),
        out_shape=jax.ShapeDtypeStruct((field_count, total_rows, coarse), jnp.float32),
        grid=(field_count,),
        in_specs=[
            pl.BlockSpec((1, rows, length), lambda f: (f, 0, 0)),
            pl.BlockSpec(main.shape, const),
            pl.BlockSpec(halo_w.shape, const),
            pl.BlockSpec(w.shape, lambda f: (0, 0, 0)),
        ],
        out_specs=pl.BlockSpec((1, total_rows, coarse), lambda f: (f, 0, 0)),
        scratch_shapes=[pltpu.VMEM((rows, coarse), jnp.bfloat16), pltpu.VMEM((rows, coarse), jnp.bfloat16)],
    )(fields3, main, halo_w, w)


def window_tables(blocks, count, full):
    smooth, deriv = line_matrices(full)
    coarse = full // 8
    out = []
    for at in range(blocks):
        base, width = window(at, count, coarse)
        picks = (base + np.arange(width)) % coarse
        part = slice(at * count, (at + 1) * count)
        out.append(np.stack([smooth[part][:, picks].T, deriv[part][:, picks].T]))
    return np.stack(out)


def pick_kernel(group_steps, step, chunk, owner_len, pack):
    def body(idx_ref, x_ref, sel_ref, o_ref, tab_ref, buf_ref):
        j = pl.program_id(0)
        rows = x_ref.shape[0]
        lanes = x_ref.shape[2]
        width = tab_ref.shape[1]

        @pl.when(j < group_steps)
        def _():
            for t in range(step):
                parts = [x_ref[:, t * pack + k, :] for k in range(pack)]
                parts.append(jnp.zeros((width - rows * pack, lanes), x_ref.dtype))
                slab = jnp.concatenate(parts, axis=0)
                at = pl.multiple_of((j * step + t) * lanes, lanes)
                tab_ref[pl.ds(at, lanes), :] = slab.T

        @pl.when(j == group_steps - 1)
        def _():
            tail = tab_ref.shape[0] - 8
            tab_ref[pl.ds(tail, 8), :] = jnp.zeros((8, width), tab_ref.dtype)

        @pl.when(j >= group_steps)
        def _():
            base = (j - group_steps) * chunk

            def one(e, carry):
                at = idx_ref[base + e]
                buf_ref[pl.ds(e, 1), :] = tab_ref[pl.ds(at, 1), :]
                return carry

            lax.fori_loop(0, chunk, one, 0, unroll=8)
            flipped = buf_ref[...].T
            sel = sel_ref[...]
            picked = flipped[:rows]
            for k in range(1, pack):
                picked = jnp.where(sel == k, flipped[k * rows:(k + 1) * rows], picked)
            for owner in range(chunk // owner_len):
                o_ref[owner] = picked[:, owner * owner_len:(owner + 1) * owner_len]

    return body


def pick_cells(x, flat, sel, owner_len, pack, chunk=2048):
    rows, groups, lanes = x.shape
    step = 8
    group_steps = groups // (step * pack)
    entries = flat.shape[0]
    chunk = min(chunk, entries)
    width = -(-(rows * pack) // 128) * 128
    per_chunk = chunk // owner_len
    grid_spec = pltpu.PrefetchScalarGridSpec(
        num_scalar_prefetch=1,
        grid=(group_steps + entries // chunk,),
        in_specs=[
            pl.BlockSpec((rows, step * pack, lanes), lambda j, idx: (0, jnp.minimum(j, group_steps - 1), 0)),
            pl.BlockSpec((1, chunk), lambda j, idx: (0, jnp.maximum(j - group_steps, 0))),
        ],
        out_specs=pl.BlockSpec((per_chunk, rows, owner_len), lambda j, idx: (jnp.maximum(j - group_steps, 0), 0, 0)),
        scratch_shapes=[pltpu.VMEM((groups // pack * lanes + 8, width), x.dtype), pltpu.VMEM((chunk, width), x.dtype)],
    )
    return pl.pallas_call(
        pick_kernel(group_steps, step, chunk, owner_len, pack),
        out_shape=jax.ShapeDtypeStruct((entries // owner_len, rows, owner_len), x.dtype),
        grid_spec=grid_spec,
    )(flat, x, sel)


def model_tensors(coarse):
    values = coarse.astype(jnp.float32)
    points = values.shape[-1]
    values = values.reshape(values.shape[0] // 3, 3, points)
    velocity = values[:3]
    species = values[3:]
    stress = [
        jnp.sum(velocity[first_comp] * velocity[second_comp], axis=0)
        for first_comp, second_comp in upper_pairs
    ]
    species_flux = jnp.sum(species[:, None, :, :] * velocity[None, :, :, :], axis=2)
    joined = jnp.concatenate([jnp.stack(stress, axis=0), species_flux.reshape(-1, points)], axis=0)
    return (model_coeff * joined).astype(jnp.bfloat16)


def window(at, count, coarse):
    reach = (count + 19) // 8 + 4
    if count % 8 or reach >= coarse:
        return 0, coarse
    return at * (count // 8) - 3, reach


def make_shards(row_count, col_count):
    def shards(fields, front_cells):
        field_count, local_x, local_y, z_length = fields.shape
        devices = row_count * col_count
        full_x = local_x * row_count
        full_y = local_y * col_count
        coarse_x = full_x // 8
        coarse_y = full_y // 8
        coarse_z = z_length // 8
        slab = coarse_z // devices
        slots = front_cells.shape[2]
        row = lax.axis_index("rows")
        col = lax.axis_index("cols")
        me = row * col_count + col

        copies = jnp.broadcast_to(front_cells, (devices,) + front_cells.shape[1:])
        every_cell = lax.all_to_all(copies, ("rows", "cols"), split_axis=0, concat_axis=0, tiled=True)

        x_base, x_count = window(row, local_x, coarse_x)
        y_base, y_count = window(col, local_y, coarse_y)
        wx = jnp.asarray(window_tables(row_count, local_x, full_x))[row]
        wy = jnp.asarray(window_tables(col_count, local_y, full_y))[col]
        group = x_count * y_count
        pack = 3
        padded = -(-group // (8 * pack)) * 8 * pack
        xs = jnp.stack([wx[1], wx[0], wx[0]])
        ys = jnp.stack([wy[0], wy[1], wy[0]])
        weights = xs[:, :, None, :, None] * ys[:, None, :, None, :]
        weights = weights.reshape(3, group, local_x * local_y)
        weights = jnp.pad(weights, ((0, 0), (0, padded - group), (0, 0))).reshape(3 * padded, -1)
        fields3 = fields.reshape(field_count, local_x * local_y, z_length)
        partials = filtered_partials(fields3, weights)

        by_owner = jnp.transpose(every_cell, (1, 0, 2))
        holder = lax.broadcasted_iota(jnp.int32, by_owner.shape, 1)
        clipped = jnp.clip(by_owner, 0, coarse_x * coarse_y * slab - 1)
        cell_pq = clipped // slab
        at_z = holder * slab + clipped % slab
        at_x = (cell_pq // coarse_y - x_base) % coarse_x
        at_y = (cell_pq % coarse_y - y_base) % coarse_y
        inside = (at_x < x_count) & (at_y < y_count) & (by_owner >= 0)
        at_group = at_x * y_count + at_y
        flat = jnp.where(inside, (at_group // pack) * coarse_z + at_z, padded // pack * coarse_z)
        sel = jnp.where(inside, at_group % pack, 0).reshape(1, -1)
        owner_len = devices * slots
        partials = partials.reshape(field_count * 3, padded, coarse_z)
        taken = pick_cells(partials, flat.reshape(-1), sel, owner_len, pack)
        arrived = lax.all_to_all(taken, ("rows", "cols"), split_axis=0, concat_axis=0, tiled=True)
        summed = jnp.sum(arrived, axis=0)
        rounded = lax.reduce_precision(summed, exponent_bits=8, mantissa_bits=7)
        mine = lax.dynamic_index_in_dim(by_owner, me, axis=0, keepdims=False).reshape(-1)
        picked = jnp.where(mine[None, :] >= 0, rounded, jnp.zeros_like(rounded))
        return model_tensors(picked)[None]

    return shards


def solution(mesh):
    in_specs = (P(None, "rows", "cols", None), P(("rows", "cols"), None, None))
    out_specs = P(("rows", "cols"), None, None)
    shards = make_shards(mesh.shape["rows"], mesh.shape["cols"])
    return jax.shard_map(shards, mesh=mesh, in_specs=in_specs, out_specs=out_specs, check_vma=False)
```

```python
import numpy as np
import jax
import jax.numpy as jnp
import ml_dtypes
from jax import lax
from jax.sharding import PartitionSpec as P
from jax.experimental import pallas as pl
from jax.experimental.pallas import tpu as pltpu

first_tap = -20
last_tap = 27
sigma_sq = 256.0 / 12.0
coarse_step = 8.0
model_coeff = 1.0 / 3.0
upper_pairs = ((0, 0), (0, 1), (0, 2), (1, 1), (1, 2), (2, 2))
block_len = 1024
halo = 128


def tap_weights(offsets):
    f32 = np.float32
    every_tap = np.arange(first_tap, last_tap + 1).astype(f32)
    weight_sum = np.sum(np.exp(-(every_tap - f32(3.5)) * (every_tap - f32(3.5)) / f32(2.0 * sigma_sq)), dtype=f32)
    shifted = offsets.astype(f32) - f32(3.5)
    inside = (offsets >= first_tap) & (offsets <= last_tap)
    gauss = np.where(inside, np.exp(-shifted * shifted / f32(2.0 * sigma_sq)), f32(0.0)).astype(f32) / weight_sum
    slope = (f32(-coarse_step) * shifted / f32(sigma_sq) * gauss).astype(f32)
    bf = ml_dtypes.bfloat16
    return gauss.astype(bf).astype(f32), slope.astype(bf).astype(f32)


def line_matrices(length):
    fine_pos = np.arange(length)[:, None]
    coarse_pos = np.arange(length // 8)[None, :]
    offsets = np.mod(fine_pos - 8 * coarse_pos, length)
    offsets = np.where(offsets >= length // 2, offsets - length, offsets)
    return tap_weights(offsets)


def z_tables(length):
    coarse = np.arange(length // 8)[None, :]
    main = np.arange(length)[:, None] - 8 * coarse
    prev = np.arange(halo)[:, None] - halo - 8 * coarse
    nxt = np.arange(halo)[:, None] + length - 8 * coarse
    return [tap_weights(o) for o in (main, prev, nxt)]


def filter_kernel(block_count, coarse_block, value_rows, slope_rows):
    def body(x_ref, main_ref, halo_ref, w_ref, o_ref, zv_ref, zs_ref):
        per_step, rows, length = x_ref.shape
        blen = length // block_count
        for b in range(block_count):
            main = x_ref[:, :, b * blen:(b + 1) * blen].reshape(per_step * rows, blen)
            start = (b * blen - halo) % length
            tail = x_ref[:, :, start:start + halo].reshape(per_step * rows, halo)
            start = ((b + 1) * blen) % length
            head = x_ref[:, :, start:start + halo].reshape(per_step * rows, halo)
            edges = jnp.concatenate([tail, head], axis=1)
            acc = jnp.dot(main, main_ref[...], preferred_element_type=jnp.float32)
            acc = acc + jnp.dot(edges, halo_ref[...], preferred_element_type=jnp.float32)
            lanes = slice(b * coarse_block, (b + 1) * coarse_block)
            zv_ref[:, lanes] = acc[:, :coarse_block].astype(jnp.bfloat16)
            zs_ref[:, lanes] = acc[:, coarse_block:].astype(jnp.bfloat16)
        for k in range(per_step):
            zv = zv_ref[k * rows:(k + 1) * rows, :]
            zs = zs_ref[k * rows:(k + 1) * rows, :]
            pv = jnp.dot(w_ref[0, :value_rows, :], zv, preferred_element_type=jnp.float32)
            pv = pv + jnp.dot(w_ref[1, :value_rows, :], zv, preferred_element_type=jnp.float32)
            ps = jnp.dot(w_ref[0, value_rows:, :], zs, preferred_element_type=jnp.float32)
            ps = ps + jnp.dot(w_ref[1, value_rows:, :], zs, preferred_element_type=jnp.float32)
            o_ref[k, :value_rows, :] = pv
            o_ref[k, value_rows:, :] = ps

    return body


def split_hi_lo(w):
    hi = w.astype(jnp.bfloat16)
    lo = (w - hi.astype(jnp.float32)).astype(jnp.bfloat16)
    return jnp.stack([hi, lo], axis=0)


def filtered_partials(fields3, weights):
    field_count, rows, length = fields3.shape
    blen = block_len if (length % block_len == 0 and length > block_len) else length
    block_count = length // blen
    coarse_block = blen // 8
    tables = z_tables(blen)
    joined = [np.concatenate([t[0], t[1]], axis=1) for t in tables]
    main = jnp.asarray(joined[0], jnp.bfloat16)
    halo_w = jnp.asarray(np.concatenate([joined[1], joined[2]], axis=0), jnp.bfloat16)
    w = split_hi_lo(weights)
    total_rows = w.shape[1]
    value_rows = total_rows // 3 * 2
    coarse = length // 8
    per_step = 2 if field_count % 2 == 0 else 1
    const = lambda f: (0, 0)
    return pl.pallas_call(
        filter_kernel(block_count, coarse_block, value_rows, total_rows - value_rows),
        out_shape=jax.ShapeDtypeStruct((field_count, total_rows, coarse), jnp.float32),
        grid=(field_count // per_step,),
        in_specs=[
            pl.BlockSpec((per_step, rows, length), lambda f: (f, 0, 0)),
            pl.BlockSpec(main.shape, const),
            pl.BlockSpec(halo_w.shape, const),
            pl.BlockSpec(w.shape, lambda f: (0, 0, 0)),
        ],
        out_specs=pl.BlockSpec((per_step, total_rows, coarse), lambda f: (f, 0, 0)),
        scratch_shapes=[pltpu.VMEM((per_step * rows, coarse), jnp.bfloat16)] * 2,
    )(fields3, main, halo_w, w)


def window_tables(blocks, count, full):
    smooth, deriv = line_matrices(full)
    coarse = full // 8
    out = []
    for at in range(blocks):
        base, width = window(at, count, coarse)
        picks = (base + np.arange(width)) % coarse
        part = slice(at * count, (at + 1) * count)
        out.append(np.stack([smooth[part][:, picks].T, deriv[part][:, picks].T]))
    return np.stack(out)


def pick_kernel(group_steps, step, chunk, owner_len, pack):
    def body(idx_ref, x_ref, sel_ref, o_ref, tab_ref, buf_ref):
        j = pl.program_id(0)
        rows = x_ref.shape[0]
        lanes = x_ref.shape[2]
        width = tab_ref.shape[1]

        @pl.when(j < group_steps)
        def _():
            for t in range(step):
                parts = [x_ref[:, t * pack + k, :] for k in range(pack)]
                parts.append(jnp.zeros((width - rows * pack, lanes), x_ref.dtype))
                slab = jnp.concatenate(parts, axis=0)
                at = pl.multiple_of((j * step + t) * lanes, lanes)
                tab_ref[pl.ds(at, lanes), :] = slab.T

        @pl.when(j == group_steps - 1)
        def _():
            tail = tab_ref.shape[0] - 8
            tab_ref[pl.ds(tail, 8), :] = jnp.zeros((8, width), tab_ref.dtype)

        @pl.when(j >= group_steps)
        def _():
            base = (j - group_steps) * chunk

            def one(e, carry):
                at = idx_ref[base + e]
                buf_ref[pl.ds(e, 1), :] = tab_ref[pl.ds(at, 1), :]
                return carry

            lax.fori_loop(0, chunk, one, 0, unroll=8)
            flipped = buf_ref[...].T
            sel = sel_ref[...]
            picked = flipped[:rows]
            for k in range(1, pack):
                picked = jnp.where(sel == k, flipped[k * rows:(k + 1) * rows], picked)
            for owner in range(chunk // owner_len):
                o_ref[owner] = picked[:, owner * owner_len:(owner + 1) * owner_len]

    return body


def pick_cells(x, flat, sel, owner_len, pack, chunk=2048):
    rows, groups, lanes = x.shape
    step = 8
    group_steps = groups // (step * pack)
    entries = flat.shape[0]
    chunk = min(chunk, entries)
    width = -(-(rows * pack) // 128) * 128
    per_chunk = chunk // owner_len
    grid_spec = pltpu.PrefetchScalarGridSpec(
        num_scalar_prefetch=1,
        grid=(group_steps + entries // chunk,),
        in_specs=[
            pl.BlockSpec((rows, step * pack, lanes), lambda j, idx: (0, jnp.minimum(j, group_steps - 1), 0)),
            pl.BlockSpec((1, chunk), lambda j, idx: (0, jnp.maximum(j - group_steps, 0))),
        ],
        out_specs=pl.BlockSpec((per_chunk, rows, owner_len), lambda j, idx: (jnp.maximum(j - group_steps, 0), 0, 0)),
        scratch_shapes=[pltpu.VMEM((groups // pack * lanes + 8, width), x.dtype), pltpu.VMEM((chunk, width), x.dtype)],
    )
    return pl.pallas_call(
        pick_kernel(group_steps, step, chunk, owner_len, pack),
        out_shape=jax.ShapeDtypeStruct((entries // owner_len, rows, owner_len), x.dtype),
        grid_spec=grid_spec,
    )(flat, x, sel)


def model_tensors(coarse):
    values = coarse.astype(jnp.float32)
    points = values.shape[-1]
    values = values.reshape(values.shape[0] // 3, 3, points)
    velocity = values[:3]
    species = values[3:]
    stress = [
        jnp.sum(velocity[first_comp] * velocity[second_comp], axis=0)
        for first_comp, second_comp in upper_pairs
    ]
    species_flux = jnp.sum(species[:, None, :, :] * velocity[None, :, :, :], axis=2)
    joined = jnp.concatenate([jnp.stack(stress, axis=0), species_flux.reshape(-1, points)], axis=0)
    return (model_coeff * joined).astype(jnp.bfloat16)


def window(at, count, coarse):
    reach = (count + 19) // 8 + 4
    if count % 8 or reach >= coarse:
        return 0, coarse
    return at * (count // 8) - 3, reach


def make_shards(row_count, col_count):
    def shards(fields, front_cells):
        field_count, local_x, local_y, z_length = fields.shape
        devices = row_count * col_count
        full_x = local_x * row_count
        full_y = local_y * col_count
        coarse_x = full_x // 8
        coarse_y = full_y // 8
        coarse_z = z_length // 8
        slab = coarse_z // devices
        slots = front_cells.shape[2]
        row = lax.axis_index("rows")
        col = lax.axis_index("cols")
        me = row * col_count + col

        copies = jnp.broadcast_to(front_cells, (devices,) + front_cells.shape[1:])
        every_cell = lax.all_to_all(copies, ("rows", "cols"), split_axis=0, concat_axis=0, tiled=True)

        x_base, x_count = window(row, local_x, coarse_x)
        y_base, y_count = window(col, local_y, coarse_y)
        wx = jnp.asarray(window_tables(row_count, local_x, full_x))[row]
        wy = jnp.asarray(window_tables(col_count, local_y, full_y))[col]
        group = x_count * y_count
        pack = 3
        padded = -(-group // (8 * pack)) * 8 * pack
        xs = jnp.stack([wx[1], wx[0], wx[0]])
        ys = jnp.stack([wy[0], wy[1], wy[0]])
        weights = xs[:, :, None, :, None] * ys[:, None, :, None, :]
        weights = weights.reshape(3, group, local_x * local_y)
        weights = jnp.pad(weights, ((0, 0), (0, padded - group), (0, 0))).reshape(3 * padded, -1)
        fields3 = fields.reshape(field_count, local_x * local_y, z_length)
        partials = filtered_partials(fields3, weights)

        by_owner = jnp.transpose(every_cell, (1, 0, 2))
        holder = lax.broadcasted_iota(jnp.int32, by_owner.shape, 1)
        clipped = jnp.clip(by_owner, 0, coarse_x * coarse_y * slab - 1)
        cell_pq = clipped // slab
        at_z = holder * slab + clipped % slab
        at_x = (cell_pq // coarse_y - x_base) % coarse_x
        at_y = (cell_pq % coarse_y - y_base) % coarse_y
        inside = (at_x < x_count) & (at_y < y_count) & (by_owner >= 0)
        at_group = at_x * y_count + at_y
        flat = jnp.where(inside, (at_group // pack) * coarse_z + at_z, padded // pack * coarse_z)
        sel = jnp.where(inside, at_group % pack, 0).reshape(1, -1)
        owner_len = devices * slots
        partials = partials.reshape(field_count * 3, padded, coarse_z)
        taken = pick_cells(partials, flat.reshape(-1), sel, owner_len, pack)
        arrived = lax.all_to_all(taken, ("rows", "cols"), split_axis=0, concat_axis=0, tiled=True)
        summed = jnp.sum(arrived, axis=0)
        rounded = lax.reduce_precision(summed, exponent_bits=8, mantissa_bits=7)
        mine = lax.dynamic_index_in_dim(by_owner, me, axis=0, keepdims=False).reshape(-1)
        picked = jnp.where(mine[None, :] >= 0, rounded, jnp.zeros_like(rounded))
        return model_tensors(picked)[None]

    return shards


def solution(mesh):
    in_specs = (P(None, "rows", "cols", None), P(("rows", "cols"), None, None))
    out_specs = P(("rows", "cols"), None, None)
    shards = make_shards(mesh.shape["rows"], mesh.shape["cols"])
    return jax.shard_map(shards, mesh=mesh, in_specs=in_specs, out_specs=out_specs, check_vma=False)
```

```python
import numpy as np
import jax
import jax.numpy as jnp
import ml_dtypes
from jax import lax
from jax.sharding import PartitionSpec as P
from jax.experimental import pallas as pl
from jax.experimental.pallas import tpu as pltpu

first_tap = -20
last_tap = 27
sigma_sq = 256.0 / 12.0
coarse_step = 8.0
model_coeff = 1.0 / 3.0
upper_pairs = ((0, 0), (0, 1), (0, 2), (1, 1), (1, 2), (2, 2))
block_len = 1024
halo = 128


def tap_weights(offsets):
    f32 = np.float32
    every_tap = np.arange(first_tap, last_tap + 1).astype(f32)
    weight_sum = np.sum(np.exp(-(every_tap - f32(3.5)) * (every_tap - f32(3.5)) / f32(2.0 * sigma_sq)), dtype=f32)
    shifted = offsets.astype(f32) - f32(3.5)
    inside = (offsets >= first_tap) & (offsets <= last_tap)
    gauss = np.where(inside, np.exp(-shifted * shifted / f32(2.0 * sigma_sq)), f32(0.0)).astype(f32) / weight_sum
    slope = (f32(-coarse_step) * shifted / f32(sigma_sq) * gauss).astype(f32)
    bf = ml_dtypes.bfloat16
    return gauss.astype(bf).astype(f32), slope.astype(bf).astype(f32)


def line_matrices(length):
    fine_pos = np.arange(length)[:, None]
    coarse_pos = np.arange(length // 8)[None, :]
    offsets = np.mod(fine_pos - 8 * coarse_pos, length)
    offsets = np.where(offsets >= length // 2, offsets - length, offsets)
    return tap_weights(offsets)


def z_tables(length):
    coarse = np.arange(length // 8)[None, :]
    main = np.arange(length)[:, None] - 8 * coarse
    prev = np.arange(halo)[:, None] - halo - 8 * coarse
    nxt = np.arange(halo)[:, None] + length - 8 * coarse
    return [tap_weights(o) for o in (main, prev, nxt)]


def filter_kernel(block_count, coarse_block, value_rows, slope_rows):
    def body(x_ref, main_ref, halo_ref, w_ref, o_ref, zv_ref, zs_ref):
        per_step, rows, length = x_ref.shape
        blen = length // block_count
        for b in range(block_count):
            main = x_ref[:, :, b * blen:(b + 1) * blen].reshape(per_step * rows, blen)
            start = (b * blen - halo) % length
            tail = x_ref[:, :, start:start + halo].reshape(per_step * rows, halo)
            start = ((b + 1) * blen) % length
            head = x_ref[:, :, start:start + halo].reshape(per_step * rows, halo)
            edges = jnp.concatenate([tail, head], axis=1)
            acc = jnp.dot(main, main_ref[...], preferred_element_type=jnp.float32)
            acc = acc + jnp.dot(edges, halo_ref[...], preferred_element_type=jnp.float32)
            lanes = slice(b * coarse_block, (b + 1) * coarse_block)
            zv_ref[:, lanes] = acc[:, :coarse_block].astype(jnp.bfloat16)
            zs_ref[:, lanes] = acc[:, coarse_block:].astype(jnp.bfloat16)
        for k in range(per_step):
            zv = zv_ref[k * rows:(k + 1) * rows, :]
            zs = zs_ref[k * rows:(k + 1) * rows, :]
            pv = jnp.dot(w_ref[0, :value_rows, :], zv, preferred_element_type=jnp.float32)
            pv = pv + jnp.dot(w_ref[1, :value_rows, :], zv, preferred_element_type=jnp.float32)
            ps = jnp.dot(w_ref[0, value_rows:, :], zs, preferred_element_type=jnp.float32)
            ps = ps + jnp.dot(w_ref[1, value_rows:, :], zs, preferred_element_type=jnp.float32)
            o_ref[k, :value_rows, :] = pv
            o_ref[k, value_rows:, :] = ps

    return body


def split_hi_lo(w):
    hi = w.astype(jnp.bfloat16)
    lo = (w - hi.astype(jnp.float32)).astype(jnp.bfloat16)
    return jnp.stack([hi, lo], axis=0)


def filtered_partials(fields3, weights):
    field_count, rows, length = fields3.shape
    blen = block_len if (length % block_len == 0 and length > block_len) else length
    block_count = length // blen
    coarse_block = blen // 8
    tables = z_tables(blen)
    joined = [np.concatenate([t[0], t[1]], axis=1) for t in tables]
    main = jnp.asarray(joined[0], jnp.bfloat16)
    halo_w = jnp.asarray(np.concatenate([joined[1], joined[2]], axis=0), jnp.bfloat16)
    w = split_hi_lo(weights)
    total_rows = w.shape[1]
    value_rows = total_rows // 3 * 2
    coarse = length // 8
    per_step = 4 if field_count % 4 == 0 else 1
    const = lambda f: (0, 0)
    return pl.pallas_call(
        filter_kernel(block_count, coarse_block, value_rows, total_rows - value_rows),
        out_shape=jax.ShapeDtypeStruct((field_count, total_rows, coarse), jnp.float32),
        grid=(field_count // per_step,),
        in_specs=[
            pl.BlockSpec((per_step, rows, length), lambda f: (f, 0, 0)),
            pl.BlockSpec(main.shape, const),
            pl.BlockSpec(halo_w.shape, const),
            pl.BlockSpec(w.shape, lambda f: (0, 0, 0)),
        ],
        out_specs=pl.BlockSpec((per_step, total_rows, coarse), lambda f: (f, 0, 0)),
        scratch_shapes=[pltpu.VMEM((per_step * rows, coarse), jnp.bfloat16)] * 2,
    )(fields3, main, halo_w, w)


def window_tables(blocks, count, full):
    smooth, deriv = line_matrices(full)
    coarse = full // 8
    out = []
    for at in range(blocks):
        base, width = window(at, count, coarse)
        picks = (base + np.arange(width)) % coarse
        part = slice(at * count, (at + 1) * count)
        out.append(np.stack([smooth[part][:, picks].T, deriv[part][:, picks].T]))
    return np.stack(out)


def pick_kernel(group_steps, step, chunk, owner_len, pack):
    def body(idx_ref, x_ref, sel_ref, o_ref, tab_ref, buf_ref):
        j = pl.program_id(0)
        rows = x_ref.shape[0]
        lanes = x_ref.shape[2]
        width = tab_ref.shape[1]

        @pl.when(j < group_steps)
        def _():
            for t in range(step):
                parts = [x_ref[:, t * pack + k, :] for k in range(pack)]
                parts.append(jnp.zeros((width - rows * pack, lanes), x_ref.dtype))
                slab = jnp.concatenate(parts, axis=0)
                at = pl.multiple_of((j * step + t) * lanes, lanes)
                tab_ref[pl.ds(at, lanes), :] = slab.T

        @pl.when(j == group_steps - 1)
        def _():
            tail = tab_ref.shape[0] - 8
            tab_ref[pl.ds(tail, 8), :] = jnp.zeros((8, width), tab_ref.dtype)

        @pl.when(j >= group_steps)
        def _():
            base = (j - group_steps) * chunk

            def one(e, carry):
                at = idx_ref[base + e]
                buf_ref[pl.ds(e, 1), :] = tab_ref[pl.ds(at, 1), :]
                return carry

            lax.fori_loop(0, chunk, one, 0, unroll=8)
            flipped = buf_ref[...].T
            sel = sel_ref[...]
            picked = flipped[:rows]
            for k in range(1, pack):
                picked = jnp.where(sel == k, flipped[k * rows:(k + 1) * rows], picked)
            for owner in range(chunk // owner_len):
                o_ref[owner] = picked[:, owner * owner_len:(owner + 1) * owner_len]

    return body


def pick_cells(x, flat, sel, owner_len, pack, chunk=2048):
    rows, groups, lanes = x.shape
    step = 8
    group_steps = groups // (step * pack)
    entries = flat.shape[0]
    chunk = min(chunk, entries)
    width = -(-(rows * pack) // 128) * 128
    per_chunk = chunk // owner_len
    grid_spec = pltpu.PrefetchScalarGridSpec(
        num_scalar_prefetch=1,
        grid=(group_steps + entries // chunk,),
        in_specs=[
            pl.BlockSpec((rows, step * pack, lanes), lambda j, idx: (0, jnp.minimum(j, group_steps - 1), 0)),
            pl.BlockSpec((1, chunk), lambda j, idx: (0, jnp.maximum(j - group_steps, 0))),
        ],
        out_specs=pl.BlockSpec((per_chunk, rows, owner_len), lambda j, idx: (jnp.maximum(j - group_steps, 0), 0, 0)),
        scratch_shapes=[pltpu.VMEM((groups // pack * lanes + 8, width), x.dtype), pltpu.VMEM((chunk, width), x.dtype)],
    )
    return pl.pallas_call(
        pick_kernel(group_steps, step, chunk, owner_len, pack),
        out_shape=jax.ShapeDtypeStruct((entries // owner_len, rows, owner_len), x.dtype),
        grid_spec=grid_spec,
    )(flat, x, sel)


def model_tensors(coarse):
    values = coarse.astype(jnp.float32)
    points = values.shape[-1]
    values = values.reshape(values.shape[0] // 3, 3, points)
    velocity = values[:3]
    species = values[3:]
    stress = [
        jnp.sum(velocity[first_comp] * velocity[second_comp], axis=0)
        for first_comp, second_comp in upper_pairs
    ]
    species_flux = jnp.sum(species[:, None, :, :] * velocity[None, :, :, :], axis=2)
    joined = jnp.concatenate([jnp.stack(stress, axis=0), species_flux.reshape(-1, points)], axis=0)
    return (model_coeff * joined).astype(jnp.bfloat16)


def window(at, count, coarse):
    reach = (count + 19) // 8 + 4
    if count % 8 or reach >= coarse:
        return 0, coarse
    return at * (count // 8) - 3, reach


def make_shards(row_count, col_count):
    def shards(fields, front_cells):
        field_count, local_x, local_y, z_length = fields.shape
        devices = row_count * col_count
        full_x = local_x * row_count
        full_y = local_y * col_count
        coarse_x = full_x // 8
        coarse_y = full_y // 8
        coarse_z = z_length // 8
        slab = coarse_z // devices
        slots = front_cells.shape[2]
        row = lax.axis_index("rows")
        col = lax.axis_index("cols")
        me = row * col_count + col

        copies = jnp.broadcast_to(front_cells, (devices,) + front_cells.shape[1:])
        every_cell = lax.all_to_all(copies, ("rows", "cols"), split_axis=0, concat_axis=0, tiled=True)

        x_base, x_count = window(row, local_x, coarse_x)
        y_base, y_count = window(col, local_y, coarse_y)
        wx = jnp.asarray(window_tables(row_count, local_x, full_x))[row]
        wy = jnp.asarray(window_tables(col_count, local_y, full_y))[col]
        group = x_count * y_count
        pack = 3
        padded = -(-group // (8 * pack)) * 8 * pack
        xs = jnp.stack([wx[1], wx[0], wx[0]])
        ys = jnp.stack([wy[0], wy[1], wy[0]])
        weights = xs[:, :, None, :, None] * ys[:, None, :, None, :]
        weights = weights.reshape(3, group, local_x * local_y)
        weights = jnp.pad(weights, ((0, 0), (0, padded - group), (0, 0))).reshape(3 * padded, -1)
        fields3 = fields.reshape(field_count, local_x * local_y, z_length)
        partials = filtered_partials(fields3, weights)

        by_owner = jnp.transpose(every_cell, (1, 0, 2))
        holder = lax.broadcasted_iota(jnp.int32, by_owner.shape, 1)
        clipped = jnp.clip(by_owner, 0, coarse_x * coarse_y * slab - 1)
        cell_pq = clipped // slab
        at_z = holder * slab + clipped % slab
        at_x = (cell_pq // coarse_y - x_base) % coarse_x
        at_y = (cell_pq % coarse_y - y_base) % coarse_y
        inside = (at_x < x_count) & (at_y < y_count) & (by_owner >= 0)
        at_group = at_x * y_count + at_y
        flat = jnp.where(inside, (at_group // pack) * coarse_z + at_z, padded // pack * coarse_z)
        sel = jnp.where(inside, at_group % pack, 0).reshape(1, -1)
        owner_len = devices * slots
        partials = partials.reshape(field_count * 3, padded, coarse_z)
        taken = pick_cells(partials, flat.reshape(-1), sel, owner_len, pack)
        arrived = lax.all_to_all(taken, ("rows", "cols"), split_axis=0, concat_axis=0, tiled=True)
        summed = jnp.sum(arrived, axis=0)
        rounded = lax.reduce_precision(summed, exponent_bits=8, mantissa_bits=7)
        mine = lax.dynamic_index_in_dim(by_owner, me, axis=0, keepdims=False).reshape(-1)
        picked = jnp.where(mine[None, :] >= 0, rounded, jnp.zeros_like(rounded))
        return model_tensors(picked)[None]

    return shards


def solution(mesh):
    in_specs = (P(None, "rows", "cols", None), P(("rows", "cols"), None, None))
    out_specs = P(("rows", "cols"), None, None)
    shards = make_shards(mesh.shape["rows"], mesh.shape["cols"])
    return jax.shard_map(shards, mesh=mesh, in_specs=in_specs, out_specs=out_specs, check_vma=False)
```

```python
import numpy as np
import jax
import jax.numpy as jnp
import ml_dtypes
from jax import lax
from jax.sharding import PartitionSpec as P
from jax.experimental import pallas as pl
from jax.experimental.pallas import tpu as pltpu

first_tap = -20
last_tap = 27
sigma_sq = 256.0 / 12.0
coarse_step = 8.0
model_coeff = 1.0 / 3.0
upper_pairs = ((0, 0), (0, 1), (0, 2), (1, 1), (1, 2), (2, 2))
block_len = 1024
halo = 128


def tap_weights(offsets):
    f32 = np.float32
    every_tap = np.arange(first_tap, last_tap + 1).astype(f32)
    weight_sum = np.sum(np.exp(-(every_tap - f32(3.5)) * (every_tap - f32(3.5)) / f32(2.0 * sigma_sq)), dtype=f32)
    shifted = offsets.astype(f32) - f32(3.5)
    inside = (offsets >= first_tap) & (offsets <= last_tap)
    gauss = np.where(inside, np.exp(-shifted * shifted / f32(2.0 * sigma_sq)), f32(0.0)).astype(f32) / weight_sum
    slope = (f32(-coarse_step) * shifted / f32(sigma_sq) * gauss).astype(f32)
    bf = ml_dtypes.bfloat16
    return gauss.astype(bf).astype(f32), slope.astype(bf).astype(f32)


def line_matrices(length):
    fine_pos = np.arange(length)[:, None]
    coarse_pos = np.arange(length // 8)[None, :]
    offsets = np.mod(fine_pos - 8 * coarse_pos, length)
    offsets = np.where(offsets >= length // 2, offsets - length, offsets)
    return tap_weights(offsets)


def z_tables(length):
    coarse = np.arange(length // 8)[None, :]
    main = np.arange(length)[:, None] - 8 * coarse
    prev = np.arange(halo)[:, None] - halo - 8 * coarse
    nxt = np.arange(halo)[:, None] + length - 8 * coarse
    return [tap_weights(o) for o in (main, prev, nxt)]


def filter_kernel(block_count, coarse_block, value_rows, slope_rows):
    def body(x_ref, main_ref, halo_ref, w_ref, o_ref, zv_ref, zs_ref):
        per_step, rows, length = x_ref.shape
        blen = length // block_count
        for b in range(block_count):
            main = x_ref[:, :, b * blen:(b + 1) * blen].reshape(per_step * rows, blen)
            start = (b * blen - halo) % length
            tail = x_ref[:, :, start:start + halo].reshape(per_step * rows, halo)
            start = ((b + 1) * blen) % length
            head = x_ref[:, :, start:start + halo].reshape(per_step * rows, halo)
            edges = jnp.concatenate([tail, head], axis=1)
            acc = jnp.dot(main, main_ref[...], preferred_element_type=jnp.float32)
            acc = acc + jnp.dot(edges, halo_ref[...], preferred_element_type=jnp.float32)
            lanes = slice(b * coarse_block, (b + 1) * coarse_block)
            zv_ref[:, lanes] = acc[:, :coarse_block].astype(jnp.bfloat16)
            zs_ref[:, lanes] = acc[:, coarse_block:].astype(jnp.bfloat16)
        for k in range(per_step):
            zv = zv_ref[k * rows:(k + 1) * rows, :]
            zs = zs_ref[k * rows:(k + 1) * rows, :]
            pv = jnp.dot(w_ref[0, :value_rows, :], zv, preferred_element_type=jnp.float32)
            pv = pv + jnp.dot(w_ref[1, :value_rows, :], zv, preferred_element_type=jnp.float32)
            ps = jnp.dot(w_ref[0, value_rows:, :], zs, preferred_element_type=jnp.float32)
            ps = ps + jnp.dot(w_ref[1, value_rows:, :], zs, preferred_element_type=jnp.float32)
            o_ref[k, :value_rows, :] = pv
            o_ref[k, value_rows:, :] = ps

    return body


def split_hi_lo(w):
    hi = w.astype(jnp.bfloat16)
    lo = (w - hi.astype(jnp.float32)).astype(jnp.bfloat16)
    return jnp.stack([hi, lo], axis=0)


def filtered_partials(fields3, weights):
    field_count, rows, length = fields3.shape
    blen = block_len if (length % block_len == 0 and length > block_len) else length
    block_count = length // blen
    coarse_block = blen // 8
    tables = z_tables(blen)
    joined = [np.concatenate([t[0], t[1]], axis=1) for t in tables]
    main = jnp.asarray(joined[0], jnp.bfloat16)
    halo_w = jnp.asarray(np.concatenate([joined[1], joined[2]], axis=0), jnp.bfloat16)
    w = split_hi_lo(weights)
    total_rows = w.shape[1]
    value_rows = total_rows // 3 * 2
    coarse = length // 8
    per_step = 4 if field_count % 4 == 0 else 1
    const = lambda f: (0, 0)
    return pl.pallas_call(
        filter_kernel(block_count, coarse_block, value_rows, total_rows - value_rows),
        out_shape=jax.ShapeDtypeStruct((field_count, total_rows, coarse), jnp.float32),
        grid=(field_count // per_step,),
        in_specs=[
            pl.BlockSpec((per_step, rows, length), lambda f: (f, 0, 0)),
            pl.BlockSpec(main.shape, const),
            pl.BlockSpec(halo_w.shape, const),
            pl.BlockSpec(w.shape, lambda f: (0, 0, 0)),
        ],
        out_specs=pl.BlockSpec((per_step, total_rows, coarse), lambda f: (f, 0, 0)),
        scratch_shapes=[pltpu.VMEM((per_step * rows, coarse), jnp.bfloat16)] * 2,
    )(fields3, main, halo_w, w)


def window_tables(blocks, count, full):
    smooth, deriv = line_matrices(full)
    coarse = full // 8
    out = []
    for at in range(blocks):
        base, width = window(at, count, coarse)
        picks = (base + np.arange(width)) % coarse
        part = slice(at * count, (at + 1) * count)
        out.append(np.stack([smooth[part][:, picks].T, deriv[part][:, picks].T]))
    return np.stack(out)


def pick_kernel(group_steps, step, chunk, owner_len, pack):
    def body(idx_ref, x_ref, sel_ref, o_ref, tab_ref, buf_ref):
        j = pl.program_id(0)
        rows = x_ref.shape[0]
        lanes = x_ref.shape[2]
        width = tab_ref.shape[1]

        @pl.when(j < group_steps)
        def _():
            for t in range(step):
                parts = [x_ref[:, t * pack + k, :] for k in range(pack)]
                parts.append(jnp.zeros((width - rows * pack, lanes), x_ref.dtype))
                slab = jnp.concatenate(parts, axis=0)
                at = pl.multiple_of((j * step + t) * lanes, lanes)
                tab_ref[pl.ds(at, lanes), :] = slab.T

        @pl.when(j == group_steps - 1)
        def _():
            tail = tab_ref.shape[0] - 8
            tab_ref[pl.ds(tail, 8), :] = jnp.zeros((8, width), tab_ref.dtype)

        @pl.when(j >= group_steps)
        def _():
            base = (j - group_steps) * chunk

            def one(e, carry):
                at = idx_ref[base + e]
                buf_ref[pl.ds(e, 1), :] = tab_ref[pl.ds(at, 1), :]
                return carry

            lax.fori_loop(0, chunk, one, 0, unroll=8)
            flipped = buf_ref[...].T
            sel = sel_ref[...]
            picked = flipped[:rows]
            for k in range(1, pack):
                picked = jnp.where(sel == k, flipped[k * rows:(k + 1) * rows], picked)
            for owner in range(chunk // owner_len):
                o_ref[owner] = picked[:, owner * owner_len:(owner + 1) * owner_len]

    return body


def pick_cells(x, flat, sel, owner_len, pack, chunk=2048):
    rows, groups, lanes = x.shape
    step = 8
    group_steps = groups // (step * pack)
    entries = flat.shape[0]
    chunk = min(chunk, entries)
    width = -(-(rows * pack) // 128) * 128
    per_chunk = chunk // owner_len
    grid_spec = pltpu.PrefetchScalarGridSpec(
        num_scalar_prefetch=1,
        grid=(group_steps + entries // chunk,),
        in_specs=[
            pl.BlockSpec((rows, step * pack, lanes), lambda j, idx: (0, jnp.minimum(j, group_steps - 1), 0)),
            pl.BlockSpec((1, chunk), lambda j, idx: (0, jnp.maximum(j - group_steps, 0))),
        ],
        out_specs=pl.BlockSpec((per_chunk, rows, owner_len), lambda j, idx: (jnp.maximum(j - group_steps, 0), 0, 0)),
        scratch_shapes=[pltpu.VMEM((groups // pack * lanes + 8, width), x.dtype), pltpu.VMEM((chunk, width), x.dtype)],
    )
    return pl.pallas_call(
        pick_kernel(group_steps, step, chunk, owner_len, pack),
        out_shape=jax.ShapeDtypeStruct((entries // owner_len, rows, owner_len), x.dtype),
        grid_spec=grid_spec,
    )(flat, x, sel)


def model_tensors(coarse):
    values = coarse.astype(jnp.float32)
    points = values.shape[-1]
    values = values.reshape(values.shape[0] // 3, 3, points)
    velocity = values[:3]
    species = values[3:]
    stress = [
        jnp.sum(velocity[first_comp] * velocity[second_comp], axis=0)
        for first_comp, second_comp in upper_pairs
    ]
    species_flux = jnp.sum(species[:, None, :, :] * velocity[None, :, :, :], axis=2)
    joined = jnp.concatenate([jnp.stack(stress, axis=0), species_flux.reshape(-1, points)], axis=0)
    return (model_coeff * joined).astype(jnp.bfloat16)


def window(at, count, coarse):
    reach = (count + 19) // 8 + 4
    if count % 8 or reach >= coarse:
        return 0, coarse
    return at * (count // 8) - 3, reach


def make_shards(row_count, col_count):
    def shards(fields, front_cells):
        field_count, local_x, local_y, z_length = fields.shape
        devices = row_count * col_count
        full_x = local_x * row_count
        full_y = local_y * col_count
        coarse_x = full_x // 8
        coarse_y = full_y // 8
        coarse_z = z_length // 8
        slab = coarse_z // devices
        slots = front_cells.shape[2]
        row = lax.axis_index("rows")
        col = lax.axis_index("cols")
        me = row * col_count + col

        copies = jnp.broadcast_to(front_cells, (devices,) + front_cells.shape[1:])
        every_cell = lax.all_to_all(copies, ("rows", "cols"), split_axis=0, concat_axis=0, tiled=True)

        x_base, x_count = window(row, local_x, coarse_x)
        y_base, y_count = window(col, local_y, coarse_y)
        wx = jnp.asarray(window_tables(row_count, local_x, full_x))[row]
        wy = jnp.asarray(window_tables(col_count, local_y, full_y))[col]
        group = x_count * y_count
        pack = 3
        padded = -(-group // (8 * pack)) * 8 * pack
        xs = jnp.stack([wx[1], wx[0], wx[0]])
        ys = jnp.stack([wy[0], wy[1], wy[0]])
        weights = xs[:, :, None, :, None] * ys[:, None, :, None, :]
        weights = weights.reshape(3, group, local_x * local_y)
        weights = jnp.pad(weights, ((0, 0), (0, padded - group), (0, 0))).reshape(3 * padded, -1)
        fields3 = fields.reshape(field_count, local_x * local_y, z_length)
        partials = filtered_partials(fields3, weights)

        by_owner = jnp.transpose(every_cell, (1, 0, 2))
        holder = lax.broadcasted_iota(jnp.int32, by_owner.shape, 1)
        clipped = jnp.clip(by_owner, 0, coarse_x * coarse_y * slab - 1)
        cell_pq = clipped // slab
        at_z = holder * slab + clipped % slab
        at_x = (cell_pq // coarse_y - x_base) % coarse_x
        at_y = (cell_pq % coarse_y - y_base) % coarse_y
        inside = (at_x < x_count) & (at_y < y_count) & (by_owner >= 0)
        at_group = at_x * y_count + at_y
        flat = jnp.where(inside, (at_group // pack) * coarse_z + at_z, padded // pack * coarse_z)
        sel = jnp.where(inside, at_group % pack, 0).reshape(1, -1)
        owner_len = devices * slots
        partials = partials.reshape(field_count * 3, padded, coarse_z)
        taken = pick_cells(partials, flat.reshape(-1), sel, owner_len, pack)
        taken = taken.reshape(row_count, col_count, field_count * 3, owner_len)
        by_row = lax.all_to_all(taken, "rows", split_axis=0, concat_axis=0, tiled=True)
        by_row = jnp.sum(by_row, axis=0)
        by_col = lax.all_to_all(by_row, "cols", split_axis=0, concat_axis=0, tiled=True)
        summed = jnp.sum(by_col, axis=0)
        rounded = lax.reduce_precision(summed, exponent_bits=8, mantissa_bits=7)
        mine = lax.dynamic_index_in_dim(by_owner, me, axis=0, keepdims=False).reshape(-1)
        picked = jnp.where(mine[None, :] >= 0, rounded, jnp.zeros_like(rounded))
        return model_tensors(picked)[None]

    return shards


def solution(mesh):
    in_specs = (P(None, "rows", "cols", None), P(("rows", "cols"), None, None))
    out_specs = P(("rows", "cols"), None, None)
    shards = make_shards(mesh.shape["rows"], mesh.shape["cols"])
    return jax.shard_map(shards, mesh=mesh, in_specs=in_specs, out_specs=out_specs, check_vma=False)
```

```python
import numpy as np
import jax
import jax.numpy as jnp
import ml_dtypes
from jax import lax
from jax.sharding import PartitionSpec as P
from jax.experimental import pallas as pl
from jax.experimental.pallas import tpu as pltpu

first_tap = -20
last_tap = 27
sigma_sq = 256.0 / 12.0
coarse_step = 8.0
model_coeff = 1.0 / 3.0
upper_pairs = ((0, 0), (0, 1), (0, 2), (1, 1), (1, 2), (2, 2))
block_len = 1024
halo = 128


def tap_weights(offsets):
    f32 = np.float32
    every_tap = np.arange(first_tap, last_tap + 1).astype(f32)
    weight_sum = np.sum(np.exp(-(every_tap - f32(3.5)) * (every_tap - f32(3.5)) / f32(2.0 * sigma_sq)), dtype=f32)
    shifted = offsets.astype(f32) - f32(3.5)
    inside = (offsets >= first_tap) & (offsets <= last_tap)
    gauss = np.where(inside, np.exp(-shifted * shifted / f32(2.0 * sigma_sq)), f32(0.0)).astype(f32) / weight_sum
    slope = (f32(-coarse_step) * shifted / f32(sigma_sq) * gauss).astype(f32)
    bf = ml_dtypes.bfloat16
    return gauss.astype(bf).astype(f32), slope.astype(bf).astype(f32)


def line_matrices(length):
    fine_pos = np.arange(length)[:, None]
    coarse_pos = np.arange(length // 8)[None, :]
    offsets = np.mod(fine_pos - 8 * coarse_pos, length)
    offsets = np.where(offsets >= length // 2, offsets - length, offsets)
    return tap_weights(offsets)


def z_tables(length):
    coarse = np.arange(length // 8)[None, :]
    main = np.arange(length)[:, None] - 8 * coarse
    prev = np.arange(halo)[:, None] - halo - 8 * coarse
    nxt = np.arange(halo)[:, None] + length - 8 * coarse
    return [tap_weights(o) for o in (main, prev, nxt)]


def filter_kernel(block_count, coarse_block, value_rows, slope_rows):
    def body(x_ref, main_ref, halo_ref, w_ref, o_ref, zv_ref, zs_ref):
        per_step, rows, length = x_ref.shape
        blen = length // block_count
        for b in range(block_count):
            main = x_ref[:, :, b * blen:(b + 1) * blen].reshape(per_step * rows, blen)
            start = (b * blen - halo) % length
            tail = x_ref[:, :, start:start + halo].reshape(per_step * rows, halo)
            start = ((b + 1) * blen) % length
            head = x_ref[:, :, start:start + halo].reshape(per_step * rows, halo)
            edges = jnp.concatenate([tail, head], axis=1)
            acc = jnp.dot(main, main_ref[...], preferred_element_type=jnp.float32)
            acc = acc + jnp.dot(edges, halo_ref[...], preferred_element_type=jnp.float32)
            lanes = slice(b * coarse_block, (b + 1) * coarse_block)
            zv_ref[:, lanes] = acc[:, :coarse_block].astype(jnp.bfloat16)
            zs_ref[:, lanes] = acc[:, coarse_block:].astype(jnp.bfloat16)
        for k in range(per_step):
            zv = zv_ref[k * rows:(k + 1) * rows, :]
            zs = zs_ref[k * rows:(k + 1) * rows, :]
            pv = jnp.dot(w_ref[0, :value_rows, :], zv, preferred_element_type=jnp.float32)
            pv = pv + jnp.dot(w_ref[1, :value_rows, :], zv, preferred_element_type=jnp.float32)
            ps = jnp.dot(w_ref[0, value_rows:, :], zs, preferred_element_type=jnp.float32)
            ps = ps + jnp.dot(w_ref[1, value_rows:, :], zs, preferred_element_type=jnp.float32)
            o_ref[k, :value_rows, :] = pv
            o_ref[k, value_rows:, :] = ps

    return body


def split_hi_lo(w):
    hi = w.astype(jnp.bfloat16)
    lo = (w - hi.astype(jnp.float32)).astype(jnp.bfloat16)
    return jnp.stack([hi, lo], axis=0)


def filtered_partials(fields3, weights):
    field_count, rows, length = fields3.shape
    blen = block_len if (length % block_len == 0 and length > block_len) else length
    block_count = length // blen
    coarse_block = blen // 8
    tables = z_tables(blen)
    joined = [np.concatenate([t[0], t[1]], axis=1) for t in tables]
    main = jnp.asarray(joined[0], jnp.bfloat16)
    halo_w = jnp.asarray(np.concatenate([joined[1], joined[2]], axis=0), jnp.bfloat16)
    w = split_hi_lo(weights)
    total_rows = w.shape[1]
    value_rows = total_rows // 3 * 2
    coarse = length // 8
    per_step = 4 if field_count % 4 == 0 else 1
    const = lambda f: (0, 0)
    return pl.pallas_call(
        filter_kernel(block_count, coarse_block, value_rows, total_rows - value_rows),
        out_shape=jax.ShapeDtypeStruct((field_count, total_rows, coarse), jnp.float32),
        grid=(field_count // per_step,),
        in_specs=[
            pl.BlockSpec((per_step, rows, length), lambda f: (f, 0, 0)),
            pl.BlockSpec(main.shape, const),
            pl.BlockSpec(halo_w.shape, const),
            pl.BlockSpec(w.shape, lambda f: (0, 0, 0)),
        ],
        out_specs=pl.BlockSpec((per_step, total_rows, coarse), lambda f: (f, 0, 0)),
        scratch_shapes=[pltpu.VMEM((per_step * rows, coarse), jnp.bfloat16)] * 2,
    )(fields3, main, halo_w, w)


def window_tables(blocks, count, full):
    smooth, deriv = line_matrices(full)
    coarse = full // 8
    out = []
    for at in range(blocks):
        base, width = window(at, count, coarse)
        picks = (base + np.arange(width)) % coarse
        part = slice(at * count, (at + 1) * count)
        out.append(np.stack([smooth[part][:, picks].T, deriv[part][:, picks].T]))
    return np.stack(out)


def pick_kernel(group_steps, step, chunk, owner_len, pack):
    def body(idx_ref, x_ref, sel_ref, o_ref, tab_ref, buf_ref):
        j = pl.program_id(0)
        rows = x_ref.shape[0]
        lanes = x_ref.shape[2]
        width = tab_ref.shape[1]

        @pl.when(j < group_steps)
        def _():
            for t in range(step):
                parts = [x_ref[:, t * pack + k, :] for k in range(pack)]
                parts.append(jnp.zeros((width - rows * pack, lanes), x_ref.dtype))
                slab = jnp.concatenate(parts, axis=0)
                at = pl.multiple_of((j * step + t) * lanes, lanes)
                tab_ref[pl.ds(at, lanes), :] = slab.T

        @pl.when(j == group_steps - 1)
        def _():
            tail = tab_ref.shape[0] - 8
            tab_ref[pl.ds(tail, 8), :] = jnp.zeros((8, width), tab_ref.dtype)

        @pl.when(j >= group_steps)
        def _():
            base = (j - group_steps) * chunk

            def one(e, carry):
                at = idx_ref[base + e] // 4
                buf_ref[pl.ds(e, 1), :] = tab_ref[pl.ds(at, 1), :]
                return carry

            lax.fori_loop(0, chunk, one, 0, unroll=8)
            flipped = buf_ref[...].T
            sel = sel_ref[...] % 4
            picked = flipped[:rows]
            for k in range(1, pack):
                picked = jnp.where(sel == k, flipped[k * rows:(k + 1) * rows], picked)
            for owner in range(chunk // owner_len):
                o_ref[owner] = picked[:, owner * owner_len:(owner + 1) * owner_len]

    return body


def pick_cells(x, coded, owner_len, pack, chunk=4096):
    rows, groups, lanes = x.shape
    step = 8
    group_steps = groups // (step * pack)
    entries = coded.shape[0]
    chunk = min(chunk, entries)
    width = -(-(rows * pack) // 128) * 128
    per_chunk = chunk // owner_len
    grid_spec = pltpu.PrefetchScalarGridSpec(
        num_scalar_prefetch=1,
        grid=(group_steps + entries // chunk,),
        in_specs=[
            pl.BlockSpec((rows, step * pack, lanes), lambda j, idx: (0, jnp.minimum(j, group_steps - 1), 0)),
            pl.BlockSpec((1, chunk), lambda j, idx: (0, jnp.maximum(j - group_steps, 0))),
        ],
        out_specs=pl.BlockSpec((per_chunk, rows, owner_len), lambda j, idx: (jnp.maximum(j - group_steps, 0), 0, 0)),
        scratch_shapes=[pltpu.VMEM((groups // pack * lanes + 8, width), x.dtype), pltpu.VMEM((chunk, width), x.dtype)],
    )
    return pl.pallas_call(
        pick_kernel(group_steps, step, chunk, owner_len, pack),
        out_shape=jax.ShapeDtypeStruct((entries // owner_len, rows, owner_len), x.dtype),
        grid_spec=grid_spec,
    )(coded, x, coded.reshape(1, -1))


def model_tensors(coarse):
    values = coarse.astype(jnp.float32)
    points = values.shape[-1]
    values = values.reshape(values.shape[0] // 3, 3, points)
    velocity = values[:3]
    species = values[3:]
    stress = [
        jnp.sum(velocity[first_comp] * velocity[second_comp], axis=0)
        for first_comp, second_comp in upper_pairs
    ]
    species_flux = jnp.sum(species[:, None, :, :] * velocity[None, :, :, :], axis=2)
    joined = jnp.concatenate([jnp.stack(stress, axis=0), species_flux.reshape(-1, points)], axis=0)
    return (model_coeff * joined).astype(jnp.bfloat16)


def window(at, count, coarse):
    reach = (count + 19) // 8 + 4
    if count % 8 or reach >= coarse:
        return 0, coarse
    return at * (count // 8) - 3, reach


def make_shards(row_count, col_count):
    def shards(fields, front_cells):
        field_count, local_x, local_y, z_length = fields.shape
        devices = row_count * col_count
        full_x = local_x * row_count
        full_y = local_y * col_count
        coarse_x = full_x // 8
        coarse_y = full_y // 8
        coarse_z = z_length // 8
        slab = coarse_z // devices
        slots = front_cells.shape[2]
        row = lax.axis_index("rows")
        col = lax.axis_index("cols")
        me = row * col_count + col

        copies = jnp.broadcast_to(front_cells, (devices,) + front_cells.shape[1:])
        every_cell = lax.all_to_all(copies, ("rows", "cols"), split_axis=0, concat_axis=0, tiled=True)

        x_base, x_count = window(row, local_x, coarse_x)
        y_base, y_count = window(col, local_y, coarse_y)
        wx = jnp.asarray(window_tables(row_count, local_x, full_x))[row]
        wy = jnp.asarray(window_tables(col_count, local_y, full_y))[col]
        group = x_count * y_count
        pack = 3
        padded = -(-group // (8 * pack)) * 8 * pack
        xs = jnp.stack([wx[1], wx[0], wx[0]])
        ys = jnp.stack([wy[0], wy[1], wy[0]])
        weights = xs[:, :, None, :, None] * ys[:, None, :, None, :]
        weights = weights.reshape(3, group, local_x * local_y)
        weights = jnp.pad(weights, ((0, 0), (0, padded - group), (0, 0))).reshape(3 * padded, -1)
        fields3 = fields.reshape(field_count, local_x * local_y, z_length)
        partials = filtered_partials(fields3, weights)

        by_owner = jnp.transpose(every_cell, (1, 0, 2))
        holder = lax.broadcasted_iota(jnp.int32, by_owner.shape, 1)
        clipped = jnp.clip(by_owner, 0, coarse_x * coarse_y * slab - 1)
        cell_pq = clipped // slab
        at_z = holder * slab + clipped % slab
        at_x = (cell_pq // coarse_y - x_base) % coarse_x
        at_y = (cell_pq % coarse_y - y_base) % coarse_y
        inside = (at_x < x_count) & (at_y < y_count) & (by_owner >= 0)
        at_group = at_x * y_count + at_y
        flat = jnp.where(inside, (at_group // pack) * coarse_z + at_z, padded // pack * coarse_z)
        coded = flat * 4 + jnp.where(inside, at_group % pack, 0)
        owner_len = devices * slots
        partials = partials.reshape(field_count * 3, padded, coarse_z)
        taken = pick_cells(partials, coded.reshape(-1), owner_len, pack)
        arrived = lax.all_to_all(taken, ("rows", "cols"), split_axis=0, concat_axis=0, tiled=True)
        summed = jnp.sum(arrived, axis=0)
        rounded = lax.reduce_precision(summed, exponent_bits=8, mantissa_bits=7)
        mine = lax.dynamic_index_in_dim(by_owner, me, axis=0, keepdims=False).reshape(-1)
        picked = jnp.where(mine[None, :] >= 0, rounded, jnp.zeros_like(rounded))
        return model_tensors(picked)[None]

    return shards


def solution(mesh):
    in_specs = (P(None, "rows", "cols", None), P(("rows", "cols"), None, None))
    out_specs = P(("rows", "cols"), None, None)
    shards = make_shards(mesh.shape["rows"], mesh.shape["cols"])
    return jax.shard_map(shards, mesh=mesh, in_specs=in_specs, out_specs=out_specs, check_vma=False)
```

```python
import numpy as np
import jax
import jax.numpy as jnp
import ml_dtypes
from jax import lax
from jax.sharding import PartitionSpec as P
from jax.experimental import pallas as pl
from jax.experimental.pallas import tpu as pltpu

first_tap = -20
last_tap = 27
sigma_sq = 256.0 / 12.0
coarse_step = 8.0
model_coeff = 1.0 / 3.0
upper_pairs = ((0, 0), (0, 1), (0, 2), (1, 1), (1, 2), (2, 2))
block_len = 1024
halo = 128


def tap_weights(offsets):
    f32 = np.float32
    every_tap = np.arange(first_tap, last_tap + 1).astype(f32)
    weight_sum = np.sum(np.exp(-(every_tap - f32(3.5)) * (every_tap - f32(3.5)) / f32(2.0 * sigma_sq)), dtype=f32)
    shifted = offsets.astype(f32) - f32(3.5)
    inside = (offsets >= first_tap) & (offsets <= last_tap)
    gauss = np.where(inside, np.exp(-shifted * shifted / f32(2.0 * sigma_sq)), f32(0.0)).astype(f32) / weight_sum
    slope = (f32(-coarse_step) * shifted / f32(sigma_sq) * gauss).astype(f32)
    bf = ml_dtypes.bfloat16
    return gauss.astype(bf).astype(f32), slope.astype(bf).astype(f32)


def line_matrices(length):
    fine_pos = np.arange(length)[:, None]
    coarse_pos = np.arange(length // 8)[None, :]
    offsets = np.mod(fine_pos - 8 * coarse_pos, length)
    offsets = np.where(offsets >= length // 2, offsets - length, offsets)
    return tap_weights(offsets)


def z_tables(length):
    coarse = np.arange(length // 8)[None, :]
    main = np.arange(length)[:, None] - 8 * coarse
    prev = np.arange(halo)[:, None] - halo - 8 * coarse
    nxt = np.arange(halo)[:, None] + length - 8 * coarse
    return [tap_weights(o) for o in (main, prev, nxt)]


def filter_kernel(block_count, coarse_block, value_rows, slope_rows):
    def body(x_ref, main_ref, halo_ref, w_ref, o_ref, zv_ref, zs_ref):
        per_step, rows, length = x_ref.shape
        blen = length // block_count
        for b in range(block_count):
            main = x_ref[:, :, b * blen:(b + 1) * blen].reshape(per_step * rows, blen)
            start = (b * blen - halo) % length
            tail = x_ref[:, :, start:start + halo].reshape(per_step * rows, halo)
            start = ((b + 1) * blen) % length
            head = x_ref[:, :, start:start + halo].reshape(per_step * rows, halo)
            edges = jnp.concatenate([tail, head], axis=1)
            acc = jnp.dot(main, main_ref[...], preferred_element_type=jnp.float32)
            acc = acc + jnp.dot(edges, halo_ref[...], preferred_element_type=jnp.float32)
            lanes = slice(b * coarse_block, (b + 1) * coarse_block)
            zv_ref[:, lanes] = acc[:, :coarse_block].astype(jnp.bfloat16)
            zs_ref[:, lanes] = acc[:, coarse_block:].astype(jnp.bfloat16)
        for k in range(per_step):
            zv = zv_ref[k * rows:(k + 1) * rows, :]
            zs = zs_ref[k * rows:(k + 1) * rows, :]
            pv = jnp.dot(w_ref[0, :value_rows, :], zv, preferred_element_type=jnp.float32)
            pv = pv + jnp.dot(w_ref[1, :value_rows, :], zv, preferred_element_type=jnp.float32)
            ps = jnp.dot(w_ref[0, value_rows:, :], zs, preferred_element_type=jnp.float32)
            ps = ps + jnp.dot(w_ref[1, value_rows:, :], zs, preferred_element_type=jnp.float32)
            o_ref[k, :value_rows, :] = pv
            o_ref[k, value_rows:, :] = ps

    return body


def split_hi_lo(w):
    hi = w.astype(jnp.bfloat16)
    lo = (w - hi.astype(jnp.float32)).astype(jnp.bfloat16)
    return jnp.stack([hi, lo], axis=0)


def filtered_partials(fields3, weights):
    field_count, rows, length = fields3.shape
    blen = block_len if (length % block_len == 0 and length > block_len) else length
    block_count = length // blen
    coarse_block = blen // 8
    tables = z_tables(blen)
    joined = [np.concatenate([t[0], t[1]], axis=1) for t in tables]
    main = jnp.asarray(joined[0], jnp.bfloat16)
    halo_w = jnp.asarray(np.concatenate([joined[1], joined[2]], axis=0), jnp.bfloat16)
    w = split_hi_lo(weights)
    total_rows = w.shape[1]
    value_rows = total_rows // 3 * 2
    coarse = length // 8
    per_step = 4 if field_count % 4 == 0 else 1
    const = lambda f: (0, 0)
    return pl.pallas_call(
        filter_kernel(block_count, coarse_block, value_rows, total_rows - value_rows),
        out_shape=jax.ShapeDtypeStruct((field_count, total_rows, coarse), jnp.float32),
        grid=(field_count // per_step,),
        in_specs=[
            pl.BlockSpec((per_step, rows, length), lambda f: (f, 0, 0)),
            pl.BlockSpec(main.shape, const),
            pl.BlockSpec(halo_w.shape, const),
            pl.BlockSpec(w.shape, lambda f: (0, 0, 0)),
        ],
        out_specs=pl.BlockSpec((per_step, total_rows, coarse), lambda f: (f, 0, 0)),
        scratch_shapes=[pltpu.VMEM((per_step * rows, coarse), jnp.bfloat16)] * 2,
    )(fields3, main, halo_w, w)


def window_tables(blocks, count, full):
    smooth, deriv = line_matrices(full)
    coarse = full // 8
    out = []
    for at in range(blocks):
        base, width = window(at, count, coarse)
        picks = (base + np.arange(width)) % coarse
        part = slice(at * count, (at + 1) * count)
        out.append(np.stack([smooth[part][:, picks].T, deriv[part][:, picks].T]))
    return np.stack(out)


def pick_kernel(group_steps, step, chunk, owner_len, pack):
    def body(idx_ref, x_ref, sel_ref, o_ref, tab_ref, buf_ref):
        j = pl.program_id(0)
        rows = x_ref.shape[0]
        lanes = x_ref.shape[2]
        width = tab_ref.shape[2]

        @pl.when(j < group_steps)
        def _():
            for t in range(step):
                parts = [x_ref[:, t * pack + k, :] for k in range(pack)]
                parts.append(jnp.zeros((width - rows * pack, lanes), x_ref.dtype))
                slab = jnp.concatenate(parts, axis=0)
                at = pl.multiple_of((j * step + t) * (lanes // 8), lanes // 8)
                tab_ref[pl.ds(at, lanes // 8), :, :] = slab.T.reshape(lanes // 8, 8, width)

        @pl.when(j == group_steps - 1)
        def _():
            tab_ref[tab_ref.shape[0] - 1] = jnp.zeros((8, width), tab_ref.dtype)

        @pl.when(j >= group_steps)
        def _():
            base = (j - group_steps) * chunk

            def eight(i, carry):
                for k in range(8):
                    code = idx_ref[base + i * 8 + k]
                    tile = lax.shift_right_logical(code, 3)
                    row = tab_ref[tile, pl.ds(code & 7, 1), :]
                    buf_ref[i, pl.ds(k, 1), :] = row
                return carry

            lax.fori_loop(0, chunk // 8, eight, 0)
            flipped = buf_ref[...].reshape(chunk, width).T
            sel = sel_ref[...]
            picked = flipped[:rows]
            for k in range(1, pack):
                picked = jnp.where(sel == k, flipped[k * rows:(k + 1) * rows], picked)
            for owner in range(chunk // owner_len):
                o_ref[owner] = picked[:, owner * owner_len:(owner + 1) * owner_len]

    return body


def pick_cells(x, flat, sel, owner_len, pack, chunk=2048):
    rows, groups, lanes = x.shape
    step = 8
    group_steps = groups // (step * pack)
    entries = flat.shape[0]
    chunk = min(chunk, entries)
    width = -(-(rows * pack) // 128) * 128
    per_chunk = chunk // owner_len
    grid_spec = pltpu.PrefetchScalarGridSpec(
        num_scalar_prefetch=1,
        grid=(group_steps + entries // chunk,),
        in_specs=[
            pl.BlockSpec((rows, step * pack, lanes), lambda j, idx: (0, jnp.minimum(j, group_steps - 1), 0)),
            pl.BlockSpec((1, chunk), lambda j, idx: (0, jnp.maximum(j - group_steps, 0))),
        ],
        out_specs=pl.BlockSpec((per_chunk, rows, owner_len), lambda j, idx: (jnp.maximum(j - group_steps, 0), 0, 0)),
        scratch_shapes=[pltpu.VMEM((groups // pack * lanes // 8 + 1, 8, width), x.dtype), pltpu.VMEM((chunk // 8, 8, width), x.dtype)],
    )
    return pl.pallas_call(
        pick_kernel(group_steps, step, chunk, owner_len, pack),
        out_shape=jax.ShapeDtypeStruct((entries // owner_len, rows, owner_len), x.dtype),
        grid_spec=grid_spec,
    )(flat, x, sel)


def model_tensors(coarse):
    values = coarse.astype(jnp.float32)
    points = values.shape[-1]
    values = values.reshape(values.shape[0] // 3, 3, points)
    velocity = values[:3]
    species = values[3:]
    stress = [
        jnp.sum(velocity[first_comp] * velocity[second_comp], axis=0)
        for first_comp, second_comp in upper_pairs
    ]
    species_flux = jnp.sum(species[:, None, :, :] * velocity[None, :, :, :], axis=2)
    joined = jnp.concatenate([jnp.stack(stress, axis=0), species_flux.reshape(-1, points)], axis=0)
    return (model_coeff * joined).astype(jnp.bfloat16)


def window(at, count, coarse):
    reach = (count + 19) // 8 + 4
    if count % 8 or reach >= coarse:
        return 0, coarse
    return at * (count // 8) - 3, reach


def make_shards(row_count, col_count):
    def shards(fields, front_cells):
        field_count, local_x, local_y, z_length = fields.shape
        devices = row_count * col_count
        full_x = local_x * row_count
        full_y = local_y * col_count
        coarse_x = full_x // 8
        coarse_y = full_y // 8
        coarse_z = z_length // 8
        slab = coarse_z // devices
        slots = front_cells.shape[2]
        row = lax.axis_index("rows")
        col = lax.axis_index("cols")
        me = row * col_count + col

        copies = jnp.broadcast_to(front_cells, (devices,) + front_cells.shape[1:])
        every_cell = lax.all_to_all(copies, ("rows", "cols"), split_axis=0, concat_axis=0, tiled=True)

        x_base, x_count = window(row, local_x, coarse_x)
        y_base, y_count = window(col, local_y, coarse_y)
        wx = jnp.asarray(window_tables(row_count, local_x, full_x))[row]
        wy = jnp.asarray(window_tables(col_count, local_y, full_y))[col]
        group = x_count * y_count
        pack = 3
        padded = -(-group // (8 * pack)) * 8 * pack
        xs = jnp.stack([wx[1], wx[0], wx[0]])
        ys = jnp.stack([wy[0], wy[1], wy[0]])
        weights = xs[:, :, None, :, None] * ys[:, None, :, None, :]
        weights = weights.reshape(3, group, local_x * local_y)
        weights = jnp.pad(weights, ((0, 0), (0, padded - group), (0, 0))).reshape(3 * padded, -1)
        fields3 = fields.reshape(field_count, local_x * local_y, z_length)
        partials = filtered_partials(fields3, weights)

        by_owner = jnp.transpose(every_cell, (1, 0, 2))
        holder = lax.broadcasted_iota(jnp.int32, by_owner.shape, 1)
        clipped = jnp.clip(by_owner, 0, coarse_x * coarse_y * slab - 1)
        cell_pq = clipped // slab
        at_z = holder * slab + clipped % slab
        at_x = (cell_pq // coarse_y - x_base) % coarse_x
        at_y = (cell_pq % coarse_y - y_base) % coarse_y
        inside = (at_x < x_count) & (at_y < y_count) & (by_owner >= 0)
        at_group = at_x * y_count + at_y
        flat = jnp.where(inside, (at_group // pack) * coarse_z + at_z, padded // pack * coarse_z)
        sel = jnp.where(inside, at_group % pack, 0).reshape(1, -1)
        owner_len = devices * slots
        partials = partials.reshape(field_count * 3, padded, coarse_z)
        taken = pick_cells(partials, flat.reshape(-1), sel, owner_len, pack)
        arrived = lax.all_to_all(taken, ("rows", "cols"), split_axis=0, concat_axis=0, tiled=True)
        summed = jnp.sum(arrived, axis=0)
        rounded = lax.reduce_precision(summed, exponent_bits=8, mantissa_bits=7)
        mine = lax.dynamic_index_in_dim(by_owner, me, axis=0, keepdims=False).reshape(-1)
        picked = jnp.where(mine[None, :] >= 0, rounded, jnp.zeros_like(rounded))
        return model_tensors(picked)[None]

    return shards


def solution(mesh):
    in_specs = (P(None, "rows", "cols", None), P(("rows", "cols"), None, None))
    out_specs = P(("rows", "cols"), None, None)
    shards = make_shards(mesh.shape["rows"], mesh.shape["cols"])
    return jax.shard_map(shards, mesh=mesh, in_specs=in_specs, out_specs=out_specs, check_vma=False)
```

```python
import numpy as np
import jax
import jax.numpy as jnp
import ml_dtypes
from jax import lax
from jax.sharding import PartitionSpec as P
from jax.experimental import pallas as pl
from jax.experimental.pallas import tpu as pltpu

first_tap = -20
last_tap = 27
sigma_sq = 256.0 / 12.0
coarse_step = 8.0
model_coeff = 1.0 / 3.0
upper_pairs = ((0, 0), (0, 1), (0, 2), (1, 1), (1, 2), (2, 2))
block_len = 1024
halo = 128


def tap_weights(offsets):
    f32 = np.float32
    every_tap = np.arange(first_tap, last_tap + 1).astype(f32)
    weight_sum = np.sum(np.exp(-(every_tap - f32(3.5)) * (every_tap - f32(3.5)) / f32(2.0 * sigma_sq)), dtype=f32)
    shifted = offsets.astype(f32) - f32(3.5)
    inside = (offsets >= first_tap) & (offsets <= last_tap)
    gauss = np.where(inside, np.exp(-shifted * shifted / f32(2.0 * sigma_sq)), f32(0.0)).astype(f32) / weight_sum
    slope = (f32(-coarse_step) * shifted / f32(sigma_sq) * gauss).astype(f32)
    bf = ml_dtypes.bfloat16
    return gauss.astype(bf).astype(f32), slope.astype(bf).astype(f32)


def line_matrices(length):
    fine_pos = np.arange(length)[:, None]
    coarse_pos = np.arange(length // 8)[None, :]
    offsets = np.mod(fine_pos - 8 * coarse_pos, length)
    offsets = np.where(offsets >= length // 2, offsets - length, offsets)
    return tap_weights(offsets)


def z_tables(length):
    coarse = np.arange(length // 8)[None, :]
    main = np.arange(length)[:, None] - 8 * coarse
    prev = np.arange(halo)[:, None] - halo - 8 * coarse
    nxt = np.arange(halo)[:, None] + length - 8 * coarse
    return [tap_weights(o) for o in (main, prev, nxt)]


def filter_kernel(block_count, coarse_block, value_rows, slope_rows):
    def body(x_ref, main_ref, halo_ref, w_ref, ov_ref, os_ref, zv_ref, zs_ref):
        per_step, rows, length = x_ref.shape
        blen = length // block_count
        for b in range(block_count):
            main = x_ref[:, :, b * blen:(b + 1) * blen].reshape(per_step * rows, blen)
            start = (b * blen - halo) % length
            tail = x_ref[:, :, start:start + halo].reshape(per_step * rows, halo)
            start = ((b + 1) * blen) % length
            head = x_ref[:, :, start:start + halo].reshape(per_step * rows, halo)
            edges = jnp.concatenate([tail, head], axis=1)
            acc = jnp.dot(main, main_ref[...], preferred_element_type=jnp.float32)
            acc = acc + jnp.dot(edges, halo_ref[...], preferred_element_type=jnp.float32)
            lanes = slice(b * coarse_block, (b + 1) * coarse_block)
            zv_ref[:, lanes] = acc[:, :coarse_block].astype(jnp.bfloat16)
            zs_ref[:, lanes] = acc[:, coarse_block:].astype(jnp.bfloat16)
        for k in range(per_step):
            zv = zv_ref[k * rows:(k + 1) * rows, :]
            zs = zs_ref[k * rows:(k + 1) * rows, :]
            pv = jnp.dot(w_ref[0, :value_rows, :], zv, preferred_element_type=jnp.float32)
            pv = pv + jnp.dot(w_ref[1, :value_rows, :], zv, preferred_element_type=jnp.float32)
            ps = jnp.dot(w_ref[0, value_rows:, :], zs, preferred_element_type=jnp.float32)
            ps = ps + jnp.dot(w_ref[1, value_rows:, :], zs, preferred_element_type=jnp.float32)
            ov_ref[k] = pv
            os_ref[k] = ps

    return body


def split_hi_lo(w):
    hi = w.astype(jnp.bfloat16)
    lo = (w - hi.astype(jnp.float32)).astype(jnp.bfloat16)
    return jnp.stack([hi, lo], axis=0)


def filtered_partials(fields3, weights):
    field_count, rows, length = fields3.shape
    blen = block_len if (length % block_len == 0 and length > block_len) else length
    block_count = length // blen
    coarse_block = blen // 8
    tables = z_tables(blen)
    joined = [np.concatenate([t[0], t[1]], axis=1) for t in tables]
    main = jnp.asarray(joined[0], jnp.bfloat16)
    halo_w = jnp.asarray(np.concatenate([joined[1], joined[2]], axis=0), jnp.bfloat16)
    w = split_hi_lo(weights)
    total_rows = w.shape[1]
    value_rows = total_rows // 3 * 2
    coarse = length // 8
    per_step = 4 if field_count % 4 == 0 else 1
    const = lambda f: (0, 0)
    return pl.pallas_call(
        filter_kernel(block_count, coarse_block, value_rows, total_rows - value_rows),
        out_shape=[
            jax.ShapeDtypeStruct((field_count, value_rows, coarse), jnp.float32),
            jax.ShapeDtypeStruct((field_count, total_rows - value_rows, coarse), jnp.float32),
        ],
        grid=(field_count // per_step,),
        in_specs=[
            pl.BlockSpec((per_step, rows, length), lambda f: (f, 0, 0)),
            pl.BlockSpec(main.shape, const),
            pl.BlockSpec(halo_w.shape, const),
            pl.BlockSpec(w.shape, lambda f: (0, 0, 0)),
        ],
        out_specs=[
            pl.BlockSpec((per_step, value_rows, coarse), lambda f: (f, 0, 0)),
            pl.BlockSpec((per_step, total_rows - value_rows, coarse), lambda f: (f, 0, 0)),
        ],
        scratch_shapes=[pltpu.VMEM((per_step * rows, coarse), jnp.bfloat16)] * 2,
    )(fields3, main, halo_w, w)


def window_tables(blocks, count, full):
    smooth, deriv = line_matrices(full)
    coarse = full // 8
    out = []
    for at in range(blocks):
        base, width = window(at, count, coarse)
        picks = (base + np.arange(width)) % coarse
        part = slice(at * count, (at + 1) * count)
        out.append(np.stack([smooth[part][:, picks].T, deriv[part][:, picks].T]))
    return np.stack(out)


def pick_kernel(group_steps, step, chunk, owner_len, pack):
    def body(idx_ref, xv_ref, xs_ref, sel_ref, o_ref, tab_ref, buf_ref):
        j = pl.program_id(0)
        fields = xv_ref.shape[0]
        lanes = xv_ref.shape[2]
        width = tab_ref.shape[2]
        per_field = 3 * pack

        @pl.when(j < group_steps)
        def _():
            for t in range(step):
                parts = []
                for f in range(fields):
                    parts.append(xv_ref[f, 2 * pack * t:2 * pack * (t + 1), :])
                    parts.append(xs_ref[f, pack * t:pack * (t + 1), :])
                parts.append(jnp.zeros((width - fields * per_field, lanes), xv_ref.dtype))
                slab = jnp.concatenate(parts, axis=0)
                at = pl.multiple_of((j * step + t) * (lanes // 8), lanes // 8)
                tab_ref[pl.ds(at, lanes // 8), :, :] = slab.T.reshape(lanes // 8, 8, width)

        @pl.when(j == group_steps - 1)
        def _():
            tab_ref[tab_ref.shape[0] - 1] = jnp.zeros((8, width), tab_ref.dtype)

        @pl.when(j >= group_steps)
        def _():
            base = (j - group_steps) * chunk

            def eight(i, carry):
                for k in range(8):
                    code = idx_ref[base + i * 8 + k]
                    tile = lax.shift_right_logical(code, 3)
                    row = tab_ref[tile, pl.ds(code & 7, 1), :]
                    buf_ref[i, pl.ds(k, 1), :] = row
                return carry

            lax.fori_loop(0, chunk // 8, eight, 0)
            flipped = buf_ref[...].reshape(chunk, width).T
            sel = sel_ref[...]
            picked = []
            for f in range(fields):
                for m in range(3):
                    choices = []
                    for k in range(pack):
                        at = f * per_field + (2 * k + m if m < 2 else 2 * pack + k)
                        choices.append(flipped[at:at + 1])
                    row = choices[0]
                    for k in range(1, pack):
                        row = jnp.where(sel == k, choices[k], row)
                    picked.append(row)
            picked = jnp.concatenate(picked, axis=0)
            for owner in range(chunk // owner_len):
                o_ref[owner] = picked[:, owner * owner_len:(owner + 1) * owner_len]

    return body


def pick_cells(xv, xs, flat, sel, owner_len, pack, chunk=2048):
    fields, groups, lanes = xs.shape
    rows = fields * 3
    step = 8
    group_steps = groups // (step * pack)
    entries = flat.shape[0]
    chunk = min(chunk, entries)
    width = -(-(rows * pack) // 128) * 128
    per_chunk = chunk // owner_len
    grid_spec = pltpu.PrefetchScalarGridSpec(
        num_scalar_prefetch=1,
        grid=(group_steps + entries // chunk,),
        in_specs=[
            pl.BlockSpec((fields, 2 * step * pack, lanes), lambda j, idx: (0, jnp.minimum(j, group_steps - 1), 0)),
            pl.BlockSpec((fields, step * pack, lanes), lambda j, idx: (0, jnp.minimum(j, group_steps - 1), 0)),
            pl.BlockSpec((1, chunk), lambda j, idx: (0, jnp.maximum(j - group_steps, 0))),
        ],
        out_specs=pl.BlockSpec((per_chunk, rows, owner_len), lambda j, idx: (jnp.maximum(j - group_steps, 0), 0, 0)),
        scratch_shapes=[pltpu.VMEM((groups // pack * lanes // 8 + 1, 8, width), xs.dtype), pltpu.VMEM((chunk // 8, 8, width), xs.dtype)],
    )
    return pl.pallas_call(
        pick_kernel(group_steps, step, chunk, owner_len, pack),
        out_shape=jax.ShapeDtypeStruct((entries // owner_len, rows, owner_len), xs.dtype),
        grid_spec=grid_spec,
    )(flat, xv, xs, sel)


def model_tensors(coarse):
    values = coarse.astype(jnp.float32)
    points = values.shape[-1]
    values = values.reshape(values.shape[0] // 3, 3, points)
    velocity = values[:3]
    species = values[3:]
    stress = [
        jnp.sum(velocity[first_comp] * velocity[second_comp], axis=0)
        for first_comp, second_comp in upper_pairs
    ]
    species_flux = jnp.sum(species[:, None, :, :] * velocity[None, :, :, :], axis=2)
    joined = jnp.concatenate([jnp.stack(stress, axis=0), species_flux.reshape(-1, points)], axis=0)
    return (model_coeff * joined).astype(jnp.bfloat16)


def window(at, count, coarse):
    reach = (count + 19) // 8 + 4
    if count % 8 or reach >= coarse:
        return 0, coarse
    return at * (count // 8) - 3, reach


def make_shards(row_count, col_count):
    def shards(fields, front_cells):
        field_count, local_x, local_y, z_length = fields.shape
        devices = row_count * col_count
        full_x = local_x * row_count
        full_y = local_y * col_count
        coarse_x = full_x // 8
        coarse_y = full_y // 8
        coarse_z = z_length // 8
        slab = coarse_z // devices
        slots = front_cells.shape[2]
        row = lax.axis_index("rows")
        col = lax.axis_index("cols")
        me = row * col_count + col

        copies = jnp.broadcast_to(front_cells, (devices,) + front_cells.shape[1:])
        every_cell = lax.all_to_all(copies, ("rows", "cols"), split_axis=0, concat_axis=0, tiled=True)

        x_base, x_count = window(row, local_x, coarse_x)
        y_base, y_count = window(col, local_y, coarse_y)
        wx = jnp.asarray(window_tables(row_count, local_x, full_x))[row]
        wy = jnp.asarray(window_tables(col_count, local_y, full_y))[col]
        group = x_count * y_count
        pack = 3
        padded = -(-group // (8 * pack)) * 8 * pack
        xs = jnp.stack([wx[1], wx[0], wx[0]])
        ys = jnp.stack([wy[0], wy[1], wy[0]])
        weights = xs[:, :, None, :, None] * ys[:, None, :, None, :]
        weights = weights.reshape(3, group, local_x * local_y)
        weights = jnp.pad(weights, ((0, 0), (0, padded - group), (0, 0)))
        weights = jnp.concatenate([jnp.transpose(weights[:2], (1, 0, 2)).reshape(2 * padded, -1), weights[2]], axis=0)
        fields3 = fields.reshape(field_count, local_x * local_y, z_length)
        partials = filtered_partials(fields3, weights)

        by_owner = jnp.transpose(every_cell, (1, 0, 2))
        holder = lax.broadcasted_iota(jnp.int32, by_owner.shape, 1)
        clipped = jnp.clip(by_owner, 0, coarse_x * coarse_y * slab - 1)
        cell_pq = clipped // slab
        at_z = holder * slab + clipped % slab
        at_x = (cell_pq // coarse_y - x_base) % coarse_x
        at_y = (cell_pq % coarse_y - y_base) % coarse_y
        inside = (at_x < x_count) & (at_y < y_count) & (by_owner >= 0)
        at_group = at_x * y_count + at_y
        flat = jnp.where(inside, (at_group // pack) * coarse_z + at_z, padded // pack * coarse_z)
        sel = jnp.where(inside, at_group % pack, 0).reshape(1, -1)
        owner_len = devices * slots
        value_part, slope_part = partials
        taken = pick_cells(value_part, slope_part, flat.reshape(-1), sel, owner_len, pack)
        arrived = lax.all_to_all(taken, ("rows", "cols"), split_axis=0, concat_axis=0, tiled=True)
        summed = jnp.sum(arrived, axis=0)
        rounded = lax.reduce_precision(summed, exponent_bits=8, mantissa_bits=7)
        mine = lax.dynamic_index_in_dim(by_owner, me, axis=0, keepdims=False).reshape(-1)
        picked = jnp.where(mine[None, :] >= 0, rounded, jnp.zeros_like(rounded))
        return model_tensors(picked)[None]

    return shards


def solution(mesh):
    in_specs = (P(None, "rows", "cols", None), P(("rows", "cols"), None, None))
    out_specs = P(("rows", "cols"), None, None)
    shards = make_shards(mesh.shape["rows"], mesh.shape["cols"])
    return jax.shard_map(shards, mesh=mesh, in_specs=in_specs, out_specs=out_specs, check_vma=False)
```

```python
import numpy as np
import jax
import jax.numpy as jnp
import ml_dtypes
from jax import lax
from jax.sharding import PartitionSpec as P
from jax.experimental import pallas as pl
from jax.experimental.pallas import tpu as pltpu

first_tap = -20
last_tap = 27
sigma_sq = 256.0 / 12.0
coarse_step = 8.0
model_coeff = 1.0 / 3.0
upper_pairs = ((0, 0), (0, 1), (0, 2), (1, 1), (1, 2), (2, 2))
block_len = 1024
halo = 128


def tap_weights(offsets):
    f32 = np.float32
    every_tap = np.arange(first_tap, last_tap + 1).astype(f32)
    weight_sum = np.sum(np.exp(-(every_tap - f32(3.5)) * (every_tap - f32(3.5)) / f32(2.0 * sigma_sq)), dtype=f32)
    shifted = offsets.astype(f32) - f32(3.5)
    inside = (offsets >= first_tap) & (offsets <= last_tap)
    gauss = np.where(inside, np.exp(-shifted * shifted / f32(2.0 * sigma_sq)), f32(0.0)).astype(f32) / weight_sum
    slope = (f32(-coarse_step) * shifted / f32(sigma_sq) * gauss).astype(f32)
    bf = ml_dtypes.bfloat16
    return gauss.astype(bf).astype(f32), slope.astype(bf).astype(f32)


def line_matrices(length):
    fine_pos = np.arange(length)[:, None]
    coarse_pos = np.arange(length // 8)[None, :]
    offsets = np.mod(fine_pos - 8 * coarse_pos, length)
    offsets = np.where(offsets >= length // 2, offsets - length, offsets)
    return tap_weights(offsets)


def z_tables(length):
    coarse = np.arange(length // 8)[None, :]
    main = np.arange(length)[:, None] - 8 * coarse
    prev = np.arange(halo)[:, None] - halo - 8 * coarse
    nxt = np.arange(halo)[:, None] + length - 8 * coarse
    return [tap_weights(o) for o in (main, prev, nxt)]


def filter_kernel(block_count, coarse_block, value_rows, slope_rows):
    def body(x_ref, main_ref, halo_ref, w_ref, ov_ref, os_ref, zv_ref, zs_ref):
        per_step, rows, length = x_ref.shape
        blen = length // block_count
        for b in range(block_count):
            main = x_ref[:, :, b * blen:(b + 1) * blen].reshape(per_step * rows, blen)
            start = (b * blen - halo) % length
            tail = x_ref[:, :, start:start + halo].reshape(per_step * rows, halo)
            start = ((b + 1) * blen) % length
            head = x_ref[:, :, start:start + halo].reshape(per_step * rows, halo)
            edges = jnp.concatenate([tail, head], axis=1)
            acc = jnp.dot(main, main_ref[...], preferred_element_type=jnp.float32)
            acc = acc + jnp.dot(edges, halo_ref[...], preferred_element_type=jnp.float32)
            lanes = slice(b * coarse_block, (b + 1) * coarse_block)
            zv_ref[:, lanes] = acc[:, :coarse_block].astype(jnp.bfloat16)
            zs_ref[:, lanes] = acc[:, coarse_block:].astype(jnp.bfloat16)
        for k in range(per_step):
            zv = zv_ref[k * rows:(k + 1) * rows, :]
            zs = zs_ref[k * rows:(k + 1) * rows, :]
            pv = jnp.dot(w_ref[0, :value_rows, :], zv, preferred_element_type=jnp.float32)
            pv = pv + jnp.dot(w_ref[1, :value_rows, :], zv, preferred_element_type=jnp.float32)
            ps = jnp.dot(w_ref[0, value_rows:, :], zs, preferred_element_type=jnp.float32)
            ps = ps + jnp.dot(w_ref[1, value_rows:, :], zs, preferred_element_type=jnp.float32)
            ov_ref[k] = pv
            os_ref[k] = ps

    return body


def split_hi_lo(w):
    hi = w.astype(jnp.bfloat16)
    lo = (w - hi.astype(jnp.float32)).astype(jnp.bfloat16)
    return jnp.stack([hi, lo], axis=0)


def filtered_partials(fields3, weights):
    field_count, rows, length = fields3.shape
    blen = block_len if (length % block_len == 0 and length > block_len) else length
    block_count = length // blen
    coarse_block = blen // 8
    tables = z_tables(blen)
    joined = [np.concatenate([t[0], t[1]], axis=1) for t in tables]
    main = jnp.asarray(joined[0], jnp.bfloat16)
    halo_w = jnp.asarray(np.concatenate([joined[1], joined[2]], axis=0), jnp.bfloat16)
    w = split_hi_lo(weights)
    total_rows = w.shape[1]
    value_rows = total_rows // 3 * 2
    coarse = length // 8
    per_step = 4 if field_count % 4 == 0 else 1
    const = lambda f: (0, 0)
    return pl.pallas_call(
        filter_kernel(block_count, coarse_block, value_rows, total_rows - value_rows),
        out_shape=[
            jax.ShapeDtypeStruct((field_count, value_rows, coarse), jnp.float32),
            jax.ShapeDtypeStruct((field_count, total_rows - value_rows, coarse), jnp.float32),
        ],
        grid=(field_count // per_step,),
        in_specs=[
            pl.BlockSpec((per_step, rows, length), lambda f: (f, 0, 0)),
            pl.BlockSpec(main.shape, const),
            pl.BlockSpec(halo_w.shape, const),
            pl.BlockSpec(w.shape, lambda f: (0, 0, 0)),
        ],
        out_specs=[
            pl.BlockSpec((per_step, value_rows, coarse), lambda f: (f, 0, 0)),
            pl.BlockSpec((per_step, total_rows - value_rows, coarse), lambda f: (f, 0, 0)),
        ],
        scratch_shapes=[pltpu.VMEM((per_step * rows, coarse), jnp.bfloat16)] * 2,
    )(fields3, main, halo_w, w)


def window_tables(blocks, count, full):
    smooth, deriv = line_matrices(full)
    coarse = full // 8
    out = []
    for at in range(blocks):
        base, width = window(at, count, coarse)
        picks = (base + np.arange(width)) % coarse
        part = slice(at * count, (at + 1) * count)
        out.append(np.stack([smooth[part][:, picks].T, deriv[part][:, picks].T]))
    return np.stack(out)


def pick_kernel(group_steps, step, chunk, owner_len, pack):
    def body(idx_ref, xv_ref, xs_ref, sel_ref, o_ref, tab_ref, buf_ref):
        j = pl.program_id(0)
        fields = xv_ref.shape[0]
        lanes = xv_ref.shape[2]
        width = tab_ref.shape[2]
        per_field = 3 * pack

        @pl.when(j < group_steps)
        def _():
            for t in range(step):
                parts = []
                for f in range(fields):
                    parts.append(xv_ref[f, 2 * pack * t:2 * pack * (t + 1), :])
                    parts.append(xs_ref[f, pack * t:pack * (t + 1), :])
                parts.append(jnp.zeros((width - fields * per_field, lanes), xv_ref.dtype))
                slab = jnp.concatenate(parts, axis=0)
                at = pl.multiple_of((j * step + t) * (lanes // 8), lanes // 8)
                tab_ref[pl.ds(at, lanes // 8), :, :] = slab.T.reshape(lanes // 8, 8, width)

        @pl.when(j == group_steps - 1)
        def _():
            tab_ref[tab_ref.shape[0] - 1] = jnp.zeros((8, width), tab_ref.dtype)

        @pl.when(j >= group_steps)
        def _():
            base = (j - group_steps) * chunk

            def eight(i, carry):
                for k in range(8):
                    code = idx_ref[base + i * 8 + k]
                    tile = lax.shift_right_logical(code, 3)
                    row = tab_ref[tile, pl.ds(code & 7, 1), :]
                    buf_ref[i, pl.ds(k, 1), :] = row
                return carry

            lax.fori_loop(0, chunk // 8, eight, 0)
            flipped = buf_ref[...].reshape(chunk, width).T
            sel = sel_ref[...]
            picked = []
            for f in range(fields):
                for m in range(3):
                    choices = []
                    for k in range(pack):
                        at = f * per_field + (2 * k + m if m < 2 else 2 * pack + k)
                        choices.append(flipped[at:at + 1])
                    row = choices[0]
                    for k in range(1, pack):
                        row = jnp.where(sel == k, choices[k], row)
                    picked.append(row)
            picked = jnp.concatenate(picked, axis=0)
            for owner in range(chunk // owner_len):
                o_ref[owner] = picked[:, owner * owner_len:(owner + 1) * owner_len]

    return body


def pick_cells(xv, xs, flat, sel, owner_len, pack, chunk=2048):
    fields, groups, lanes = xs.shape
    rows = fields * 3
    step = 8
    group_steps = groups // (step * pack)
    entries = flat.shape[0]
    chunk = min(chunk, entries)
    width = -(-(rows * pack) // 128) * 128
    per_chunk = chunk // owner_len
    grid_spec = pltpu.PrefetchScalarGridSpec(
        num_scalar_prefetch=1,
        grid=(group_steps + entries // chunk,),
        in_specs=[
            pl.BlockSpec((fields, 2 * step * pack, lanes), lambda j, idx: (0, jnp.minimum(j, group_steps - 1), 0)),
            pl.BlockSpec((fields, step * pack, lanes), lambda j, idx: (0, jnp.minimum(j, group_steps - 1), 0)),
            pl.BlockSpec((1, chunk), lambda j, idx: (0, jnp.maximum(j - group_steps, 0))),
        ],
        out_specs=pl.BlockSpec((per_chunk, rows, owner_len), lambda j, idx: (jnp.maximum(j - group_steps, 0), 0, 0)),
        scratch_shapes=[pltpu.VMEM((groups // pack * lanes // 8 + 1, 8, width), xs.dtype), pltpu.VMEM((chunk // 8, 8, width), xs.dtype)],
    )
    return pl.pallas_call(
        pick_kernel(group_steps, step, chunk, owner_len, pack),
        out_shape=jax.ShapeDtypeStruct((entries // owner_len, rows, owner_len), xs.dtype),
        grid_spec=grid_spec,
    )(flat, xv, xs, sel)


def model_tensors(coarse):
    values = coarse.astype(jnp.float32)
    points = values.shape[-1]
    values = values.reshape(values.shape[0] // 3, 3, points)
    velocity = values[:3]
    species = values[3:]
    stress = [
        jnp.sum(velocity[first_comp] * velocity[second_comp], axis=0)
        for first_comp, second_comp in upper_pairs
    ]
    species_flux = jnp.sum(species[:, None, :, :] * velocity[None, :, :, :], axis=2)
    joined = jnp.concatenate([jnp.stack(stress, axis=0), species_flux.reshape(-1, points)], axis=0)
    return (model_coeff * joined).astype(jnp.bfloat16)


def window(at, count, coarse):
    reach = (count + 19) // 8 + 4
    if count % 8 or reach >= coarse:
        return 0, coarse
    return at * (count // 8) - 3, reach


def make_shards(row_count, col_count):
    def shards(fields, front_cells):
        field_count, local_x, local_y, z_length = fields.shape
        devices = row_count * col_count
        full_x = local_x * row_count
        full_y = local_y * col_count
        coarse_x = full_x // 8
        coarse_y = full_y // 8
        coarse_z = z_length // 8
        slab = coarse_z // devices
        slots = front_cells.shape[2]
        row = lax.axis_index("rows")
        col = lax.axis_index("cols")
        me = row * col_count + col

        copies = jnp.broadcast_to(front_cells[:, :, None, :], (devices,) + front_cells.shape[1:2] + (1,) + front_cells.shape[2:])
        by_owner = lax.all_to_all(copies, ("rows", "cols"), split_axis=0, concat_axis=2, tiled=True)[0]

        x_base, x_count = window(row, local_x, coarse_x)
        y_base, y_count = window(col, local_y, coarse_y)
        wx = jnp.asarray(window_tables(row_count, local_x, full_x))[row]
        wy = jnp.asarray(window_tables(col_count, local_y, full_y))[col]
        group = x_count * y_count
        pack = 3
        padded = -(-group // (8 * pack)) * 8 * pack
        xs = jnp.stack([wx[1], wx[0], wx[0]])
        ys = jnp.stack([wy[0], wy[1], wy[0]])
        weights = xs[:, :, None, :, None] * ys[:, None, :, None, :]
        weights = weights.reshape(3, group, local_x * local_y)
        weights = jnp.pad(weights, ((0, 0), (0, padded - group), (0, 0)))
        weights = jnp.concatenate([jnp.transpose(weights[:2], (1, 0, 2)).reshape(2 * padded, -1), weights[2]], axis=0)
        fields3 = fields.reshape(field_count, local_x * local_y, z_length)
        partials = filtered_partials(fields3, weights)

        holder = lax.broadcasted_iota(jnp.int32, by_owner.shape, 1)
        clipped = jnp.clip(by_owner, 0, coarse_x * coarse_y * slab - 1)
        cell_pq = clipped // slab
        at_z = holder * slab + clipped % slab
        at_x = (cell_pq // coarse_y - x_base) % coarse_x
        at_y = (cell_pq % coarse_y - y_base) % coarse_y
        inside = (at_x < x_count) & (at_y < y_count) & (by_owner >= 0)
        at_group = at_x * y_count + at_y
        flat = jnp.where(inside, (at_group // pack) * coarse_z + at_z, padded // pack * coarse_z)
        sel = jnp.where(inside, at_group % pack, 0).reshape(1, -1)
        owner_len = devices * slots
        value_part, slope_part = partials
        taken = pick_cells(value_part, slope_part, flat.reshape(-1), sel, owner_len, pack)
        arrived = lax.all_to_all(taken, ("rows", "cols"), split_axis=0, concat_axis=0, tiled=True)
        summed = jnp.sum(arrived, axis=0)
        rounded = lax.reduce_precision(summed, exponent_bits=8, mantissa_bits=7)
        mine = lax.dynamic_index_in_dim(by_owner, me, axis=0, keepdims=False).reshape(-1)
        picked = jnp.where(mine[None, :] >= 0, rounded, jnp.zeros_like(rounded))
        return model_tensors(picked)[None]

    return shards


def solution(mesh):
    in_specs = (P(None, "rows", "cols", None), P(("rows", "cols"), None, None))
    out_specs = P(("rows", "cols"), None, None)
    shards = make_shards(mesh.shape["rows"], mesh.shape["cols"])
    return jax.shard_map(shards, mesh=mesh, in_specs=in_specs, out_specs=out_specs, check_vma=False)
```

```python
import numpy as np
import jax
import jax.numpy as jnp
import ml_dtypes
from jax import lax
from jax.sharding import PartitionSpec as P
from jax.experimental import pallas as pl
from jax.experimental.pallas import tpu as pltpu

first_tap = -20
last_tap = 27
sigma_sq = 256.0 / 12.0
coarse_step = 8.0
model_coeff = 1.0 / 3.0
upper_pairs = ((0, 0), (0, 1), (0, 2), (1, 1), (1, 2), (2, 2))
block_len = 1024
halo = 128


def tap_weights(offsets):
    f32 = np.float32
    every_tap = np.arange(first_tap, last_tap + 1).astype(f32)
    weight_sum = np.sum(np.exp(-(every_tap - f32(3.5)) * (every_tap - f32(3.5)) / f32(2.0 * sigma_sq)), dtype=f32)
    shifted = offsets.astype(f32) - f32(3.5)
    inside = (offsets >= first_tap) & (offsets <= last_tap)
    gauss = np.where(inside, np.exp(-shifted * shifted / f32(2.0 * sigma_sq)), f32(0.0)).astype(f32) / weight_sum
    slope = (f32(-coarse_step) * shifted / f32(sigma_sq) * gauss).astype(f32)
    bf = ml_dtypes.bfloat16
    return gauss.astype(bf).astype(f32), slope.astype(bf).astype(f32)


def line_matrices(length):
    fine_pos = np.arange(length)[:, None]
    coarse_pos = np.arange(length // 8)[None, :]
    offsets = np.mod(fine_pos - 8 * coarse_pos, length)
    offsets = np.where(offsets >= length // 2, offsets - length, offsets)
    return tap_weights(offsets)


def z_tables(length):
    coarse = np.arange(length // 8)[None, :]
    main = np.arange(length)[:, None] - 8 * coarse
    prev = np.arange(halo)[:, None] - halo - 8 * coarse
    nxt = np.arange(halo)[:, None] + length - 8 * coarse
    return [tap_weights(o) for o in (main, prev, nxt)]


def filter_kernel(block_count, coarse_block, value_rows, slope_rows):
    def body(x_ref, main_ref, halo_ref, w_ref, ov_ref, os_ref, zv_ref, zs_ref):
        per_step, rows, length = x_ref.shape
        blen = length // block_count
        for b in range(block_count):
            main = x_ref[:, :, b * blen:(b + 1) * blen].reshape(per_step * rows, blen)
            start = (b * blen - halo) % length
            tail = x_ref[:, :, start:start + halo].reshape(per_step * rows, halo)
            start = ((b + 1) * blen) % length
            head = x_ref[:, :, start:start + halo].reshape(per_step * rows, halo)
            edges = jnp.concatenate([tail, head], axis=1)
            acc = jnp.dot(main, main_ref[...], preferred_element_type=jnp.float32)
            acc = acc + jnp.dot(edges, halo_ref[...], preferred_element_type=jnp.float32)
            lanes = slice(b * coarse_block, (b + 1) * coarse_block)
            zv_ref[:, lanes] = acc[:, :coarse_block].astype(jnp.bfloat16)
            zs_ref[:, lanes] = acc[:, coarse_block:].astype(jnp.bfloat16)
        for k in range(per_step):
            zv = zv_ref[k * rows:(k + 1) * rows, :]
            zs = zs_ref[k * rows:(k + 1) * rows, :]
            pv = jnp.dot(w_ref[0, :value_rows, :], zv, preferred_element_type=jnp.float32)
            pv = pv + jnp.dot(w_ref[1, :value_rows, :], zv, preferred_element_type=jnp.float32)
            ps = jnp.dot(w_ref[0, value_rows:, :], zs, preferred_element_type=jnp.float32)
            ps = ps + jnp.dot(w_ref[1, value_rows:, :], zs, preferred_element_type=jnp.float32)
            ov_ref[k] = pv
            os_ref[k] = ps

    return body


def split_hi_lo(w):
    hi = w.astype(jnp.bfloat16)
    lo = (w - hi.astype(jnp.float32)).astype(jnp.bfloat16)
    return jnp.stack([hi, lo], axis=0)


def filtered_partials(fields3, weights):
    field_count, rows, length = fields3.shape
    blen = block_len if (length % block_len == 0 and length > block_len) else length
    block_count = length // blen
    coarse_block = blen // 8
    tables = z_tables(blen)
    joined = [np.concatenate([t[0], t[1]], axis=1) for t in tables]
    main = jnp.asarray(joined[0], jnp.bfloat16)
    halo_w = jnp.asarray(np.concatenate([joined[1], joined[2]], axis=0), jnp.bfloat16)
    w = split_hi_lo(weights)
    total_rows = w.shape[1]
    value_rows = total_rows // 3 * 2
    coarse = length // 8
    per_step = 4 if field_count % 4 == 0 else 1
    const = lambda f: (0, 0)
    return pl.pallas_call(
        filter_kernel(block_count, coarse_block, value_rows, total_rows - value_rows),
        out_shape=[
            jax.ShapeDtypeStruct((field_count, value_rows, coarse), jnp.float32),
            jax.ShapeDtypeStruct((field_count, total_rows - value_rows, coarse), jnp.float32),
        ],
        grid=(field_count // per_step,),
        in_specs=[
            pl.BlockSpec((per_step, rows, length), lambda f: (f, 0, 0)),
            pl.BlockSpec(main.shape, const),
            pl.BlockSpec(halo_w.shape, const),
            pl.BlockSpec(w.shape, lambda f: (0, 0, 0)),
        ],
        out_specs=[
            pl.BlockSpec((per_step, value_rows, coarse), lambda f: (f, 0, 0)),
            pl.BlockSpec((per_step, total_rows - value_rows, coarse), lambda f: (f, 0, 0)),
        ],
        scratch_shapes=[pltpu.VMEM((per_step * rows, coarse), jnp.bfloat16)] * 2,
    )(fields3, main, halo_w, w)


def window_tables(blocks, count, full):
    smooth, deriv = line_matrices(full)
    coarse = full // 8
    out = []
    for at in range(blocks):
        base, width = window(at, count, coarse)
        picks = (base + np.arange(width)) % coarse
        part = slice(at * count, (at + 1) * count)
        out.append(np.stack([smooth[part][:, picks].T, deriv[part][:, picks].T]))
    return np.stack(out)


def pick_kernel(group_steps, step, chunk, owner_len, pack):
    def body(idx_ref, xv_ref, xs_ref, sel_ref, o_ref, tab_ref, buf_ref):
        j = pl.program_id(0)
        fields = xv_ref.shape[0]
        lanes = xv_ref.shape[2]
        width = tab_ref.shape[2]
        per_field = 3 * pack

        @pl.when(j < group_steps)
        def _():
            for t in range(step):
                parts = []
                for f in range(fields):
                    parts.append(xv_ref[f, 2 * pack * t:2 * pack * (t + 1), :])
                    parts.append(xs_ref[f, pack * t:pack * (t + 1), :])
                parts.append(jnp.zeros((width - fields * per_field, lanes), xv_ref.dtype))
                slab = jnp.concatenate(parts, axis=0)
                at = pl.multiple_of((j * step + t) * (lanes // 8), lanes // 8)
                tab_ref[pl.ds(at, lanes // 8), :, :] = slab.T.reshape(lanes // 8, 8, width)

        @pl.when(j == group_steps - 1)
        def _():
            tab_ref[tab_ref.shape[0] - 1] = jnp.zeros((8, width), tab_ref.dtype)

        @pl.when(j >= group_steps)
        def _():
            base = (j - group_steps) * chunk

            def eight(i, carry):
                for k in range(8):
                    code = idx_ref[base + i * 8 + k]
                    tile = lax.shift_right_logical(code, 3)
                    row = tab_ref[tile, pl.ds(code & 7, 1), :]
                    buf_ref[i, pl.ds(k, 1), :] = row
                return carry

            lax.fori_loop(0, chunk // 8, eight, 0, unroll=4)
            flipped = buf_ref[...].reshape(chunk, width).T
            sel = sel_ref[...]
            picked = []
            for f in range(fields):
                for m in range(3):
                    choices = []
                    for k in range(pack):
                        at = f * per_field + (2 * k + m if m < 2 else 2 * pack + k)
                        choices.append(flipped[at:at + 1])
                    row = choices[0]
                    for k in range(1, pack):
                        row = jnp.where(sel == k, choices[k], row)
                    picked.append(row)
            picked = jnp.concatenate(picked, axis=0)
            for owner in range(chunk // owner_len):
                o_ref[owner] = picked[:, owner * owner_len:(owner + 1) * owner_len]

    return body


def pick_cells(xv, xs, flat, sel, owner_len, pack, chunk=2048):
    fields, groups, lanes = xs.shape
    rows = fields * 3
    step = 8
    group_steps = groups // (step * pack)
    entries = flat.shape[0]
    chunk = min(chunk, entries)
    width = -(-(rows * pack) // 128) * 128
    per_chunk = chunk // owner_len
    grid_spec = pltpu.PrefetchScalarGridSpec(
        num_scalar_prefetch=1,
        grid=(group_steps + entries // chunk,),
        in_specs=[
            pl.BlockSpec((fields, 2 * step * pack, lanes), lambda j, idx: (0, jnp.minimum(j, group_steps - 1), 0)),
            pl.BlockSpec((fields, step * pack, lanes), lambda j, idx: (0, jnp.minimum(j, group_steps - 1), 0)),
            pl.BlockSpec((1, chunk), lambda j, idx: (0, jnp.maximum(j - group_steps, 0))),
        ],
        out_specs=pl.BlockSpec((per_chunk, rows, owner_len), lambda j, idx: (jnp.maximum(j - group_steps, 0), 0, 0)),
        scratch_shapes=[pltpu.VMEM((groups // pack * lanes // 8 + 1, 8, width), xs.dtype), pltpu.VMEM((chunk // 8, 8, width), xs.dtype)],
    )
    return pl.pallas_call(
        pick_kernel(group_steps, step, chunk, owner_len, pack),
        out_shape=jax.ShapeDtypeStruct((entries // owner_len, rows, owner_len), xs.dtype),
        grid_spec=grid_spec,
    )(flat, xv, xs, sel)


def model_tensors(coarse):
    values = coarse.astype(jnp.float32)
    points = values.shape[-1]
    values = values.reshape(values.shape[0] // 3, 3, points)
    velocity = values[:3]
    species = values[3:]
    stress = [
        jnp.sum(velocity[first_comp] * velocity[second_comp], axis=0)
        for first_comp, second_comp in upper_pairs
    ]
    species_flux = jnp.sum(species[:, None, :, :] * velocity[None, :, :, :], axis=2)
    joined = jnp.concatenate([jnp.stack(stress, axis=0), species_flux.reshape(-1, points)], axis=0)
    return (model_coeff * joined).astype(jnp.bfloat16)


def window(at, count, coarse):
    reach = (count + 19) // 8 + 4
    if count % 8 or reach >= coarse:
        return 0, coarse
    return at * (count // 8) - 3, reach


def make_shards(row_count, col_count):
    def shards(fields, front_cells):
        field_count, local_x, local_y, z_length = fields.shape
        devices = row_count * col_count
        full_x = local_x * row_count
        full_y = local_y * col_count
        coarse_x = full_x // 8
        coarse_y = full_y // 8
        coarse_z = z_length // 8
        slab = coarse_z // devices
        slots = front_cells.shape[2]
        row = lax.axis_index("rows")
        col = lax.axis_index("cols")
        me = row * col_count + col

        copies = jnp.broadcast_to(front_cells, (devices,) + front_cells.shape[1:])
        every_cell = lax.all_to_all(copies, ("rows", "cols"), split_axis=0, concat_axis=0, tiled=True)

        x_base, x_count = window(row, local_x, coarse_x)
        y_base, y_count = window(col, local_y, coarse_y)
        wx = jnp.asarray(window_tables(row_count, local_x, full_x))[row]
        wy = jnp.asarray(window_tables(col_count, local_y, full_y))[col]
        group = x_count * y_count
        pack = 3
        padded = -(-group // (8 * pack)) * 8 * pack
        xs = jnp.stack([wx[1], wx[0], wx[0]])
        ys = jnp.stack([wy[0], wy[1], wy[0]])
        weights = xs[:, :, None, :, None] * ys[:, None, :, None, :]
        weights = weights.reshape(3, group, local_x * local_y)
        weights = jnp.pad(weights, ((0, 0), (0, padded - group), (0, 0)))
        weights = jnp.concatenate([jnp.transpose(weights[:2], (1, 0, 2)).reshape(2 * padded, -1), weights[2]], axis=0)
        fields3 = fields.reshape(field_count, local_x * local_y, z_length)
        partials = filtered_partials(fields3, weights)

        by_owner = jnp.transpose(every_cell, (1, 0, 2))
        holder = lax.broadcasted_iota(jnp.int32, by_owner.shape, 1)
        clipped = jnp.clip(by_owner, 0, coarse_x * coarse_y * slab - 1)
        cell_pq = clipped // slab
        at_z = holder * slab + clipped % slab
        at_x = (cell_pq // coarse_y - x_base) % coarse_x
        at_y = (cell_pq % coarse_y - y_base) % coarse_y
        inside = (at_x < x_count) & (at_y < y_count) & (by_owner >= 0)
        at_group = at_x * y_count + at_y
        flat = jnp.where(inside, (at_group // pack) * coarse_z + at_z, padded // pack * coarse_z)
        sel = jnp.where(inside, at_group % pack, 0).reshape(1, -1)
        owner_len = devices * slots
        value_part, slope_part = partials
        taken = pick_cells(value_part, slope_part, flat.reshape(-1), sel, owner_len, pack)
        arrived = lax.all_to_all(taken, ("rows", "cols"), split_axis=0, concat_axis=0, tiled=True)
        summed = jnp.sum(arrived, axis=0)
        rounded = lax.reduce_precision(summed, exponent_bits=8, mantissa_bits=7)
        mine = lax.dynamic_index_in_dim(by_owner, me, axis=0, keepdims=False).reshape(-1)
        picked = jnp.where(mine[None, :] >= 0, rounded, jnp.zeros_like(rounded))
        return model_tensors(picked)[None]

    return shards


def solution(mesh):
    in_specs = (P(None, "rows", "cols", None), P(("rows", "cols"), None, None))
    out_specs = P(("rows", "cols"), None, None)
    shards = make_shards(mesh.shape["rows"], mesh.shape["cols"])
    return jax.shard_map(shards, mesh=mesh, in_specs=in_specs, out_specs=out_specs, check_vma=False)
```

```python
import numpy as np
import jax
import jax.numpy as jnp
import ml_dtypes
from jax import lax
from jax.sharding import PartitionSpec as P
from jax.experimental import pallas as pl
from jax.experimental.pallas import tpu as pltpu

first_tap = -20
last_tap = 27
sigma_sq = 256.0 / 12.0
coarse_step = 8.0
model_coeff = 1.0 / 3.0
upper_pairs = ((0, 0), (0, 1), (0, 2), (1, 1), (1, 2), (2, 2))
block_len = 1024
halo = 128


def tap_weights(offsets):
    f32 = np.float32
    every_tap = np.arange(first_tap, last_tap + 1).astype(f32)
    weight_sum = np.sum(np.exp(-(every_tap - f32(3.5)) * (every_tap - f32(3.5)) / f32(2.0 * sigma_sq)), dtype=f32)
    shifted = offsets.astype(f32) - f32(3.5)
    inside = (offsets >= first_tap) & (offsets <= last_tap)
    gauss = np.where(inside, np.exp(-shifted * shifted / f32(2.0 * sigma_sq)), f32(0.0)).astype(f32) / weight_sum
    slope = (f32(-coarse_step) * shifted / f32(sigma_sq) * gauss).astype(f32)
    bf = ml_dtypes.bfloat16
    return gauss.astype(bf).astype(f32), slope.astype(bf).astype(f32)


def line_matrices(length):
    fine_pos = np.arange(length)[:, None]
    coarse_pos = np.arange(length // 8)[None, :]
    offsets = np.mod(fine_pos - 8 * coarse_pos, length)
    offsets = np.where(offsets >= length // 2, offsets - length, offsets)
    return tap_weights(offsets)


def z_tables(length):
    coarse = np.arange(length // 8)[None, :]
    main = np.arange(length)[:, None] - 8 * coarse
    prev = np.arange(halo)[:, None] - halo - 8 * coarse
    nxt = np.arange(halo)[:, None] + length - 8 * coarse
    return [tap_weights(o) for o in (main, prev, nxt)]


def filter_kernel(block_count, coarse_block, value_rows, slope_rows):
    def body(x_ref, main_ref, halo_ref, w_ref, ov_ref, os_ref, zv_ref, zs_ref):
        per_step, rows, length = x_ref.shape
        blen = length // block_count
        for b in range(block_count):
            main = x_ref[:, :, b * blen:(b + 1) * blen].reshape(per_step * rows, blen)
            start = (b * blen - halo) % length
            tail = x_ref[:, :, start:start + halo].reshape(per_step * rows, halo)
            start = ((b + 1) * blen) % length
            head = x_ref[:, :, start:start + halo].reshape(per_step * rows, halo)
            edges = jnp.concatenate([tail, head], axis=1)
            acc = jnp.dot(main, main_ref[...], preferred_element_type=jnp.float32)
            acc = acc + jnp.dot(edges, halo_ref[...], preferred_element_type=jnp.float32)
            lanes = slice(b * coarse_block, (b + 1) * coarse_block)
            zv_ref[:, lanes] = acc[:, :coarse_block].astype(jnp.bfloat16)
            zs_ref[:, lanes] = acc[:, coarse_block:].astype(jnp.bfloat16)
        for k in range(per_step):
            zv = zv_ref[k * rows:(k + 1) * rows, :]
            zs = zs_ref[k * rows:(k + 1) * rows, :]
            pv = jnp.dot(w_ref[0, :value_rows, :], zv, preferred_element_type=jnp.float32)
            pv = pv + jnp.dot(w_ref[1, :value_rows, :], zv, preferred_element_type=jnp.float32)
            ps = jnp.dot(w_ref[0, value_rows:, :], zs, preferred_element_type=jnp.float32)
            ps = ps + jnp.dot(w_ref[1, value_rows:, :], zs, preferred_element_type=jnp.float32)
            ov_ref[k] = pv
            os_ref[k] = ps

    return body


def split_hi_lo(w):
    hi = w.astype(jnp.bfloat16)
    lo = (w - hi.astype(jnp.float32)).astype(jnp.bfloat16)
    return jnp.stack([hi, lo], axis=0)


def filtered_partials(fields3, weights):
    field_count, rows, length = fields3.shape
    blen = block_len if (length % block_len == 0 and length > block_len) else length
    block_count = length // blen
    coarse_block = blen // 8
    tables = z_tables(blen)
    joined = [np.concatenate([t[0], t[1]], axis=1) for t in tables]
    main = jnp.asarray(joined[0], jnp.bfloat16)
    halo_w = jnp.asarray(np.concatenate([joined[1], joined[2]], axis=0), jnp.bfloat16)
    w = split_hi_lo(weights)
    total_rows = w.shape[1]
    value_rows = total_rows // 3 * 2
    coarse = length // 8
    per_step = 4 if field_count % 4 == 0 else 1
    const = lambda f: (0, 0)
    return pl.pallas_call(
        filter_kernel(block_count, coarse_block, value_rows, total_rows - value_rows),
        out_shape=[
            jax.ShapeDtypeStruct((field_count, value_rows, coarse), jnp.float32),
            jax.ShapeDtypeStruct((field_count, total_rows - value_rows, coarse), jnp.float32),
        ],
        grid=(field_count // per_step,),
        in_specs=[
            pl.BlockSpec((per_step, rows, length), lambda f: (f, 0, 0)),
            pl.BlockSpec(main.shape, const),
            pl.BlockSpec(halo_w.shape, const),
            pl.BlockSpec(w.shape, lambda f: (0, 0, 0)),
        ],
        out_specs=[
            pl.BlockSpec((per_step, value_rows, coarse), lambda f: (f, 0, 0)),
            pl.BlockSpec((per_step, total_rows - value_rows, coarse), lambda f: (f, 0, 0)),
        ],
        scratch_shapes=[pltpu.VMEM((per_step * rows, coarse), jnp.bfloat16)] * 2,
    )(fields3, main, halo_w, w)


def window_tables(blocks, count, full):
    smooth, deriv = line_matrices(full)
    coarse = full // 8
    out = []
    for at in range(blocks):
        base, width = window(at, count, coarse)
        picks = (base + np.arange(width)) % coarse
        part = slice(at * count, (at + 1) * count)
        out.append(np.stack([smooth[part][:, picks].T, deriv[part][:, picks].T]))
    return np.stack(out)


def pick_kernel(group_steps, step, chunk, owner_len, pack):
    def body(idx_ref, xv_ref, xs_ref, sel_ref, o_ref, tab_ref, buf_ref):
        j = pl.program_id(0)
        fields = xv_ref.shape[0]
        lanes = xv_ref.shape[2]
        width = tab_ref.shape[2]
        per_field = 3 * pack

        @pl.when(j < group_steps)
        def _():
            for t in range(step):
                parts = []
                for f in range(fields):
                    parts.append(xv_ref[f, 2 * pack * t:2 * pack * (t + 1), :])
                    parts.append(xs_ref[f, pack * t:pack * (t + 1), :])
                parts.append(jnp.zeros((width - fields * per_field, lanes), xv_ref.dtype))
                slab = jnp.concatenate(parts, axis=0)
                at = pl.multiple_of((j * step + t) * (lanes // 8), lanes // 8)
                tab_ref[pl.ds(at, lanes // 8), :, :] = slab.T.reshape(lanes // 8, 8, width)

        @pl.when(j == group_steps - 1)
        def _():
            tab_ref[tab_ref.shape[0] - 1] = jnp.zeros((8, width), tab_ref.dtype)

        @pl.when(j >= group_steps)
        def _():
            base = (j - group_steps) * chunk

            def eight(i, carry):
                for k in range(8):
                    code = idx_ref[base + i * 8 + k]
                    tile = lax.shift_right_logical(code, 3)
                    row = tab_ref[tile, pl.ds(code & 7, 1), :]
                    buf_ref[i, pl.ds(k, 1), :] = row
                return carry

            lax.fori_loop(0, chunk // 8, eight, 0, unroll=16)
            flipped = buf_ref[...].reshape(chunk, width).T
            sel = sel_ref[...]
            picked = []
            for f in range(fields):
                for m in range(3):
                    choices = []
                    for k in range(pack):
                        at = f * per_field + (2 * k + m if m < 2 else 2 * pack + k)
                        choices.append(flipped[at:at + 1])
                    row = choices[0]
                    for k in range(1, pack):
                        row = jnp.where(sel == k, choices[k], row)
                    picked.append(row)
            picked = jnp.concatenate(picked, axis=0)
            for owner in range(chunk // owner_len):
                o_ref[owner] = picked[:, owner * owner_len:(owner + 1) * owner_len]

    return body


def pick_cells(xv, xs, flat, sel, owner_len, pack, chunk=2048):
    fields, groups, lanes = xs.shape
    rows = fields * 3
    step = 8
    group_steps = groups // (step * pack)
    entries = flat.shape[0]
    chunk = min(chunk, entries)
    width = -(-(rows * pack) // 128) * 128
    per_chunk = chunk // owner_len
    grid_spec = pltpu.PrefetchScalarGridSpec(
        num_scalar_prefetch=1,
        grid=(group_steps + entries // chunk,),
        in_specs=[
            pl.BlockSpec((fields, 2 * step * pack, lanes), lambda j, idx: (0, jnp.minimum(j, group_steps - 1), 0)),
            pl.BlockSpec((fields, step * pack, lanes), lambda j, idx: (0, jnp.minimum(j, group_steps - 1), 0)),
            pl.BlockSpec((1, chunk), lambda j, idx: (0, jnp.maximum(j - group_steps, 0))),
        ],
        out_specs=pl.BlockSpec((per_chunk, rows, owner_len), lambda j, idx: (jnp.maximum(j - group_steps, 0), 0, 0)),
        scratch_shapes=[pltpu.VMEM((groups // pack * lanes // 8 + 1, 8, width), xs.dtype), pltpu.VMEM((chunk // 8, 8, width), xs.dtype)],
    )
    return pl.pallas_call(
        pick_kernel(group_steps, step, chunk, owner_len, pack),
        out_shape=jax.ShapeDtypeStruct((entries // owner_len, rows, owner_len), xs.dtype),
        grid_spec=grid_spec,
    )(flat, xv, xs, sel)


def model_tensors(coarse):
    values = coarse.astype(jnp.float32)
    points = values.shape[-1]
    values = values.reshape(values.shape[0] // 3, 3, points)
    velocity = values[:3]
    species = values[3:]
    stress = [
        jnp.sum(velocity[first_comp] * velocity[second_comp], axis=0)
        for first_comp, second_comp in upper_pairs
    ]
    species_flux = jnp.sum(species[:, None, :, :] * velocity[None, :, :, :], axis=2)
    joined = jnp.concatenate([jnp.stack(stress, axis=0), species_flux.reshape(-1, points)], axis=0)
    return (model_coeff * joined).astype(jnp.bfloat16)


def window(at, count, coarse):
    reach = (count + 19) // 8 + 4
    if count % 8 or reach >= coarse:
        return 0, coarse
    return at * (count // 8) - 3, reach


def make_shards(row_count, col_count):
    def shards(fields, front_cells):
        field_count, local_x, local_y, z_length = fields.shape
        devices = row_count * col_count
        full_x = local_x * row_count
        full_y = local_y * col_count
        coarse_x = full_x // 8
        coarse_y = full_y // 8
        coarse_z = z_length // 8
        slab = coarse_z // devices
        slots = front_cells.shape[2]
        row = lax.axis_index("rows")
        col = lax.axis_index("cols")
        me = row * col_count + col

        copies = jnp.broadcast_to(front_cells, (devices,) + front_cells.shape[1:])
        every_cell = lax.all_to_all(copies, ("rows", "cols"), split_axis=0, concat_axis=0, tiled=True)

        x_base, x_count = window(row, local_x, coarse_x)
        y_base, y_count = window(col, local_y, coarse_y)
        wx = jnp.asarray(window_tables(row_count, local_x, full_x))[row]
        wy = jnp.asarray(window_tables(col_count, local_y, full_y))[col]
        group = x_count * y_count
        pack = 3
        padded = -(-group // (8 * pack)) * 8 * pack
        xs = jnp.stack([wx[1], wx[0], wx[0]])
        ys = jnp.stack([wy[0], wy[1], wy[0]])
        weights = xs[:, :, None, :, None] * ys[:, None, :, None, :]
        weights = weights.reshape(3, group, local_x * local_y)
        weights = jnp.pad(weights, ((0, 0), (0, padded - group), (0, 0)))
        weights = jnp.concatenate([jnp.transpose(weights[:2], (1, 0, 2)).reshape(2 * padded, -1), weights[2]], axis=0)
        fields3 = fields.reshape(field_count, local_x * local_y, z_length)
        partials = filtered_partials(fields3, weights)

        by_owner = jnp.transpose(every_cell, (1, 0, 2))
        holder = lax.broadcasted_iota(jnp.int32, by_owner.shape, 1)
        clipped = jnp.clip(by_owner, 0, coarse_x * coarse_y * slab - 1)
        cell_pq = clipped // slab
        at_z = holder * slab + clipped % slab
        at_x = (cell_pq // coarse_y - x_base) % coarse_x
        at_y = (cell_pq % coarse_y - y_base) % coarse_y
        inside = (at_x < x_count) & (at_y < y_count) & (by_owner >= 0)
        at_group = at_x * y_count + at_y
        flat = jnp.where(inside, (at_group // pack) * coarse_z + at_z, padded // pack * coarse_z)
        sel = jnp.where(inside, at_group % pack, 0).reshape(1, -1)
        owner_len = devices * slots
        value_part, slope_part = partials
        taken = pick_cells(value_part, slope_part, flat.reshape(-1), sel, owner_len, pack)
        arrived = lax.all_to_all(taken, ("rows", "cols"), split_axis=0, concat_axis=0, tiled=True)
        summed = jnp.sum(arrived, axis=0)
        rounded = lax.reduce_precision(summed, exponent_bits=8, mantissa_bits=7)
        mine = lax.dynamic_index_in_dim(by_owner, me, axis=0, keepdims=False).reshape(-1)
        picked = jnp.where(mine[None, :] >= 0, rounded, jnp.zeros_like(rounded))
        return model_tensors(picked)[None]

    return shards


def solution(mesh):
    in_specs = (P(None, "rows", "cols", None), P(("rows", "cols"), None, None))
    out_specs = P(("rows", "cols"), None, None)
    shards = make_shards(mesh.shape["rows"], mesh.shape["cols"])
    return jax.shard_map(shards, mesh=mesh, in_specs=in_specs, out_specs=out_specs, check_vma=False)
```

```python
import numpy as np
import jax
import jax.numpy as jnp
import ml_dtypes
from jax import lax
from jax.sharding import PartitionSpec as P
from jax.experimental import pallas as pl
from jax.experimental.pallas import tpu as pltpu

first_tap = -20
last_tap = 27
sigma_sq = 256.0 / 12.0
coarse_step = 8.0
model_coeff = 1.0 / 3.0
upper_pairs = ((0, 0), (0, 1), (0, 2), (1, 1), (1, 2), (2, 2))
block_len = 1024
halo = 128


def tap_weights(offsets):
    f32 = np.float32
    every_tap = np.arange(first_tap, last_tap + 1).astype(f32)
    weight_sum = np.sum(np.exp(-(every_tap - f32(3.5)) * (every_tap - f32(3.5)) / f32(2.0 * sigma_sq)), dtype=f32)
    shifted = offsets.astype(f32) - f32(3.5)
    inside = (offsets >= first_tap) & (offsets <= last_tap)
    gauss = np.where(inside, np.exp(-shifted * shifted / f32(2.0 * sigma_sq)), f32(0.0)).astype(f32) / weight_sum
    slope = (f32(-coarse_step) * shifted / f32(sigma_sq) * gauss).astype(f32)
    bf = ml_dtypes.bfloat16
    return gauss.astype(bf).astype(f32), slope.astype(bf).astype(f32)


def line_matrices(length):
    fine_pos = np.arange(length)[:, None]
    coarse_pos = np.arange(length // 8)[None, :]
    offsets = np.mod(fine_pos - 8 * coarse_pos, length)
    offsets = np.where(offsets >= length // 2, offsets - length, offsets)
    return tap_weights(offsets)


def z_tables(length):
    coarse = np.arange(length // 8)[None, :]
    main = np.arange(length)[:, None] - 8 * coarse
    prev = np.arange(halo)[:, None] - halo - 8 * coarse
    nxt = np.arange(halo)[:, None] + length - 8 * coarse
    return [tap_weights(o) for o in (main, prev, nxt)]


def filter_kernel(block_count, coarse_block, value_rows, slope_rows):
    def body(x_ref, main_ref, halo_ref, w_ref, ov_ref, os_ref, zv_ref, zs_ref):
        per_step, rows, length = x_ref.shape
        blen = length // block_count
        for b in range(block_count):
            main = x_ref[:, :, b * blen:(b + 1) * blen].reshape(per_step * rows, blen)
            start = (b * blen - halo) % length
            tail = x_ref[:, :, start:start + halo].reshape(per_step * rows, halo)
            start = ((b + 1) * blen) % length
            head = x_ref[:, :, start:start + halo].reshape(per_step * rows, halo)
            edges = jnp.concatenate([tail, head], axis=1)
            acc = jnp.dot(main, main_ref[...], preferred_element_type=jnp.float32)
            acc = acc + jnp.dot(edges, halo_ref[...], preferred_element_type=jnp.float32)
            lanes = slice(b * coarse_block, (b + 1) * coarse_block)
            zv_ref[:, lanes] = acc[:, :coarse_block].astype(jnp.bfloat16)
            zs_ref[:, lanes] = acc[:, coarse_block:].astype(jnp.bfloat16)
        for k in range(per_step):
            zv = zv_ref[k * rows:(k + 1) * rows, :]
            zs = zs_ref[k * rows:(k + 1) * rows, :]
            pv = jnp.dot(w_ref[0, :value_rows, :], zv, preferred_element_type=jnp.float32)
            pv = pv + jnp.dot(w_ref[1, :value_rows, :], zv, preferred_element_type=jnp.float32)
            ps = jnp.dot(w_ref[0, value_rows:, :], zs, preferred_element_type=jnp.float32)
            ps = ps + jnp.dot(w_ref[1, value_rows:, :], zs, preferred_element_type=jnp.float32)
            ov_ref[k] = pv
            os_ref[k] = ps

    return body


def split_hi_lo(w):
    hi = w.astype(jnp.bfloat16)
    lo = (w - hi.astype(jnp.float32)).astype(jnp.bfloat16)
    return jnp.stack([hi, lo], axis=0)


def filtered_partials(fields3, weights):
    field_count, rows, length = fields3.shape
    blen = block_len if (length % block_len == 0 and length > block_len) else length
    block_count = length // blen
    coarse_block = blen // 8
    tables = z_tables(blen)
    joined = [np.concatenate([t[0], t[1]], axis=1) for t in tables]
    main = jnp.asarray(joined[0], jnp.bfloat16)
    halo_w = jnp.asarray(np.concatenate([joined[1], joined[2]], axis=0), jnp.bfloat16)
    w = split_hi_lo(weights)
    total_rows = w.shape[1]
    value_rows = total_rows // 3 * 2
    coarse = length // 8
    per_step = 4 if field_count % 4 == 0 else 1
    const = lambda f: (0, 0)
    return pl.pallas_call(
        filter_kernel(block_count, coarse_block, value_rows, total_rows - value_rows),
        out_shape=[
            jax.ShapeDtypeStruct((field_count, value_rows, coarse), jnp.float32),
            jax.ShapeDtypeStruct((field_count, total_rows - value_rows, coarse), jnp.float32),
        ],
        grid=(field_count // per_step,),
        in_specs=[
            pl.BlockSpec((per_step, rows, length), lambda f: (f, 0, 0)),
            pl.BlockSpec(main.shape, const),
            pl.BlockSpec(halo_w.shape, const),
            pl.BlockSpec(w.shape, lambda f: (0, 0, 0)),
        ],
        out_specs=[
            pl.BlockSpec((per_step, value_rows, coarse), lambda f: (f, 0, 0)),
            pl.BlockSpec((per_step, total_rows - value_rows, coarse), lambda f: (f, 0, 0)),
        ],
        scratch_shapes=[pltpu.VMEM((per_step * rows, coarse), jnp.bfloat16)] * 2,
    )(fields3, main, halo_w, w)


def window_tables(blocks, count, full):
    smooth, deriv = line_matrices(full)
    coarse = full // 8
    out = []
    for at in range(blocks):
        base, width = window(at, count, coarse)
        picks = (base + np.arange(width)) % coarse
        part = slice(at * count, (at + 1) * count)
        out.append(np.stack([smooth[part][:, picks].T, deriv[part][:, picks].T]))
    return np.stack(out)


def pick_kernel(group_steps, step, chunk, owner_len, pack):
    def body(idx_ref, xv_ref, xs_ref, sel_ref, o_ref, tab_ref, buf_ref):
        j = pl.program_id(0)
        fields = xv_ref.shape[0]
        lanes = xv_ref.shape[2]
        width = tab_ref.shape[2]
        per_field = 3 * pack

        @pl.when(j < group_steps)
        def _():
            for t in range(step):
                parts = []
                for f in range(fields):
                    parts.append(xv_ref[f, 2 * pack * t:2 * pack * (t + 1), :])
                    parts.append(xs_ref[f, pack * t:pack * (t + 1), :])
                parts.append(jnp.zeros((width - fields * per_field, lanes), xv_ref.dtype))
                slab = jnp.concatenate(parts, axis=0)
                at = pl.multiple_of((j * step + t) * (lanes // 8), lanes // 8)
                tab_ref[pl.ds(at, lanes // 8), :, :] = slab.T.reshape(lanes // 8, 8, width)

        @pl.when(j == group_steps - 1)
        def _():
            tab_ref[tab_ref.shape[0] - 1] = jnp.zeros((8, width), tab_ref.dtype)

        @pl.when(j >= group_steps)
        def _():
            base = (j - group_steps) * chunk

            def eight(i, carry):
                for k in range(8):
                    code = idx_ref[base + i * 8 + k]
                    tile = lax.shift_right_logical(code, 3)
                    row = tab_ref[tile, pl.ds(code & 7, 1), :]
                    buf_ref[i, pl.ds(k, 1), :] = row
                return carry

            lax.fori_loop(0, chunk // 8, eight, 0, unroll=16)
            flipped = buf_ref[...].reshape(chunk, width).T
            sel = sel_ref[...]
            picked = []
            for f in range(fields):
                for m in range(3):
                    choices = []
                    for k in range(pack):
                        at = f * per_field + (2 * k + m if m < 2 else 2 * pack + k)
                        choices.append(flipped[at:at + 1])
                    row = choices[0]
                    for k in range(1, pack):
                        row = jnp.where(sel == k, choices[k], row)
                    picked.append(row)
            picked = jnp.concatenate(picked, axis=0)
            for owner in range(chunk // owner_len):
                o_ref[owner] = picked[:, owner * owner_len:(owner + 1) * owner_len]

    return body


def pick_cells(xv, xs, flat, sel, owner_len, pack, chunk=4096):
    fields, groups, lanes = xs.shape
    rows = fields * 3
    step = 8
    group_steps = groups // (step * pack)
    entries = flat.shape[0]
    chunk = min(chunk, entries)
    width = -(-(rows * pack) // 128) * 128
    per_chunk = chunk // owner_len
    grid_spec = pltpu.PrefetchScalarGridSpec(
        num_scalar_prefetch=1,
        grid=(group_steps + entries // chunk,),
        in_specs=[
            pl.BlockSpec((fields, 2 * step * pack, lanes), lambda j, idx: (0, jnp.minimum(j, group_steps - 1), 0)),
            pl.BlockSpec((fields, step * pack, lanes), lambda j, idx: (0, jnp.minimum(j, group_steps - 1), 0)),
            pl.BlockSpec((1, chunk), lambda j, idx: (0, jnp.maximum(j - group_steps, 0))),
        ],
        out_specs=pl.BlockSpec((per_chunk, rows, owner_len), lambda j, idx: (jnp.maximum(j - group_steps, 0), 0, 0)),
        scratch_shapes=[pltpu.VMEM((groups // pack * lanes // 8 + 1, 8, width), xs.dtype), pltpu.VMEM((chunk // 8, 8, width), xs.dtype)],
    )
    return pl.pallas_call(
        pick_kernel(group_steps, step, chunk, owner_len, pack),
        out_shape=jax.ShapeDtypeStruct((entries // owner_len, rows, owner_len), xs.dtype),
        grid_spec=grid_spec,
    )(flat, xv, xs, sel)


def model_tensors(coarse):
    values = coarse.astype(jnp.float32)
    points = values.shape[-1]
    values = values.reshape(values.shape[0] // 3, 3, points)
    velocity = values[:3]
    species = values[3:]
    stress = [
        jnp.sum(velocity[first_comp] * velocity[second_comp], axis=0)
        for first_comp, second_comp in upper_pairs
    ]
    species_flux = jnp.sum(species[:, None, :, :] * velocity[None, :, :, :], axis=2)
    joined = jnp.concatenate([jnp.stack(stress, axis=0), species_flux.reshape(-1, points)], axis=0)
    return (model_coeff * joined).astype(jnp.bfloat16)


def window(at, count, coarse):
    reach = (count + 19) // 8 + 4
    if count % 8 or reach >= coarse:
        return 0, coarse
    return at * (count // 8) - 3, reach


def make_shards(row_count, col_count):
    def shards(fields, front_cells):
        field_count, local_x, local_y, z_length = fields.shape
        devices = row_count * col_count
        full_x = local_x * row_count
        full_y = local_y * col_count
        coarse_x = full_x // 8
        coarse_y = full_y // 8
        coarse_z = z_length // 8
        slab = coarse_z // devices
        slots = front_cells.shape[2]
        row = lax.axis_index("rows")
        col = lax.axis_index("cols")
        me = row * col_count + col

        copies = jnp.broadcast_to(front_cells, (devices,) + front_cells.shape[1:])
        every_cell = lax.all_to_all(copies, ("rows", "cols"), split_axis=0, concat_axis=0, tiled=True)

        x_base, x_count = window(row, local_x, coarse_x)
        y_base, y_count = window(col, local_y, coarse_y)
        wx = jnp.asarray(window_tables(row_count, local_x, full_x))[row]
        wy = jnp.asarray(window_tables(col_count, local_y, full_y))[col]
        group = x_count * y_count
        pack = 3
        padded = -(-group // (8 * pack)) * 8 * pack
        xs = jnp.stack([wx[1], wx[0], wx[0]])
        ys = jnp.stack([wy[0], wy[1], wy[0]])
        weights = xs[:, :, None, :, None] * ys[:, None, :, None, :]
        weights = weights.reshape(3, group, local_x * local_y)
        weights = jnp.pad(weights, ((0, 0), (0, padded - group), (0, 0)))
        weights = jnp.concatenate([jnp.transpose(weights[:2], (1, 0, 2)).reshape(2 * padded, -1), weights[2]], axis=0)
        fields3 = fields.reshape(field_count, local_x * local_y, z_length)
        partials = filtered_partials(fields3, weights)

        by_owner = jnp.transpose(every_cell, (1, 0, 2))
        holder = lax.broadcasted_iota(jnp.int32, by_owner.shape, 1)
        clipped = jnp.clip(by_owner, 0, coarse_x * coarse_y * slab - 1)
        cell_pq = clipped // slab
        at_z = holder * slab + clipped % slab
        at_x = (cell_pq // coarse_y - x_base) % coarse_x
        at_y = (cell_pq % coarse_y - y_base) % coarse_y
        inside = (at_x < x_count) & (at_y < y_count) & (by_owner >= 0)
        at_group = at_x * y_count + at_y
        flat = jnp.where(inside, (at_group // pack) * coarse_z + at_z, padded // pack * coarse_z)
        sel = jnp.where(inside, at_group % pack, 0).reshape(1, -1)
        owner_len = devices * slots
        value_part, slope_part = partials
        taken = pick_cells(value_part, slope_part, flat.reshape(-1), sel, owner_len, pack)
        arrived = lax.all_to_all(taken, ("rows", "cols"), split_axis=0, concat_axis=0, tiled=True)
        summed = jnp.sum(arrived, axis=0)
        rounded = lax.reduce_precision(summed, exponent_bits=8, mantissa_bits=7)
        mine = lax.dynamic_index_in_dim(by_owner, me, axis=0, keepdims=False).reshape(-1)
        picked = jnp.where(mine[None, :] >= 0, rounded, jnp.zeros_like(rounded))
        return model_tensors(picked)[None]

    return shards


def solution(mesh):
    in_specs = (P(None, "rows", "cols", None), P(("rows", "cols"), None, None))
    out_specs = P(("rows", "cols"), None, None)
    shards = make_shards(mesh.shape["rows"], mesh.shape["cols"])
    return jax.shard_map(shards, mesh=mesh, in_specs=in_specs, out_specs=out_specs, check_vma=False)
```

```python
import numpy as np
import jax
import jax.numpy as jnp
import ml_dtypes
from jax import lax
from jax.sharding import PartitionSpec as P
from jax.experimental import pallas as pl
from jax.experimental.pallas import tpu as pltpu

first_tap = -20
last_tap = 27
sigma_sq = 256.0 / 12.0
coarse_step = 8.0
model_coeff = 1.0 / 3.0
upper_pairs = ((0, 0), (0, 1), (0, 2), (1, 1), (1, 2), (2, 2))
block_len = 1024
halo = 128


def tap_weights(offsets):
    f32 = np.float32
    every_tap = np.arange(first_tap, last_tap + 1).astype(f32)
    weight_sum = np.sum(np.exp(-(every_tap - f32(3.5)) * (every_tap - f32(3.5)) / f32(2.0 * sigma_sq)), dtype=f32)
    shifted = offsets.astype(f32) - f32(3.5)
    inside = (offsets >= first_tap) & (offsets <= last_tap)
    gauss = np.where(inside, np.exp(-shifted * shifted / f32(2.0 * sigma_sq)), f32(0.0)).astype(f32) / weight_sum
    slope = (f32(-coarse_step) * shifted / f32(sigma_sq) * gauss).astype(f32)
    bf = ml_dtypes.bfloat16
    return gauss.astype(bf).astype(f32), slope.astype(bf).astype(f32)


def line_matrices(length):
    fine_pos = np.arange(length)[:, None]
    coarse_pos = np.arange(length // 8)[None, :]
    offsets = np.mod(fine_pos - 8 * coarse_pos, length)
    offsets = np.where(offsets >= length // 2, offsets - length, offsets)
    return tap_weights(offsets)


def z_tables(length):
    coarse = np.arange(length // 8)[None, :]
    main = np.arange(length)[:, None] - 8 * coarse
    prev = np.arange(halo)[:, None] - halo - 8 * coarse
    nxt = np.arange(halo)[:, None] + length - 8 * coarse
    return [tap_weights(o) for o in (main, prev, nxt)]


def filter_kernel(block_count, coarse_block, value_rows, slope_rows):
    def body(x_ref, main_ref, halo_ref, w_ref, ov_ref, os_ref, zv_ref, zs_ref):
        per_step, rows, length = x_ref.shape
        blen = length // block_count
        for b in range(block_count):
            main = x_ref[:, :, b * blen:(b + 1) * blen].reshape(per_step * rows, blen)
            start = (b * blen - halo) % length
            tail = x_ref[:, :, start:start + halo].reshape(per_step * rows, halo)
            start = ((b + 1) * blen) % length
            head = x_ref[:, :, start:start + halo].reshape(per_step * rows, halo)
            edges = jnp.concatenate([tail, head], axis=1)
            acc = jnp.dot(main, main_ref[...], preferred_element_type=jnp.float32)
            acc = acc + jnp.dot(edges, halo_ref[...], preferred_element_type=jnp.float32)
            lanes = slice(b * coarse_block, (b + 1) * coarse_block)
            zv_ref[:, lanes] = acc[:, :coarse_block].astype(jnp.bfloat16)
            zs_ref[:, lanes] = acc[:, coarse_block:].astype(jnp.bfloat16)
        for k in range(per_step):
            zv = zv_ref[k * rows:(k + 1) * rows, :]
            zs = zs_ref[k * rows:(k + 1) * rows, :]
            pv = jnp.dot(w_ref[0, :value_rows, :], zv, preferred_element_type=jnp.float32)
            pv = pv + jnp.dot(w_ref[1, :value_rows, :], zv, preferred_element_type=jnp.float32)
            ps = jnp.dot(w_ref[0, value_rows:, :], zs, preferred_element_type=jnp.float32)
            ps = ps + jnp.dot(w_ref[1, value_rows:, :], zs, preferred_element_type=jnp.float32)
            ov_ref[k] = pv
            os_ref[k] = ps

    return body


def split_hi_lo(w):
    hi = w.astype(jnp.bfloat16)
    lo = (w - hi.astype(jnp.float32)).astype(jnp.bfloat16)
    return jnp.stack([hi, lo], axis=0)


def filtered_partials(fields3, weights):
    field_count, rows, length = fields3.shape
    blen = block_len if (length % block_len == 0 and length > block_len) else length
    block_count = length // blen
    coarse_block = blen // 8
    tables = z_tables(blen)
    joined = [np.concatenate([t[0], t[1]], axis=1) for t in tables]
    main = jnp.asarray(joined[0], jnp.bfloat16)
    halo_w = jnp.asarray(np.concatenate([joined[1], joined[2]], axis=0), jnp.bfloat16)
    w = split_hi_lo(weights)
    total_rows = w.shape[1]
    value_rows = total_rows // 3 * 2
    coarse = length // 8
    per_step = 4 if field_count % 4 == 0 else 1
    const = lambda f: (0, 0)
    return pl.pallas_call(
        filter_kernel(block_count, coarse_block, value_rows, total_rows - value_rows),
        out_shape=[
            jax.ShapeDtypeStruct((field_count, value_rows, coarse), jnp.float32),
            jax.ShapeDtypeStruct((field_count, total_rows - value_rows, coarse), jnp.float32),
        ],
        grid=(field_count // per_step,),
        in_specs=[
            pl.BlockSpec((per_step, rows, length), lambda f: (f, 0, 0)),
            pl.BlockSpec(main.shape, const),
            pl.BlockSpec(halo_w.shape, const),
            pl.BlockSpec(w.shape, lambda f: (0, 0, 0)),
        ],
        out_specs=[
            pl.BlockSpec((per_step, value_rows, coarse), lambda f: (f, 0, 0)),
            pl.BlockSpec((per_step, total_rows - value_rows, coarse), lambda f: (f, 0, 0)),
        ],
        scratch_shapes=[pltpu.VMEM((per_step * rows, coarse), jnp.bfloat16)] * 2,
    )(fields3, main, halo_w, w)


def window_tables(blocks, count, full):
    smooth, deriv = line_matrices(full)
    coarse = full // 8
    out = []
    for at in range(blocks):
        base, width = window(at, count, coarse)
        picks = (base + np.arange(width)) % coarse
        part = slice(at * count, (at + 1) * count)
        out.append(np.stack([smooth[part][:, picks].T, deriv[part][:, picks].T]))
    return np.stack(out)


def pick_kernel(group_steps, step, chunk, owner_len, pack):
    def body(idx_ref, xv_ref, xs_ref, sel_ref, o_ref, tab_ref, buf_ref):
        j = pl.program_id(0)
        fields = xv_ref.shape[0]
        lanes = xv_ref.shape[2]
        width = tab_ref.shape[2]
        per_field = 3 * pack

        @pl.when(j < group_steps)
        def _():
            for t in range(step):
                parts = []
                for f in range(fields):
                    parts.append(xv_ref[f, 2 * pack * t:2 * pack * (t + 1), :])
                    parts.append(xs_ref[f, pack * t:pack * (t + 1), :])
                parts.append(jnp.zeros((width - fields * per_field, lanes), xv_ref.dtype))
                slab = jnp.concatenate(parts, axis=0)
                at = pl.multiple_of((j * step + t) * (lanes // 8), lanes // 8)
                tab_ref[pl.ds(at, lanes // 8), :, :] = slab.T.reshape(lanes // 8, 8, width)

        @pl.when(j == group_steps - 1)
        def _():
            tab_ref[tab_ref.shape[0] - 1] = jnp.zeros((8, width), tab_ref.dtype)

        @pl.when(j >= group_steps)
        def _():
            base = (j - group_steps) * chunk

            def eight(i, carry):
                for k in range(8):
                    code = idx_ref[base + i * 8 + k]
                    tile = lax.shift_right_logical(code, 3)
                    row = tab_ref[tile, pl.ds(code & 7, 1), :]
                    buf_ref[i, pl.ds(k, 1), :] = row
                return carry

            lax.fori_loop(0, chunk // 8, eight, 0, unroll=32)
            flipped = buf_ref[...].reshape(chunk, width).T
            sel = sel_ref[...]
            picked = []
            for f in range(fields):
                for m in range(3):
                    choices = []
                    for k in range(pack):
                        at = f * per_field + (2 * k + m if m < 2 else 2 * pack + k)
                        choices.append(flipped[at:at + 1])
                    row = choices[0]
                    for k in range(1, pack):
                        row = jnp.where(sel == k, choices[k], row)
                    picked.append(row)
            picked = jnp.concatenate(picked, axis=0)
            for owner in range(chunk // owner_len):
                o_ref[owner] = picked[:, owner * owner_len:(owner + 1) * owner_len]

    return body


def pick_cells(xv, xs, flat, sel, owner_len, pack, chunk=4096):
    fields, groups, lanes = xs.shape
    rows = fields * 3
    step = 8
    group_steps = groups // (step * pack)
    entries = flat.shape[0]
    chunk = min(chunk, entries)
    width = -(-(rows * pack) // 128) * 128
    per_chunk = chunk // owner_len
    grid_spec = pltpu.PrefetchScalarGridSpec(
        num_scalar_prefetch=1,
        grid=(group_steps + entries // chunk,),
        in_specs=[
            pl.BlockSpec((fields, 2 * step * pack, lanes), lambda j, idx: (0, jnp.minimum(j, group_steps - 1), 0)),
            pl.BlockSpec((fields, step * pack, lanes), lambda j, idx: (0, jnp.minimum(j, group_steps - 1), 0)),
            pl.BlockSpec((1, chunk), lambda j, idx: (0, jnp.maximum(j - group_steps, 0))),
        ],
        out_specs=pl.BlockSpec((per_chunk, rows, owner_len), lambda j, idx: (jnp.maximum(j - group_steps, 0), 0, 0)),
        scratch_shapes=[pltpu.VMEM((groups // pack * lanes // 8 + 1, 8, width), xs.dtype), pltpu.VMEM((chunk // 8, 8, width), xs.dtype)],
    )
    return pl.pallas_call(
        pick_kernel(group_steps, step, chunk, owner_len, pack),
        out_shape=jax.ShapeDtypeStruct((entries // owner_len, rows, owner_len), xs.dtype),
        grid_spec=grid_spec,
    )(flat, xv, xs, sel)


def model_tensors(coarse):
    values = coarse.astype(jnp.float32)
    points = values.shape[-1]
    values = values.reshape(values.shape[0] // 3, 3, points)
    velocity = values[:3]
    species = values[3:]
    stress = [
        jnp.sum(velocity[first_comp] * velocity[second_comp], axis=0)
        for first_comp, second_comp in upper_pairs
    ]
    species_flux = jnp.sum(species[:, None, :, :] * velocity[None, :, :, :], axis=2)
    joined = jnp.concatenate([jnp.stack(stress, axis=0), species_flux.reshape(-1, points)], axis=0)
    return (model_coeff * joined).astype(jnp.bfloat16)


def window(at, count, coarse):
    reach = (count + 19) // 8 + 4
    if count % 8 or reach >= coarse:
        return 0, coarse
    return at * (count // 8) - 3, reach


def make_shards(row_count, col_count):
    def shards(fields, front_cells):
        field_count, local_x, local_y, z_length = fields.shape
        devices = row_count * col_count
        full_x = local_x * row_count
        full_y = local_y * col_count
        coarse_x = full_x // 8
        coarse_y = full_y // 8
        coarse_z = z_length // 8
        slab = coarse_z // devices
        slots = front_cells.shape[2]
        row = lax.axis_index("rows")
        col = lax.axis_index("cols")
        me = row * col_count + col

        copies = jnp.broadcast_to(front_cells, (devices,) + front_cells.shape[1:])
        every_cell = lax.all_to_all(copies, ("rows", "cols"), split_axis=0, concat_axis=0, tiled=True)

        x_base, x_count = window(row, local_x, coarse_x)
        y_base, y_count = window(col, local_y, coarse_y)
        wx = jnp.asarray(window_tables(row_count, local_x, full_x))[row]
        wy = jnp.asarray(window_tables(col_count, local_y, full_y))[col]
        group = x_count * y_count
        pack = 3
        padded = -(-group // (8 * pack)) * 8 * pack
        xs = jnp.stack([wx[1], wx[0], wx[0]])
        ys = jnp.stack([wy[0], wy[1], wy[0]])
        weights = xs[:, :, None, :, None] * ys[:, None, :, None, :]
        weights = weights.reshape(3, group, local_x * local_y)
        weights = jnp.pad(weights, ((0, 0), (0, padded - group), (0, 0)))
        weights = jnp.concatenate([jnp.transpose(weights[:2], (1, 0, 2)).reshape(2 * padded, -1), weights[2]], axis=0)
        fields3 = fields.reshape(field_count, local_x * local_y, z_length)
        partials = filtered_partials(fields3, weights)

        by_owner = jnp.transpose(every_cell, (1, 0, 2))
        holder = lax.broadcasted_iota(jnp.int32, by_owner.shape, 1)
        clipped = jnp.clip(by_owner, 0, coarse_x * coarse_y * slab - 1)
        cell_pq = clipped // slab
        at_z = holder * slab + clipped % slab
        at_x = (cell_pq // coarse_y - x_base) % coarse_x
        at_y = (cell_pq % coarse_y - y_base) % coarse_y
        inside = (at_x < x_count) & (at_y < y_count) & (by_owner >= 0)
        at_group = at_x * y_count + at_y
        flat = jnp.where(inside, (at_group // pack) * coarse_z + at_z, padded // pack * coarse_z)
        sel = jnp.where(inside, at_group % pack, 0).reshape(1, -1)
        owner_len = devices * slots
        value_part, slope_part = partials
        taken = pick_cells(value_part, slope_part, flat.reshape(-1), sel, owner_len, pack)
        arrived = lax.all_to_all(taken, ("rows", "cols"), split_axis=0, concat_axis=0, tiled=True)
        summed = jnp.sum(arrived, axis=0)
        rounded = lax.reduce_precision(summed, exponent_bits=8, mantissa_bits=7)
        mine = lax.dynamic_index_in_dim(by_owner, me, axis=0, keepdims=False).reshape(-1)
        picked = jnp.where(mine[None, :] >= 0, rounded, jnp.zeros_like(rounded))
        return model_tensors(picked)[None]

    return shards


def solution(mesh):
    in_specs = (P(None, "rows", "cols", None), P(("rows", "cols"), None, None))
    out_specs = P(("rows", "cols"), None, None)
    shards = make_shards(mesh.shape["rows"], mesh.shape["cols"])
    return jax.shard_map(shards, mesh=mesh, in_specs=in_specs, out_specs=out_specs, check_vma=False)
```

```python
import numpy as np
import jax
import jax.numpy as jnp
import ml_dtypes
from jax import lax
from jax.sharding import PartitionSpec as P
from jax.experimental import pallas as pl
from jax.experimental.pallas import tpu as pltpu

first_tap = -20
last_tap = 27
sigma_sq = 256.0 / 12.0
coarse_step = 8.0
model_coeff = 1.0 / 3.0
upper_pairs = ((0, 0), (0, 1), (0, 2), (1, 1), (1, 2), (2, 2))
block_len = 1024
halo = 128


def tap_weights(offsets):
    f32 = np.float32
    every_tap = np.arange(first_tap, last_tap + 1).astype(f32)
    weight_sum = np.sum(np.exp(-(every_tap - f32(3.5)) * (every_tap - f32(3.5)) / f32(2.0 * sigma_sq)), dtype=f32)
    shifted = offsets.astype(f32) - f32(3.5)
    inside = (offsets >= first_tap) & (offsets <= last_tap)
    gauss = np.where(inside, np.exp(-shifted * shifted / f32(2.0 * sigma_sq)), f32(0.0)).astype(f32) / weight_sum
    slope = (f32(-coarse_step) * shifted / f32(sigma_sq) * gauss).astype(f32)
    bf = ml_dtypes.bfloat16
    return gauss.astype(bf).astype(f32), slope.astype(bf).astype(f32)


def line_matrices(length):
    fine_pos = np.arange(length)[:, None]
    coarse_pos = np.arange(length // 8)[None, :]
    offsets = np.mod(fine_pos - 8 * coarse_pos, length)
    offsets = np.where(offsets >= length // 2, offsets - length, offsets)
    return tap_weights(offsets)


def z_tables(length):
    coarse = np.arange(length // 8)[None, :]
    main = np.arange(length)[:, None] - 8 * coarse
    prev = np.arange(halo)[:, None] - halo - 8 * coarse
    nxt = np.arange(halo)[:, None] + length - 8 * coarse
    return [tap_weights(o) for o in (main, prev, nxt)]


def filter_kernel(block_count, coarse_block, value_rows, slope_rows):
    def body(x_ref, main_ref, halo_ref, w_ref, ov_ref, os_ref, zv_ref, zs_ref):
        per_step, rows, length = x_ref.shape
        blen = length // block_count
        for b in range(block_count):
            main = x_ref[:, :, b * blen:(b + 1) * blen].reshape(per_step * rows, blen)
            start = (b * blen - halo) % length
            tail = x_ref[:, :, start:start + halo].reshape(per_step * rows, halo)
            start = ((b + 1) * blen) % length
            head = x_ref[:, :, start:start + halo].reshape(per_step * rows, halo)
            edges = jnp.concatenate([tail, head], axis=1)
            acc = jnp.dot(main, main_ref[...], preferred_element_type=jnp.float32)
            acc = acc + jnp.dot(edges, halo_ref[...], preferred_element_type=jnp.float32)
            lanes = slice(b * coarse_block, (b + 1) * coarse_block)
            zv_ref[:, lanes] = acc[:, :coarse_block].astype(jnp.bfloat16)
            zs_ref[:, lanes] = acc[:, coarse_block:].astype(jnp.bfloat16)
        for k in range(per_step):
            zv = zv_ref[k * rows:(k + 1) * rows, :]
            zs = zs_ref[k * rows:(k + 1) * rows, :]
            pv = jnp.dot(w_ref[0, :value_rows, :], zv, preferred_element_type=jnp.float32)
            pv = pv + jnp.dot(w_ref[1, :value_rows, :], zv, preferred_element_type=jnp.float32)
            ps = jnp.dot(w_ref[0, value_rows:, :], zs, preferred_element_type=jnp.float32)
            ps = ps + jnp.dot(w_ref[1, value_rows:, :], zs, preferred_element_type=jnp.float32)
            ov_ref[k] = pv
            os_ref[k] = ps

    return body


def split_hi_lo(w):
    hi = w.astype(jnp.bfloat16)
    lo = (w - hi.astype(jnp.float32)).astype(jnp.bfloat16)
    return jnp.stack([hi, lo], axis=0)


def filtered_partials(fields3, weights):
    field_count, rows, length = fields3.shape
    blen = block_len if (length % block_len == 0 and length > block_len) else length
    block_count = length // blen
    coarse_block = blen // 8
    tables = z_tables(blen)
    joined = [np.concatenate([t[0], t[1]], axis=1) for t in tables]
    main = jnp.asarray(joined[0], jnp.bfloat16)
    halo_w = jnp.asarray(np.concatenate([joined[1], joined[2]], axis=0), jnp.bfloat16)
    w = split_hi_lo(weights)
    total_rows = w.shape[1]
    value_rows = total_rows // 3 * 2
    coarse = length // 8
    per_step = 6 if field_count % 6 == 0 else 1
    const = lambda f: (0, 0)
    return pl.pallas_call(
        filter_kernel(block_count, coarse_block, value_rows, total_rows - value_rows),
        out_shape=[
            jax.ShapeDtypeStruct((field_count, value_rows, coarse), jnp.float32),
            jax.ShapeDtypeStruct((field_count, total_rows - value_rows, coarse), jnp.float32),
        ],
        grid=(field_count // per_step,),
        in_specs=[
            pl.BlockSpec((per_step, rows, length), lambda f: (f, 0, 0)),
            pl.BlockSpec(main.shape, const),
            pl.BlockSpec(halo_w.shape, const),
            pl.BlockSpec(w.shape, lambda f: (0, 0, 0)),
        ],
        out_specs=[
            pl.BlockSpec((per_step, value_rows, coarse), lambda f: (f, 0, 0)),
            pl.BlockSpec((per_step, total_rows - value_rows, coarse), lambda f: (f, 0, 0)),
        ],
        scratch_shapes=[pltpu.VMEM((per_step * rows, coarse), jnp.bfloat16)] * 2,
    )(fields3, main, halo_w, w)


def window_tables(blocks, count, full):
    smooth, deriv = line_matrices(full)
    coarse = full // 8
    out = []
    for at in range(blocks):
        base, width = window(at, count, coarse)
        picks = (base + np.arange(width)) % coarse
        part = slice(at * count, (at + 1) * count)
        out.append(np.stack([smooth[part][:, picks].T, deriv[part][:, picks].T]))
    return np.stack(out)


def pick_kernel(group_steps, step, chunk, owner_len, pack):
    def body(idx_ref, xv_ref, xs_ref, sel_ref, o_ref, tab_ref, buf_ref):
        j = pl.program_id(0)
        fields = xv_ref.shape[0]
        lanes = xv_ref.shape[2]
        width = tab_ref.shape[2]
        per_field = 3 * pack

        @pl.when(j < group_steps)
        def _():
            for t in range(step):
                parts = []
                for f in range(fields):
                    parts.append(xv_ref[f, 2 * pack * t:2 * pack * (t + 1), :])
                    parts.append(xs_ref[f, pack * t:pack * (t + 1), :])
                parts.append(jnp.zeros((width - fields * per_field, lanes), xv_ref.dtype))
                slab = jnp.concatenate(parts, axis=0)
                at = pl.multiple_of((j * step + t) * (lanes // 8), lanes // 8)
                tab_ref[pl.ds(at, lanes // 8), :, :] = slab.T.reshape(lanes // 8, 8, width)

        @pl.when(j == group_steps - 1)
        def _():
            tab_ref[tab_ref.shape[0] - 1] = jnp.zeros((8, width), tab_ref.dtype)

        @pl.when(j >= group_steps)
        def _():
            base = (j - group_steps) * chunk

            def eight(i, carry):
                for k in range(8):
                    code = idx_ref[base + i * 8 + k]
                    tile = lax.shift_right_logical(code, 3)
                    row = tab_ref[tile, pl.ds(code & 7, 1), :]
                    buf_ref[i, pl.ds(k, 1), :] = row
                return carry

            lax.fori_loop(0, chunk // 8, eight, 0, unroll=16)
            flipped = buf_ref[...].reshape(chunk, width).T
            sel = sel_ref[...]
            picked = []
            for f in range(fields):
                for m in range(3):
                    choices = []
                    for k in range(pack):
                        at = f * per_field + (2 * k + m if m < 2 else 2 * pack + k)
                        choices.append(flipped[at:at + 1])
                    row = choices[0]
                    for k in range(1, pack):
                        row = jnp.where(sel == k, choices[k], row)
                    picked.append(row)
            picked = jnp.concatenate(picked, axis=0)
            for owner in range(chunk // owner_len):
                o_ref[owner] = picked[:, owner * owner_len:(owner + 1) * owner_len]

    return body


def pick_cells(xv, xs, flat, sel, owner_len, pack, chunk=4096):
    fields, groups, lanes = xs.shape
    rows = fields * 3
    step = 8
    group_steps = groups // (step * pack)
    entries = flat.shape[0]
    chunk = min(chunk, entries)
    width = -(-(rows * pack) // 128) * 128
    per_chunk = chunk // owner_len
    grid_spec = pltpu.PrefetchScalarGridSpec(
        num_scalar_prefetch=1,
        grid=(group_steps + entries // chunk,),
        in_specs=[
            pl.BlockSpec((fields, 2 * step * pack, lanes), lambda j, idx: (0, jnp.minimum(j, group_steps - 1), 0)),
            pl.BlockSpec((fields, step * pack, lanes), lambda j, idx: (0, jnp.minimum(j, group_steps - 1), 0)),
            pl.BlockSpec((1, chunk), lambda j, idx: (0, jnp.maximum(j - group_steps, 0))),
        ],
        out_specs=pl.BlockSpec((per_chunk, rows, owner_len), lambda j, idx: (jnp.maximum(j - group_steps, 0), 0, 0)),
        scratch_shapes=[pltpu.VMEM((groups // pack * lanes // 8 + 1, 8, width), xs.dtype), pltpu.VMEM((chunk // 8, 8, width), xs.dtype)],
    )
    return pl.pallas_call(
        pick_kernel(group_steps, step, chunk, owner_len, pack),
        out_shape=jax.ShapeDtypeStruct((entries // owner_len, rows, owner_len), xs.dtype),
        grid_spec=grid_spec,
    )(flat, xv, xs, sel)


def model_tensors(coarse):
    values = coarse.astype(jnp.float32)
    points = values.shape[-1]
    values = values.reshape(values.shape[0] // 3, 3, points)
    velocity = values[:3]
    species = values[3:]
    stress = [
        jnp.sum(velocity[first_comp] * velocity[second_comp], axis=0)
        for first_comp, second_comp in upper_pairs
    ]
    species_flux = jnp.sum(species[:, None, :, :] * velocity[None, :, :, :], axis=2)
    joined = jnp.concatenate([jnp.stack(stress, axis=0), species_flux.reshape(-1, points)], axis=0)
    return (model_coeff * joined).astype(jnp.bfloat16)


def window(at, count, coarse):
    reach = (count + 19) // 8 + 4
    if count % 8 or reach >= coarse:
        return 0, coarse
    return at * (count // 8) - 3, reach


def make_shards(row_count, col_count):
    def shards(fields, front_cells):
        field_count, local_x, local_y, z_length = fields.shape
        devices = row_count * col_count
        full_x = local_x * row_count
        full_y = local_y * col_count
        coarse_x = full_x // 8
        coarse_y = full_y // 8
        coarse_z = z_length // 8
        slab = coarse_z // devices
        slots = front_cells.shape[2]
        row = lax.axis_index("rows")
        col = lax.axis_index("cols")
        me = row * col_count + col

        copies = jnp.broadcast_to(front_cells, (devices,) + front_cells.shape[1:])
        every_cell = lax.all_to_all(copies, ("rows", "cols"), split_axis=0, concat_axis=0, tiled=True)

        x_base, x_count = window(row, local_x, coarse_x)
        y_base, y_count = window(col, local_y, coarse_y)
        wx = jnp.asarray(window_tables(row_count, local_x, full_x))[row]
        wy = jnp.asarray(window_tables(col_count, local_y, full_y))[col]
        group = x_count * y_count
        pack = 3
        padded = -(-group // (8 * pack)) * 8 * pack
        xs = jnp.stack([wx[1], wx[0], wx[0]])
        ys = jnp.stack([wy[0], wy[1], wy[0]])
        weights = xs[:, :, None, :, None] * ys[:, None, :, None, :]
        weights = weights.reshape(3, group, local_x * local_y)
        weights = jnp.pad(weights, ((0, 0), (0, padded - group), (0, 0)))
        weights = jnp.concatenate([jnp.transpose(weights[:2], (1, 0, 2)).reshape(2 * padded, -1), weights[2]], axis=0)
        fields3 = fields.reshape(field_count, local_x * local_y, z_length)
        partials = filtered_partials(fields3, weights)

        by_owner = jnp.transpose(every_cell, (1, 0, 2))
        holder = lax.broadcasted_iota(jnp.int32, by_owner.shape, 1)
        clipped = jnp.clip(by_owner, 0, coarse_x * coarse_y * slab - 1)
        cell_pq = clipped // slab
        at_z = holder * slab + clipped % slab
        at_x = (cell_pq // coarse_y - x_base) % coarse_x
        at_y = (cell_pq % coarse_y - y_base) % coarse_y
        inside = (at_x < x_count) & (at_y < y_count) & (by_owner >= 0)
        at_group = at_x * y_count + at_y
        flat = jnp.where(inside, (at_group // pack) * coarse_z + at_z, padded // pack * coarse_z)
        sel = jnp.where(inside, at_group % pack, 0).reshape(1, -1)
        owner_len = devices * slots
        value_part, slope_part = partials
        taken = pick_cells(value_part, slope_part, flat.reshape(-1), sel, owner_len, pack)
        arrived = lax.all_to_all(taken, ("rows", "cols"), split_axis=0, concat_axis=0, tiled=True)
        summed = jnp.sum(arrived, axis=0)
        rounded = lax.reduce_precision(summed, exponent_bits=8, mantissa_bits=7)
        mine = lax.dynamic_index_in_dim(by_owner, me, axis=0, keepdims=False).reshape(-1)
        picked = jnp.where(mine[None, :] >= 0, rounded, jnp.zeros_like(rounded))
        return model_tensors(picked)[None]

    return shards


def solution(mesh):
    in_specs = (P(None, "rows", "cols", None), P(("rows", "cols"), None, None))
    out_specs = P(("rows", "cols"), None, None)
    shards = make_shards(mesh.shape["rows"], mesh.shape["cols"])
    return jax.shard_map(shards, mesh=mesh, in_specs=in_specs, out_specs=out_specs, check_vma=False)
```

```python
import numpy as np
import jax
import jax.numpy as jnp
import ml_dtypes
from jax import lax
from jax.sharding import PartitionSpec as P
from jax.experimental import pallas as pl
from jax.experimental.pallas import tpu as pltpu

first_tap = -20
last_tap = 27
sigma_sq = 256.0 / 12.0
coarse_step = 8.0
model_coeff = 1.0 / 3.0
upper_pairs = ((0, 0), (0, 1), (0, 2), (1, 1), (1, 2), (2, 2))
block_len = 1024
halo = 128


def tap_weights(offsets):
    f32 = np.float32
    every_tap = np.arange(first_tap, last_tap + 1).astype(f32)
    weight_sum = np.sum(np.exp(-(every_tap - f32(3.5)) * (every_tap - f32(3.5)) / f32(2.0 * sigma_sq)), dtype=f32)
    shifted = offsets.astype(f32) - f32(3.5)
    inside = (offsets >= first_tap) & (offsets <= last_tap)
    gauss = np.where(inside, np.exp(-shifted * shifted / f32(2.0 * sigma_sq)), f32(0.0)).astype(f32) / weight_sum
    slope = (f32(-coarse_step) * shifted / f32(sigma_sq) * gauss).astype(f32)
    bf = ml_dtypes.bfloat16
    return gauss.astype(bf).astype(f32), slope.astype(bf).astype(f32)


def line_matrices(length):
    fine_pos = np.arange(length)[:, None]
    coarse_pos = np.arange(length // 8)[None, :]
    offsets = np.mod(fine_pos - 8 * coarse_pos, length)
    offsets = np.where(offsets >= length // 2, offsets - length, offsets)
    return tap_weights(offsets)


def z_tables(length):
    coarse = np.arange(length // 8)[None, :]
    main = np.arange(length)[:, None] - 8 * coarse
    prev = np.arange(halo)[:, None] - halo - 8 * coarse
    nxt = np.arange(halo)[:, None] + length - 8 * coarse
    return [tap_weights(o) for o in (main, prev, nxt)]


def filter_kernel(block_count, coarse_block, value_rows, slope_rows):
    def body(x_ref, main_ref, halo_ref, w_ref, ov_ref, os_ref, zv_ref, zs_ref):
        per_step, rows, length = x_ref.shape
        blen = length // block_count
        for b in range(block_count):
            main = x_ref[:, :, b * blen:(b + 1) * blen].reshape(per_step * rows, blen)
            start = (b * blen - halo) % length
            tail = x_ref[:, :, start:start + halo].reshape(per_step * rows, halo)
            start = ((b + 1) * blen) % length
            head = x_ref[:, :, start:start + halo].reshape(per_step * rows, halo)
            edges = jnp.concatenate([tail, head], axis=1)
            acc = jnp.dot(main, main_ref[...], preferred_element_type=jnp.float32)
            acc = acc + jnp.dot(edges, halo_ref[...], preferred_element_type=jnp.float32)
            lanes = slice(b * coarse_block, (b + 1) * coarse_block)
            zv_ref[:, lanes] = acc[:, :coarse_block].astype(jnp.bfloat16)
            zs_ref[:, lanes] = acc[:, coarse_block:].astype(jnp.bfloat16)
        for k in range(per_step):
            zv = zv_ref[k * rows:(k + 1) * rows, :]
            zs = zs_ref[k * rows:(k + 1) * rows, :]
            pv = jnp.dot(w_ref[0, :value_rows, :], zv, preferred_element_type=jnp.float32)
            pv = pv + jnp.dot(w_ref[1, :value_rows, :], zv, preferred_element_type=jnp.float32)
            ps = jnp.dot(w_ref[0, value_rows:, :], zs, preferred_element_type=jnp.float32)
            ps = ps + jnp.dot(w_ref[1, value_rows:, :], zs, preferred_element_type=jnp.float32)
            ov_ref[k] = pv
            os_ref[k] = ps

    return body


def split_hi_lo(w):
    hi = w.astype(jnp.bfloat16)
    lo = (w - hi.astype(jnp.float32)).astype(jnp.bfloat16)
    return jnp.stack([hi, lo], axis=0)


def filtered_partials(fields3, weights):
    field_count, rows, length = fields3.shape
    blen = block_len if (length % block_len == 0 and length > block_len) else length
    block_count = length // blen
    coarse_block = blen // 8
    tables = z_tables(blen)
    joined = [np.concatenate([t[0], t[1]], axis=1) for t in tables]
    main = jnp.asarray(joined[0], jnp.bfloat16)
    halo_w = jnp.asarray(np.concatenate([joined[1], joined[2]], axis=0), jnp.bfloat16)
    w = split_hi_lo(weights)
    total_rows = w.shape[1]
    value_rows = total_rows // 3 * 2
    coarse = length // 8
    per_step = 4 if field_count % 4 == 0 else 1
    const = lambda f: (0, 0)
    return pl.pallas_call(
        filter_kernel(block_count, coarse_block, value_rows, total_rows - value_rows),
        out_shape=[
            jax.ShapeDtypeStruct((field_count, value_rows, coarse), jnp.float32),
            jax.ShapeDtypeStruct((field_count, total_rows - value_rows, coarse), jnp.float32),
        ],
        grid=(field_count // per_step,),
        in_specs=[
            pl.BlockSpec((per_step, rows, length), lambda f: (f, 0, 0)),
            pl.BlockSpec(main.shape, const),
            pl.BlockSpec(halo_w.shape, const),
            pl.BlockSpec(w.shape, lambda f: (0, 0, 0)),
        ],
        out_specs=[
            pl.BlockSpec((per_step, value_rows, coarse), lambda f: (f, 0, 0)),
            pl.BlockSpec((per_step, total_rows - value_rows, coarse), lambda f: (f, 0, 0)),
        ],
        scratch_shapes=[pltpu.VMEM((per_step * rows, coarse), jnp.bfloat16)] * 2,
    )(fields3, main, halo_w, w)


def window_tables(blocks, count, full):
    smooth, deriv = line_matrices(full)
    coarse = full // 8
    out = []
    for at in range(blocks):
        base, width = window(at, count, coarse)
        picks = (base + np.arange(width)) % coarse
        part = slice(at * count, (at + 1) * count)
        out.append(np.stack([smooth[part][:, picks].T, deriv[part][:, picks].T]))
    return np.stack(out)


def pick_kernel(group_steps, step, chunk, owner_len, pack):
    def body(idx_ref, xv_ref, xs_ref, sel_ref, o_ref, tab_ref, buf_ref):
        j = pl.program_id(0)
        fields = xv_ref.shape[0]
        lanes = xv_ref.shape[2]
        width = tab_ref.shape[2]
        per_field = 3 * pack

        @pl.when(j < group_steps)
        def _():
            for t in range(step):
                parts = []
                for k in range(pack):
                    for f in range(fields):
                        at = 2 * (pack * t + k)
                        parts.append(xv_ref[f, at:at + 2, :])
                        parts.append(xs_ref[f, pack * t + k:pack * t + k + 1, :])
                parts.append(jnp.zeros((width - fields * per_field, lanes), xv_ref.dtype))
                slab = jnp.concatenate(parts, axis=0)
                at = pl.multiple_of((j * step + t) * (lanes // 8), lanes // 8)
                tab_ref[pl.ds(at, lanes // 8), :, :] = slab.T.reshape(lanes // 8, 8, width)

        @pl.when(j == group_steps - 1)
        def _():
            tab_ref[tab_ref.shape[0] - 1] = jnp.zeros((8, width), tab_ref.dtype)

        @pl.when(j >= group_steps)
        def _():
            base = (j - group_steps) * chunk

            def eight(i, carry):
                for k in range(8):
                    code = idx_ref[base + i * 8 + k]
                    tile = lax.shift_right_logical(code, 3)
                    row = tab_ref[tile, pl.ds(code & 7, 1), :]
                    buf_ref[i, pl.ds(k, 1), :] = row
                return carry

            lax.fori_loop(0, chunk // 8, eight, 0, unroll=16)
            flipped = buf_ref[...].reshape(chunk, width).T
            sel = sel_ref[...]
            rows = fields * 3
            picked = flipped[:rows]
            for k in range(1, pack):
                picked = jnp.where(sel == k, flipped[k * rows:(k + 1) * rows], picked)
            for owner in range(chunk // owner_len):
                o_ref[owner] = picked[:, owner * owner_len:(owner + 1) * owner_len]

    return body


def pick_cells(xv, xs, flat, sel, owner_len, pack, chunk=4096):
    fields, groups, lanes = xs.shape
    rows = fields * 3
    step = 8
    group_steps = groups // (step * pack)
    entries = flat.shape[0]
    chunk = min(chunk, entries)
    width = -(-(rows * pack) // 128) * 128
    per_chunk = chunk // owner_len
    grid_spec = pltpu.PrefetchScalarGridSpec(
        num_scalar_prefetch=1,
        grid=(group_steps + entries // chunk,),
        in_specs=[
            pl.BlockSpec((fields, 2 * step * pack, lanes), lambda j, idx: (0, jnp.minimum(j, group_steps - 1), 0)),
            pl.BlockSpec((fields, step * pack, lanes), lambda j, idx: (0, jnp.minimum(j, group_steps - 1), 0)),
            pl.BlockSpec((1, chunk), lambda j, idx: (0, jnp.maximum(j - group_steps, 0))),
        ],
        out_specs=pl.BlockSpec((per_chunk, rows, owner_len), lambda j, idx: (jnp.maximum(j - group_steps, 0), 0, 0)),
        scratch_shapes=[pltpu.VMEM((groups // pack * lanes // 8 + 1, 8, width), xs.dtype), pltpu.VMEM((chunk // 8, 8, width), xs.dtype)],
    )
    return pl.pallas_call(
        pick_kernel(group_steps, step, chunk, owner_len, pack),
        out_shape=jax.ShapeDtypeStruct((entries // owner_len, rows, owner_len), xs.dtype),
        grid_spec=grid_spec,
    )(flat, xv, xs, sel)


def model_tensors(coarse):
    values = coarse.astype(jnp.float32)
    points = values.shape[-1]
    values = values.reshape(values.shape[0] // 3, 3, points)
    velocity = values[:3]
    species = values[3:]
    stress = [
        jnp.sum(velocity[first_comp] * velocity[second_comp], axis=0)
        for first_comp, second_comp in upper_pairs
    ]
    species_flux = jnp.sum(species[:, None, :, :] * velocity[None, :, :, :], axis=2)
    joined = jnp.concatenate([jnp.stack(stress, axis=0), species_flux.reshape(-1, points)], axis=0)
    return (model_coeff * joined).astype(jnp.bfloat16)


def window(at, count, coarse):
    reach = (count + 19) // 8 + 4
    if count % 8 or reach >= coarse:
        return 0, coarse
    return at * (count // 8) - 3, reach


def make_shards(row_count, col_count):
    def shards(fields, front_cells):
        field_count, local_x, local_y, z_length = fields.shape
        devices = row_count * col_count
        full_x = local_x * row_count
        full_y = local_y * col_count
        coarse_x = full_x // 8
        coarse_y = full_y // 8
        coarse_z = z_length // 8
        slab = coarse_z // devices
        slots = front_cells.shape[2]
        row = lax.axis_index("rows")
        col = lax.axis_index("cols")
        me = row * col_count + col

        copies = jnp.broadcast_to(front_cells, (devices,) + front_cells.shape[1:])
        every_cell = lax.all_to_all(copies, ("rows", "cols"), split_axis=0, concat_axis=0, tiled=True)

        x_base, x_count = window(row, local_x, coarse_x)
        y_base, y_count = window(col, local_y, coarse_y)
        wx = jnp.asarray(window_tables(row_count, local_x, full_x))[row]
        wy = jnp.asarray(window_tables(col_count, local_y, full_y))[col]
        group = x_count * y_count
        pack = 3
        padded = -(-group // (8 * pack)) * 8 * pack
        xs = jnp.stack([wx[1], wx[0], wx[0]])
        ys = jnp.stack([wy[0], wy[1], wy[0]])
        weights = xs[:, :, None, :, None] * ys[:, None, :, None, :]
        weights = weights.reshape(3, group, local_x * local_y)
        weights = jnp.pad(weights, ((0, 0), (0, padded - group), (0, 0)))
        weights = jnp.concatenate([jnp.transpose(weights[:2], (1, 0, 2)).reshape(2 * padded, -1), weights[2]], axis=0)
        fields3 = fields.reshape(field_count, local_x * local_y, z_length)
        partials = filtered_partials(fields3, weights)

        by_owner = jnp.transpose(every_cell, (1, 0, 2))
        holder = lax.broadcasted_iota(jnp.int32, by_owner.shape, 1)
        clipped = jnp.clip(by_owner, 0, coarse_x * coarse_y * slab - 1)
        cell_pq = clipped // slab
        at_z = holder * slab + clipped % slab
        at_x = (cell_pq // coarse_y - x_base) % coarse_x
        at_y = (cell_pq % coarse_y - y_base) % coarse_y
        inside = (at_x < x_count) & (at_y < y_count) & (by_owner >= 0)
        at_group = at_x * y_count + at_y
        flat = jnp.where(inside, (at_group // pack) * coarse_z + at_z, padded // pack * coarse_z)
        sel = jnp.where(inside, at_group % pack, 0).reshape(1, -1)
        owner_len = devices * slots
        value_part, slope_part = partials
        taken = pick_cells(value_part, slope_part, flat.reshape(-1), sel, owner_len, pack)
        arrived = lax.all_to_all(taken, ("rows", "cols"), split_axis=0, concat_axis=0, tiled=True)
        summed = jnp.sum(arrived, axis=0)
        rounded = lax.reduce_precision(summed, exponent_bits=8, mantissa_bits=7)
        mine = lax.dynamic_index_in_dim(by_owner, me, axis=0, keepdims=False).reshape(-1)
        picked = jnp.where(mine[None, :] >= 0, rounded, jnp.zeros_like(rounded))
        return model_tensors(picked)[None]

    return shards


def solution(mesh):
    in_specs = (P(None, "rows", "cols", None), P(("rows", "cols"), None, None))
    out_specs = P(("rows", "cols"), None, None)
    shards = make_shards(mesh.shape["rows"], mesh.shape["cols"])
    return jax.shard_map(shards, mesh=mesh, in_specs=in_specs, out_specs=out_specs, check_vma=False)
```

```python
import numpy as np
import jax
import jax.numpy as jnp
import ml_dtypes
from jax import lax
from jax.sharding import PartitionSpec as P
from jax.experimental import pallas as pl
from jax.experimental.pallas import tpu as pltpu

first_tap = -20
last_tap = 27
sigma_sq = 256.0 / 12.0
coarse_step = 8.0
model_coeff = 1.0 / 3.0
upper_pairs = ((0, 0), (0, 1), (0, 2), (1, 1), (1, 2), (2, 2))
block_len = 1024
halo = 128


def tap_weights(offsets):
    f32 = np.float32
    every_tap = np.arange(first_tap, last_tap + 1).astype(f32)
    weight_sum = np.sum(np.exp(-(every_tap - f32(3.5)) * (every_tap - f32(3.5)) / f32(2.0 * sigma_sq)), dtype=f32)
    shifted = offsets.astype(f32) - f32(3.5)
    inside = (offsets >= first_tap) & (offsets <= last_tap)
    gauss = np.where(inside, np.exp(-shifted * shifted / f32(2.0 * sigma_sq)), f32(0.0)).astype(f32) / weight_sum
    slope = (f32(-coarse_step) * shifted / f32(sigma_sq) * gauss).astype(f32)
    bf = ml_dtypes.bfloat16
    return gauss.astype(bf).astype(f32), slope.astype(bf).astype(f32)


def line_matrices(length):
    fine_pos = np.arange(length)[:, None]
    coarse_pos = np.arange(length // 8)[None, :]
    offsets = np.mod(fine_pos - 8 * coarse_pos, length)
    offsets = np.where(offsets >= length // 2, offsets - length, offsets)
    return tap_weights(offsets)


def z_tables(length):
    coarse = np.arange(length // 8)[None, :]
    main = np.arange(length)[:, None] - 8 * coarse
    prev = np.arange(halo)[:, None] - halo - 8 * coarse
    nxt = np.arange(halo)[:, None] + length - 8 * coarse
    return [tap_weights(o) for o in (main, prev, nxt)]


def filter_kernel(block_count, coarse_block, value_rows, slope_rows):
    def body(x_ref, main_ref, halo_ref, w_ref, ov_ref, os_ref, zv_ref, zs_ref):
        per_step, rows, length = x_ref.shape
        blen = length // block_count
        for b in range(block_count):
            main = x_ref[:, :, b * blen:(b + 1) * blen].reshape(per_step * rows, blen)
            start = (b * blen - halo) % length
            tail = x_ref[:, :, start:start + halo].reshape(per_step * rows, halo)
            start = ((b + 1) * blen) % length
            head = x_ref[:, :, start:start + halo].reshape(per_step * rows, halo)
            edges = jnp.concatenate([tail, head], axis=1)
            acc = jnp.dot(main, main_ref[...], preferred_element_type=jnp.float32)
            acc = acc + jnp.dot(edges, halo_ref[...], preferred_element_type=jnp.float32)
            lanes = slice(b * coarse_block, (b + 1) * coarse_block)
            zv_ref[:, lanes] = acc[:, :coarse_block].astype(jnp.bfloat16)
            zs_ref[:, lanes] = acc[:, coarse_block:].astype(jnp.bfloat16)
        for k in range(per_step):
            zv = zv_ref[k * rows:(k + 1) * rows, :]
            zs = zs_ref[k * rows:(k + 1) * rows, :]
            pv = jnp.dot(w_ref[0, :value_rows, :], zv, preferred_element_type=jnp.float32)
            pv = pv + jnp.dot(w_ref[1, :value_rows, :], zv, preferred_element_type=jnp.float32)
            ps = jnp.dot(w_ref[0, value_rows:, :], zs, preferred_element_type=jnp.float32)
            ps = ps + jnp.dot(w_ref[1, value_rows:, :], zs, preferred_element_type=jnp.float32)
            ov_ref[k] = pv
            os_ref[k] = ps

    return body


def split_hi_lo(w):
    hi = w.astype(jnp.bfloat16)
    lo = (w - hi.astype(jnp.float32)).astype(jnp.bfloat16)
    return jnp.stack([hi, lo], axis=0)


def filtered_partials(fields3, weights):
    field_count, rows, length = fields3.shape
    blen = block_len if (length % block_len == 0 and length > block_len) else length
    block_count = length // blen
    coarse_block = blen // 8
    tables = z_tables(blen)
    joined = [np.concatenate([t[0], t[1]], axis=1) for t in tables]
    main = jnp.asarray(joined[0], jnp.bfloat16)
    halo_w = jnp.asarray(np.concatenate([joined[1], joined[2]], axis=0), jnp.bfloat16)
    w = split_hi_lo(weights)
    total_rows = w.shape[1]
    value_rows = total_rows // 3 * 2
    coarse = length // 8
    per_step = 3 if field_count % 3 == 0 else 1
    const = lambda f: (0, 0)
    return pl.pallas_call(
        filter_kernel(block_count, coarse_block, value_rows, total_rows - value_rows),
        out_shape=[
            jax.ShapeDtypeStruct((field_count, value_rows, coarse), jnp.float32),
            jax.ShapeDtypeStruct((field_count, total_rows - value_rows, coarse), jnp.float32),
        ],
        grid=(field_count // per_step,),
        in_specs=[
            pl.BlockSpec((per_step, rows, length), lambda f: (f, 0, 0)),
            pl.BlockSpec(main.shape, const),
            pl.BlockSpec(halo_w.shape, const),
            pl.BlockSpec(w.shape, lambda f: (0, 0, 0)),
        ],
        out_specs=[
            pl.BlockSpec((per_step, value_rows, coarse), lambda f: (f, 0, 0)),
            pl.BlockSpec((per_step, total_rows - value_rows, coarse), lambda f: (f, 0, 0)),
        ],
        scratch_shapes=[pltpu.VMEM((per_step * rows, coarse), jnp.bfloat16)] * 2,
    )(fields3, main, halo_w, w)


def window_tables(blocks, count, full):
    smooth, deriv = line_matrices(full)
    coarse = full // 8
    out = []
    for at in range(blocks):
        base, width = window(at, count, coarse)
        picks = (base + np.arange(width)) % coarse
        part = slice(at * count, (at + 1) * count)
        out.append(np.stack([smooth[part][:, picks].T, deriv[part][:, picks].T]))
    return np.stack(out)


def pick_kernel(group_steps, step, chunk, owner_len, pack):
    def body(idx_ref, xv_ref, xs_ref, sel_ref, o_ref, tab_ref, buf_ref):
        j = pl.program_id(0)
        fields = xv_ref.shape[0]
        lanes = xv_ref.shape[2]
        width = tab_ref.shape[2]
        per_field = 3 * pack

        @pl.when(j < group_steps)
        def _():
            for t in range(step):
                parts = []
                for k in range(pack):
                    for f in range(fields):
                        at = 2 * (pack * t + k)
                        parts.append(xv_ref[f, at:at + 2, :])
                        parts.append(xs_ref[f, pack * t + k:pack * t + k + 1, :])
                parts.append(jnp.zeros((width - fields * per_field, lanes), xv_ref.dtype))
                slab = jnp.concatenate(parts, axis=0)
                at = pl.multiple_of((j * step + t) * (lanes // 8), lanes // 8)
                tab_ref[pl.ds(at, lanes // 8), :, :] = slab.T.reshape(lanes // 8, 8, width)

        @pl.when(j == group_steps - 1)
        def _():
            tab_ref[tab_ref.shape[0] - 1] = jnp.zeros((8, width), tab_ref.dtype)

        @pl.when(j >= group_steps)
        def _():
            base = (j - group_steps) * chunk

            def eight(i, carry):
                for k in range(8):
                    code = idx_ref[base + i * 8 + k]
                    tile = lax.shift_right_logical(code, 3)
                    row = tab_ref[tile, pl.ds(code & 7, 1), :]
                    buf_ref[i, pl.ds(k, 1), :] = row
                return carry

            lax.fori_loop(0, chunk // 8, eight, 0, unroll=16)
            flipped = buf_ref[...].reshape(chunk, width).T
            sel = sel_ref[...]
            rows = fields * 3
            picked = flipped[:rows]
            for k in range(1, pack):
                picked = jnp.where(sel == k, flipped[k * rows:(k + 1) * rows], picked)
            for owner in range(chunk // owner_len):
                o_ref[owner] = picked[:, owner * owner_len:(owner + 1) * owner_len]

    return body


def pick_cells(xv, xs, flat, sel, owner_len, pack, chunk=4096):
    fields, groups, lanes = xs.shape
    rows = fields * 3
    step = 8
    group_steps = groups // (step * pack)
    entries = flat.shape[0]
    chunk = min(chunk, entries)
    width = -(-(rows * pack) // 128) * 128
    per_chunk = chunk // owner_len
    grid_spec = pltpu.PrefetchScalarGridSpec(
        num_scalar_prefetch=1,
        grid=(group_steps + entries // chunk,),
        in_specs=[
            pl.BlockSpec((fields, 2 * step * pack, lanes), lambda j, idx: (0, jnp.minimum(j, group_steps - 1), 0)),
            pl.BlockSpec((fields, step * pack, lanes), lambda j, idx: (0, jnp.minimum(j, group_steps - 1), 0)),
            pl.BlockSpec((1, chunk), lambda j, idx: (0, jnp.maximum(j - group_steps, 0))),
        ],
        out_specs=pl.BlockSpec((per_chunk, rows, owner_len), lambda j, idx: (jnp.maximum(j - group_steps, 0), 0, 0)),
        scratch_shapes=[pltpu.VMEM((groups // pack * lanes // 8 + 1, 8, width), xs.dtype), pltpu.VMEM((chunk // 8, 8, width), xs.dtype)],
    )
    return pl.pallas_call(
        pick_kernel(group_steps, step, chunk, owner_len, pack),
        out_shape=jax.ShapeDtypeStruct((entries // owner_len, rows, owner_len), xs.dtype),
        grid_spec=grid_spec,
    )(flat, xv, xs, sel)


def model_tensors(coarse):
    values = coarse.astype(jnp.float32)
    points = values.shape[-1]
    values = values.reshape(values.shape[0] // 3, 3, points)
    velocity = values[:3]
    species = values[3:]
    stress = [
        jnp.sum(velocity[first_comp] * velocity[second_comp], axis=0)
        for first_comp, second_comp in upper_pairs
    ]
    species_flux = jnp.sum(species[:, None, :, :] * velocity[None, :, :, :], axis=2)
    joined = jnp.concatenate([jnp.stack(stress, axis=0), species_flux.reshape(-1, points)], axis=0)
    return (model_coeff * joined).astype(jnp.bfloat16)


def window(at, count, coarse):
    reach = (count + 19) // 8 + 4
    if count % 8 or reach >= coarse:
        return 0, coarse
    return at * (count // 8) - 3, reach


def make_shards(row_count, col_count):
    def shards(fields, front_cells):
        field_count, local_x, local_y, z_length = fields.shape
        devices = row_count * col_count
        full_x = local_x * row_count
        full_y = local_y * col_count
        coarse_x = full_x // 8
        coarse_y = full_y // 8
        coarse_z = z_length // 8
        slab = coarse_z // devices
        slots = front_cells.shape[2]
        row = lax.axis_index("rows")
        col = lax.axis_index("cols")
        me = row * col_count + col

        copies = jnp.broadcast_to(front_cells, (devices,) + front_cells.shape[1:])
        every_cell = lax.all_to_all(copies, ("rows", "cols"), split_axis=0, concat_axis=0, tiled=True)

        x_base, x_count = window(row, local_x, coarse_x)
        y_base, y_count = window(col, local_y, coarse_y)
        wx = jnp.asarray(window_tables(row_count, local_x, full_x))[row]
        wy = jnp.asarray(window_tables(col_count, local_y, full_y))[col]
        group = x_count * y_count
        pack = 3
        padded = -(-group // (8 * pack)) * 8 * pack
        xs = jnp.stack([wx[1], wx[0], wx[0]])
        ys = jnp.stack([wy[0], wy[1], wy[0]])
        weights = xs[:, :, None, :, None] * ys[:, None, :, None, :]
        weights = weights.reshape(3, group, local_x * local_y)
        weights = jnp.pad(weights, ((0, 0), (0, padded - group), (0, 0)))
        weights = jnp.concatenate([jnp.transpose(weights[:2], (1, 0, 2)).reshape(2 * padded, -1), weights[2]], axis=0)
        fields3 = fields.reshape(field_count, local_x * local_y, z_length)
        partials = filtered_partials(fields3, weights)

        by_owner = jnp.transpose(every_cell, (1, 0, 2))
        holder = lax.broadcasted_iota(jnp.int32, by_owner.shape, 1)
        clipped = jnp.clip(by_owner, 0, coarse_x * coarse_y * slab - 1)
        cell_pq = clipped // slab
        at_z = holder * slab + clipped % slab
        at_x = (cell_pq // coarse_y - x_base) % coarse_x
        at_y = (cell_pq % coarse_y - y_base) % coarse_y
        inside = (at_x < x_count) & (at_y < y_count) & (by_owner >= 0)
        at_group = at_x * y_count + at_y
        flat = jnp.where(inside, (at_group // pack) * coarse_z + at_z, padded // pack * coarse_z)
        sel = jnp.where(inside, at_group % pack, 0).reshape(1, -1)
        owner_len = devices * slots
        value_part, slope_part = partials
        taken = pick_cells(value_part, slope_part, flat.reshape(-1), sel, owner_len, pack)
        arrived = lax.all_to_all(taken, ("rows", "cols"), split_axis=0, concat_axis=0, tiled=True)
        summed = jnp.sum(arrived, axis=0)
        rounded = lax.reduce_precision(summed, exponent_bits=8, mantissa_bits=7)
        mine = lax.dynamic_index_in_dim(by_owner, me, axis=0, keepdims=False).reshape(-1)
        picked = jnp.where(mine[None, :] >= 0, rounded, jnp.zeros_like(rounded))
        return model_tensors(picked)[None]

    return shards


def solution(mesh):
    in_specs = (P(None, "rows", "cols", None), P(("rows", "cols"), None, None))
    out_specs = P(("rows", "cols"), None, None)
    shards = make_shards(mesh.shape["rows"], mesh.shape["cols"])
    return jax.shard_map(shards, mesh=mesh, in_specs=in_specs, out_specs=out_specs, check_vma=False)
```

```python
import numpy as np
import jax
import jax.numpy as jnp
import ml_dtypes
from jax import lax
from jax.sharding import PartitionSpec as P
from jax.experimental import pallas as pl
from jax.experimental.pallas import tpu as pltpu

first_tap = -20
last_tap = 27
sigma_sq = 256.0 / 12.0
coarse_step = 8.0
model_coeff = 1.0 / 3.0
upper_pairs = ((0, 0), (0, 1), (0, 2), (1, 1), (1, 2), (2, 2))
block_len = 1024
halo = 128


def tap_weights(offsets):
    f32 = np.float32
    every_tap = np.arange(first_tap, last_tap + 1).astype(f32)
    weight_sum = np.sum(np.exp(-(every_tap - f32(3.5)) * (every_tap - f32(3.5)) / f32(2.0 * sigma_sq)), dtype=f32)
    shifted = offsets.astype(f32) - f32(3.5)
    inside = (offsets >= first_tap) & (offsets <= last_tap)
    gauss = np.where(inside, np.exp(-shifted * shifted / f32(2.0 * sigma_sq)), f32(0.0)).astype(f32) / weight_sum
    slope = (f32(-coarse_step) * shifted / f32(sigma_sq) * gauss).astype(f32)
    bf = ml_dtypes.bfloat16
    return gauss.astype(bf).astype(f32), slope.astype(bf).astype(f32)


def line_matrices(length):
    fine_pos = np.arange(length)[:, None]
    coarse_pos = np.arange(length // 8)[None, :]
    offsets = np.mod(fine_pos - 8 * coarse_pos, length)
    offsets = np.where(offsets >= length // 2, offsets - length, offsets)
    return tap_weights(offsets)


def z_tables(length):
    coarse = np.arange(length // 8)[None, :]
    main = np.arange(length)[:, None] - 8 * coarse
    prev = np.arange(halo)[:, None] - halo - 8 * coarse
    nxt = np.arange(halo)[:, None] + length - 8 * coarse
    return [tap_weights(o) for o in (main, prev, nxt)]


def filter_kernel(block_count, coarse_block, value_rows, slope_rows):
    def body(x_ref, main_ref, halo_ref, w_ref, ov_ref, os_ref, zv_ref, zs_ref):
        per_step, rows, length = x_ref.shape
        blen = length // block_count
        for b in range(block_count):
            main = x_ref[:, :, b * blen:(b + 1) * blen].reshape(per_step * rows, blen)
            start = (b * blen - halo) % length
            tail = x_ref[:, :, start:start + halo].reshape(per_step * rows, halo)
            start = ((b + 1) * blen) % length
            head = x_ref[:, :, start:start + halo].reshape(per_step * rows, halo)
            edges = jnp.concatenate([tail, head], axis=1)
            acc = jnp.dot(main, main_ref[...], preferred_element_type=jnp.float32)
            acc = acc + jnp.dot(edges, halo_ref[...], preferred_element_type=jnp.float32)
            lanes = slice(b * coarse_block, (b + 1) * coarse_block)
            zv_ref[:, lanes] = acc[:, :coarse_block].astype(jnp.bfloat16)
            zs_ref[:, lanes] = acc[:, coarse_block:].astype(jnp.bfloat16)
        for k in range(per_step):
            zv = zv_ref[k * rows:(k + 1) * rows, :]
            zs = zs_ref[k * rows:(k + 1) * rows, :]
            pv = jnp.dot(w_ref[0, :value_rows, :], zv, preferred_element_type=jnp.float32)
            pv = pv + jnp.dot(w_ref[1, :value_rows, :], zv, preferred_element_type=jnp.float32)
            ps = jnp.dot(w_ref[0, value_rows:, :], zs, preferred_element_type=jnp.float32)
            ps = ps + jnp.dot(w_ref[1, value_rows:, :], zs, preferred_element_type=jnp.float32)
            ov_ref[k] = pv
            os_ref[k] = ps

    return body


def split_hi_lo(w):
    hi = w.astype(jnp.bfloat16)
    lo = (w - hi.astype(jnp.float32)).astype(jnp.bfloat16)
    return jnp.stack([hi, lo], axis=0)


def filtered_partials(fields3, weights):
    field_count, rows, length = fields3.shape
    blen = block_len if (length % block_len == 0 and length > block_len) else length
    block_count = length // blen
    coarse_block = blen // 8
    tables = z_tables(blen)
    joined = [np.concatenate([t[0], t[1]], axis=1) for t in tables]
    main = jnp.asarray(joined[0], jnp.bfloat16)
    halo_w = jnp.asarray(np.concatenate([joined[1], joined[2]], axis=0), jnp.bfloat16)
    w = split_hi_lo(weights)
    total_rows = w.shape[1]
    value_rows = total_rows // 3 * 2
    coarse = length // 8
    per_step = 2 if field_count % 2 == 0 else 1
    const = lambda f: (0, 0)
    return pl.pallas_call(
        filter_kernel(block_count, coarse_block, value_rows, total_rows - value_rows),
        out_shape=[
            jax.ShapeDtypeStruct((field_count, value_rows, coarse), jnp.float32),
            jax.ShapeDtypeStruct((field_count, total_rows - value_rows, coarse), jnp.float32),
        ],
        grid=(field_count // per_step,),
        in_specs=[
            pl.BlockSpec((per_step, rows, length), lambda f: (f, 0, 0)),
            pl.BlockSpec(main.shape, const),
            pl.BlockSpec(halo_w.shape, const),
            pl.BlockSpec(w.shape, lambda f: (0, 0, 0)),
        ],
        out_specs=[
            pl.BlockSpec((per_step, value_rows, coarse), lambda f: (f, 0, 0)),
            pl.BlockSpec((per_step, total_rows - value_rows, coarse), lambda f: (f, 0, 0)),
        ],
        scratch_shapes=[pltpu.VMEM((per_step * rows, coarse), jnp.bfloat16)] * 2,
    )(fields3, main, halo_w, w)


def window_tables(blocks, count, full):
    smooth, deriv = line_matrices(full)
    coarse = full // 8
    out = []
    for at in range(blocks):
        base, width = window(at, count, coarse)
        picks = (base + np.arange(width)) % coarse
        part = slice(at * count, (at + 1) * count)
        out.append(np.stack([smooth[part][:, picks].T, deriv[part][:, picks].T]))
    return np.stack(out)


def pick_kernel(group_steps, step, chunk, owner_len, pack):
    def body(idx_ref, xv_ref, xs_ref, sel_ref, o_ref, tab_ref, buf_ref):
        j = pl.program_id(0)
        fields = xv_ref.shape[0]
        lanes = xv_ref.shape[2]
        width = tab_ref.shape[2]
        per_field = 3 * pack

        @pl.when(j < group_steps)
        def _():
            for t in range(step):
                parts = []
                for k in range(pack):
                    for f in range(fields):
                        at = 2 * (pack * t + k)
                        parts.append(xv_ref[f, at:at + 2, :])
                        parts.append(xs_ref[f, pack * t + k:pack * t + k + 1, :])
                parts.append(jnp.zeros((width - fields * per_field, lanes), xv_ref.dtype))
                slab = jnp.concatenate(parts, axis=0)
                at = pl.multiple_of((j * step + t) * (lanes // 8), lanes // 8)
                tab_ref[pl.ds(at, lanes // 8), :, :] = slab.T.reshape(lanes // 8, 8, width)

        @pl.when(j == group_steps - 1)
        def _():
            tab_ref[tab_ref.shape[0] - 1] = jnp.zeros((8, width), tab_ref.dtype)

        @pl.when(j >= group_steps)
        def _():
            base = (j - group_steps) * chunk

            def eight(i, carry):
                for k in range(8):
                    code = idx_ref[base + i * 8 + k]
                    tile = lax.shift_right_logical(code, 3)
                    row = tab_ref[tile, pl.ds(code & 7, 1), :]
                    buf_ref[i, pl.ds(k, 1), :] = row
                return carry

            lax.fori_loop(0, chunk // 8, eight, 0, unroll=16)
            flipped = buf_ref[...].reshape(chunk, width).T
            sel = sel_ref[...]
            rows = fields * 3
            picked = flipped[:rows]
            for k in range(1, pack):
                picked = jnp.where(sel == k, flipped[k * rows:(k + 1) * rows], picked)
            for owner in range(chunk // owner_len):
                o_ref[owner] = picked[:, owner * owner_len:(owner + 1) * owner_len]

    return body


def pick_cells(xv, xs, flat, sel, owner_len, pack, chunk=4096):
    fields, groups, lanes = xs.shape
    rows = fields * 3
    step = 8
    group_steps = groups // (step * pack)
    entries = flat.shape[0]
    chunk = min(chunk, entries)
    width = -(-(rows * pack) // 128) * 128
    per_chunk = chunk // owner_len
    grid_spec = pltpu.PrefetchScalarGridSpec(
        num_scalar_prefetch=1,
        grid=(group_steps + entries // chunk,),
        in_specs=[
            pl.BlockSpec((fields, 2 * step * pack, lanes), lambda j, idx: (0, jnp.minimum(j, group_steps - 1), 0)),
            pl.BlockSpec((fields, step * pack, lanes), lambda j, idx: (0, jnp.minimum(j, group_steps - 1), 0)),
            pl.BlockSpec((1, chunk), lambda j, idx: (0, jnp.maximum(j - group_steps, 0))),
        ],
        out_specs=pl.BlockSpec((per_chunk, rows, owner_len), lambda j, idx: (jnp.maximum(j - group_steps, 0), 0, 0)),
        scratch_shapes=[pltpu.VMEM((groups // pack * lanes // 8 + 1, 8, width), xs.dtype), pltpu.VMEM((chunk // 8, 8, width), xs.dtype)],
    )
    return pl.pallas_call(
        pick_kernel(group_steps, step, chunk, owner_len, pack),
        out_shape=jax.ShapeDtypeStruct((entries // owner_len, rows, owner_len), xs.dtype),
        grid_spec=grid_spec,
    )(flat, xv, xs, sel)


def model_tensors(coarse):
    values = coarse.astype(jnp.float32)
    points = values.shape[-1]
    values = values.reshape(values.shape[0] // 3, 3, points)
    velocity = values[:3]
    species = values[3:]
    stress = [
        jnp.sum(velocity[first_comp] * velocity[second_comp], axis=0)
        for first_comp, second_comp in upper_pairs
    ]
    species_flux = jnp.sum(species[:, None, :, :] * velocity[None, :, :, :], axis=2)
    joined = jnp.concatenate([jnp.stack(stress, axis=0), species_flux.reshape(-1, points)], axis=0)
    return (model_coeff * joined).astype(jnp.bfloat16)


def window(at, count, coarse):
    reach = (count + 19) // 8 + 4
    if count % 8 or reach >= coarse:
        return 0, coarse
    return at * (count // 8) - 3, reach


def make_shards(row_count, col_count):
    def shards(fields, front_cells):
        field_count, local_x, local_y, z_length = fields.shape
        devices = row_count * col_count
        full_x = local_x * row_count
        full_y = local_y * col_count
        coarse_x = full_x // 8
        coarse_y = full_y // 8
        coarse_z = z_length // 8
        slab = coarse_z // devices
        slots = front_cells.shape[2]
        row = lax.axis_index("rows")
        col = lax.axis_index("cols")
        me = row * col_count + col

        copies = jnp.broadcast_to(front_cells, (devices,) + front_cells.shape[1:])
        every_cell = lax.all_to_all(copies, ("rows", "cols"), split_axis=0, concat_axis=0, tiled=True)

        x_base, x_count = window(row, local_x, coarse_x)
        y_base, y_count = window(col, local_y, coarse_y)
        wx = jnp.asarray(window_tables(row_count, local_x, full_x))[row]
        wy = jnp.asarray(window_tables(col_count, local_y, full_y))[col]
        group = x_count * y_count
        pack = 3
        padded = -(-group // (8 * pack)) * 8 * pack
        xs = jnp.stack([wx[1], wx[0], wx[0]])
        ys = jnp.stack([wy[0], wy[1], wy[0]])
        weights = xs[:, :, None, :, None] * ys[:, None, :, None, :]
        weights = weights.reshape(3, group, local_x * local_y)
        weights = jnp.pad(weights, ((0, 0), (0, padded - group), (0, 0)))
        weights = jnp.concatenate([jnp.transpose(weights[:2], (1, 0, 2)).reshape(2 * padded, -1), weights[2]], axis=0)
        fields3 = fields.reshape(field_count, local_x * local_y, z_length)
        partials = filtered_partials(fields3, weights)

        by_owner = jnp.transpose(every_cell, (1, 0, 2))
        holder = lax.broadcasted_iota(jnp.int32, by_owner.shape, 1)
        clipped = jnp.clip(by_owner, 0, coarse_x * coarse_y * slab - 1)
        cell_pq = clipped // slab
        at_z = holder * slab + clipped % slab
        at_x = (cell_pq // coarse_y - x_base) % coarse_x
        at_y = (cell_pq % coarse_y - y_base) % coarse_y
        inside = (at_x < x_count) & (at_y < y_count) & (by_owner >= 0)
        at_group = at_x * y_count + at_y
        flat = jnp.where(inside, (at_group // pack) * coarse_z + at_z, padded // pack * coarse_z)
        sel = jnp.where(inside, at_group % pack, 0).reshape(1, -1)
        owner_len = devices * slots
        value_part, slope_part = partials
        taken = pick_cells(value_part, slope_part, flat.reshape(-1), sel, owner_len, pack)
        arrived = lax.all_to_all(taken, ("rows", "cols"), split_axis=0, concat_axis=0, tiled=True)
        summed = jnp.sum(arrived, axis=0)
        rounded = lax.reduce_precision(summed, exponent_bits=8, mantissa_bits=7)
        mine = lax.dynamic_index_in_dim(by_owner, me, axis=0, keepdims=False).reshape(-1)
        picked = jnp.where(mine[None, :] >= 0, rounded, jnp.zeros_like(rounded))
        return model_tensors(picked)[None]

    return shards


def solution(mesh):
    in_specs = (P(None, "rows", "cols", None), P(("rows", "cols"), None, None))
    out_specs = P(("rows", "cols"), None, None)
    shards = make_shards(mesh.shape["rows"], mesh.shape["cols"])
    return jax.shard_map(shards, mesh=mesh, in_specs=in_specs, out_specs=out_specs, check_vma=False)
```

```python
import numpy as np
import jax
import jax.numpy as jnp
import ml_dtypes
from jax import lax
from jax.sharding import PartitionSpec as P
from jax.experimental import pallas as pl
from jax.experimental.pallas import tpu as pltpu

first_tap = -20
last_tap = 27
sigma_sq = 256.0 / 12.0
coarse_step = 8.0
model_coeff = 1.0 / 3.0
upper_pairs = ((0, 0), (0, 1), (0, 2), (1, 1), (1, 2), (2, 2))
block_len = 1024
halo = 128


def tap_weights(offsets):
    f32 = np.float32
    every_tap = np.arange(first_tap, last_tap + 1).astype(f32)
    weight_sum = np.sum(np.exp(-(every_tap - f32(3.5)) * (every_tap - f32(3.5)) / f32(2.0 * sigma_sq)), dtype=f32)
    shifted = offsets.astype(f32) - f32(3.5)
    inside = (offsets >= first_tap) & (offsets <= last_tap)
    gauss = np.where(inside, np.exp(-shifted * shifted / f32(2.0 * sigma_sq)), f32(0.0)).astype(f32) / weight_sum
    slope = (f32(-coarse_step) * shifted / f32(sigma_sq) * gauss).astype(f32)
    bf = ml_dtypes.bfloat16
    return gauss.astype(bf).astype(f32), slope.astype(bf).astype(f32)


def line_matrices(length):
    fine_pos = np.arange(length)[:, None]
    coarse_pos = np.arange(length // 8)[None, :]
    offsets = np.mod(fine_pos - 8 * coarse_pos, length)
    offsets = np.where(offsets >= length // 2, offsets - length, offsets)
    return tap_weights(offsets)


def z_tables(length):
    coarse = np.arange(length // 8)[None, :]
    main = np.arange(length)[:, None] - 8 * coarse
    prev = np.arange(halo)[:, None] - halo - 8 * coarse
    nxt = np.arange(halo)[:, None] + length - 8 * coarse
    return [tap_weights(o) for o in (main, prev, nxt)]


def filter_kernel(block_count, coarse_block, value_rows, slope_rows):
    def body(x_ref, main_ref, halo_ref, w_ref, ov_ref, os_ref, zv_ref, zs_ref):
        per_step, rows, length = x_ref.shape
        blen = length // block_count
        for b in range(block_count):
            main = x_ref[:, :, b * blen:(b + 1) * blen].reshape(per_step * rows, blen)
            start = (b * blen - halo) % length
            tail = x_ref[:, :, start:start + halo].reshape(per_step * rows, halo)
            start = ((b + 1) * blen) % length
            head = x_ref[:, :, start:start + halo].reshape(per_step * rows, halo)
            acc = jnp.dot(main, main_ref[...], preferred_element_type=jnp.float32)
            acc = acc + jnp.dot(tail, halo_ref[:halo, :], preferred_element_type=jnp.float32)
            acc = acc + jnp.dot(head, halo_ref[halo:, :], preferred_element_type=jnp.float32)
            lanes = slice(b * coarse_block, (b + 1) * coarse_block)
            zv_ref[:, lanes] = acc[:, :coarse_block].astype(jnp.bfloat16)
            zs_ref[:, lanes] = acc[:, coarse_block:].astype(jnp.bfloat16)
        for k in range(per_step):
            zv = zv_ref[k * rows:(k + 1) * rows, :]
            zs = zs_ref[k * rows:(k + 1) * rows, :]
            pv = jnp.dot(w_ref[0, :value_rows, :], zv, preferred_element_type=jnp.float32)
            pv = pv + jnp.dot(w_ref[1, :value_rows, :], zv, preferred_element_type=jnp.float32)
            ps = jnp.dot(w_ref[0, value_rows:, :], zs, preferred_element_type=jnp.float32)
            ps = ps + jnp.dot(w_ref[1, value_rows:, :], zs, preferred_element_type=jnp.float32)
            ov_ref[k] = pv
            os_ref[k] = ps

    return body


def split_hi_lo(w):
    hi = w.astype(jnp.bfloat16)
    lo = (w - hi.astype(jnp.float32)).astype(jnp.bfloat16)
    return jnp.stack([hi, lo], axis=0)


def filtered_partials(fields3, weights):
    field_count, rows, length = fields3.shape
    blen = block_len if (length % block_len == 0 and length > block_len) else length
    block_count = length // blen
    coarse_block = blen // 8
    tables = z_tables(blen)
    joined = [np.concatenate([t[0], t[1]], axis=1) for t in tables]
    main = jnp.asarray(joined[0], jnp.bfloat16)
    halo_w = jnp.asarray(np.concatenate([joined[1], joined[2]], axis=0), jnp.bfloat16)
    w = split_hi_lo(weights)
    total_rows = w.shape[1]
    value_rows = total_rows // 3 * 2
    coarse = length // 8
    per_step = 3 if field_count % 3 == 0 else 1
    const = lambda f: (0, 0)
    return pl.pallas_call(
        filter_kernel(block_count, coarse_block, value_rows, total_rows - value_rows),
        out_shape=[
            jax.ShapeDtypeStruct((field_count, value_rows, coarse), jnp.float32),
            jax.ShapeDtypeStruct((field_count, total_rows - value_rows, coarse), jnp.float32),
        ],
        grid=(field_count // per_step,),
        in_specs=[
            pl.BlockSpec((per_step, rows, length), lambda f: (f, 0, 0)),
            pl.BlockSpec(main.shape, const),
            pl.BlockSpec(halo_w.shape, const),
            pl.BlockSpec(w.shape, lambda f: (0, 0, 0)),
        ],
        out_specs=[
            pl.BlockSpec((per_step, value_rows, coarse), lambda f: (f, 0, 0)),
            pl.BlockSpec((per_step, total_rows - value_rows, coarse), lambda f: (f, 0, 0)),
        ],
        scratch_shapes=[pltpu.VMEM((per_step * rows, coarse), jnp.bfloat16)] * 2,
    )(fields3, main, halo_w, w)


def window_tables(blocks, count, full):
    smooth, deriv = line_matrices(full)
    coarse = full // 8
    out = []
    for at in range(blocks):
        base, width = window(at, count, coarse)
        picks = (base + np.arange(width)) % coarse
        part = slice(at * count, (at + 1) * count)
        out.append(np.stack([smooth[part][:, picks].T, deriv[part][:, picks].T]))
    return np.stack(out)


def pick_kernel(group_steps, step, chunk, owner_len, pack):
    def body(idx_ref, xv_ref, xs_ref, sel_ref, o_ref, tab_ref, buf_ref):
        j = pl.program_id(0)
        fields = xv_ref.shape[0]
        lanes = xv_ref.shape[2]
        width = tab_ref.shape[2]
        per_field = 3 * pack

        @pl.when(j < group_steps)
        def _():
            for t in range(step):
                parts = []
                for k in range(pack):
                    for f in range(fields):
                        at = 2 * (pack * t + k)
                        parts.append(xv_ref[f, at:at + 2, :])
                        parts.append(xs_ref[f, pack * t + k:pack * t + k + 1, :])
                parts.append(jnp.zeros((width - fields * per_field, lanes), xv_ref.dtype))
                slab = jnp.concatenate(parts, axis=0)
                at = pl.multiple_of((j * step + t) * (lanes // 8), lanes // 8)
                tab_ref[pl.ds(at, lanes // 8), :, :] = slab.T.reshape(lanes // 8, 8, width)

        @pl.when(j == group_steps - 1)
        def _():
            tab_ref[tab_ref.shape[0] - 1] = jnp.zeros((8, width), tab_ref.dtype)

        @pl.when(j >= group_steps)
        def _():
            base = (j - group_steps) * chunk

            def eight(i, carry):
                for k in range(8):
                    code = idx_ref[base + i * 8 + k]
                    tile = lax.shift_right_logical(code, 3)
                    row = tab_ref[tile, pl.ds(code & 7, 1), :]
                    buf_ref[i, pl.ds(k, 1), :] = row
                return carry

            lax.fori_loop(0, chunk // 8, eight, 0, unroll=16)
            flipped = buf_ref[...].reshape(chunk, width).T
            sel = sel_ref[...]
            rows = fields * 3
            picked = flipped[:rows]
            for k in range(1, pack):
                picked = jnp.where(sel == k, flipped[k * rows:(k + 1) * rows], picked)
            for owner in range(chunk // owner_len):
                o_ref[owner] = picked[:, owner * owner_len:(owner + 1) * owner_len]

    return body


def pick_cells(xv, xs, flat, sel, owner_len, pack, chunk=4096):
    fields, groups, lanes = xs.shape
    rows = fields * 3
    step = 8
    group_steps = groups // (step * pack)
    entries = flat.shape[0]
    chunk = min(chunk, entries)
    width = -(-(rows * pack) // 128) * 128
    per_chunk = chunk // owner_len
    grid_spec = pltpu.PrefetchScalarGridSpec(
        num_scalar_prefetch=1,
        grid=(group_steps + entries // chunk,),
        in_specs=[
            pl.BlockSpec((fields, 2 * step * pack, lanes), lambda j, idx: (0, jnp.minimum(j, group_steps - 1), 0)),
            pl.BlockSpec((fields, step * pack, lanes), lambda j, idx: (0, jnp.minimum(j, group_steps - 1), 0)),
            pl.BlockSpec((1, chunk), lambda j, idx: (0, jnp.maximum(j - group_steps, 0))),
        ],
        out_specs=pl.BlockSpec((per_chunk, rows, owner_len), lambda j, idx: (jnp.maximum(j - group_steps, 0), 0, 0)),
        scratch_shapes=[pltpu.VMEM((groups // pack * lanes // 8 + 1, 8, width), xs.dtype), pltpu.VMEM((chunk // 8, 8, width), xs.dtype)],
    )
    return pl.pallas_call(
        pick_kernel(group_steps, step, chunk, owner_len, pack),
        out_shape=jax.ShapeDtypeStruct((entries // owner_len, rows, owner_len), xs.dtype),
        grid_spec=grid_spec,
    )(flat, xv, xs, sel)


def model_tensors(coarse):
    values = coarse.astype(jnp.float32)
    points = values.shape[-1]
    values = values.reshape(values.shape[0] // 3, 3, points)
    velocity = values[:3]
    species = values[3:]
    stress = [
        jnp.sum(velocity[first_comp] * velocity[second_comp], axis=0)
        for first_comp, second_comp in upper_pairs
    ]
    species_flux = jnp.sum(species[:, None, :, :] * velocity[None, :, :, :], axis=2)
    joined = jnp.concatenate([jnp.stack(stress, axis=0), species_flux.reshape(-1, points)], axis=0)
    return (model_coeff * joined).astype(jnp.bfloat16)


def window(at, count, coarse):
    reach = (count + 19) // 8 + 4
    if count % 8 or reach >= coarse:
        return 0, coarse
    return at * (count // 8) - 3, reach


def make_shards(row_count, col_count):
    def shards(fields, front_cells):
        field_count, local_x, local_y, z_length = fields.shape
        devices = row_count * col_count
        full_x = local_x * row_count
        full_y = local_y * col_count
        coarse_x = full_x // 8
        coarse_y = full_y // 8
        coarse_z = z_length // 8
        slab = coarse_z // devices
        slots = front_cells.shape[2]
        row = lax.axis_index("rows")
        col = lax.axis_index("cols")
        me = row * col_count + col

        copies = jnp.broadcast_to(front_cells, (devices,) + front_cells.shape[1:])
        every_cell = lax.all_to_all(copies, ("rows", "cols"), split_axis=0, concat_axis=0, tiled=True)

        x_base, x_count = window(row, local_x, coarse_x)
        y_base, y_count = window(col, local_y, coarse_y)
        wx = jnp.asarray(window_tables(row_count, local_x, full_x))[row]
        wy = jnp.asarray(window_tables(col_count, local_y, full_y))[col]
        group = x_count * y_count
        pack = 3
        padded = -(-group // (8 * pack)) * 8 * pack
        xs = jnp.stack([wx[1], wx[0], wx[0]])
        ys = jnp.stack([wy[0], wy[1], wy[0]])
        weights = xs[:, :, None, :, None] * ys[:, None, :, None, :]
        weights = weights.reshape(3, group, local_x * local_y)
        weights = jnp.pad(weights, ((0, 0), (0, padded - group), (0, 0)))
        weights = jnp.concatenate([jnp.transpose(weights[:2], (1, 0, 2)).reshape(2 * padded, -1), weights[2]], axis=0)
        fields3 = fields.reshape(field_count, local_x * local_y, z_length)
        partials = filtered_partials(fields3, weights)

        by_owner = jnp.transpose(every_cell, (1, 0, 2))
        holder = lax.broadcasted_iota(jnp.int32, by_owner.shape, 1)
        clipped = jnp.clip(by_owner, 0, coarse_x * coarse_y * slab - 1)
        cell_pq = clipped // slab
        at_z = holder * slab + clipped % slab
        at_x = (cell_pq // coarse_y - x_base) % coarse_x
        at_y = (cell_pq % coarse_y - y_base) % coarse_y
        inside = (at_x < x_count) & (at_y < y_count) & (by_owner >= 0)
        at_group = at_x * y_count + at_y
        flat = jnp.where(inside, (at_group // pack) * coarse_z + at_z, padded // pack * coarse_z)
        sel = jnp.where(inside, at_group % pack, 0).reshape(1, -1)
        owner_len = devices * slots
        value_part, slope_part = partials
        taken = pick_cells(value_part, slope_part, flat.reshape(-1), sel, owner_len, pack)
        arrived = lax.all_to_all(taken, ("rows", "cols"), split_axis=0, concat_axis=0, tiled=True)
        summed = jnp.sum(arrived, axis=0)
        rounded = lax.reduce_precision(summed, exponent_bits=8, mantissa_bits=7)
        mine = lax.dynamic_index_in_dim(by_owner, me, axis=0, keepdims=False).reshape(-1)
        picked = jnp.where(mine[None, :] >= 0, rounded, jnp.zeros_like(rounded))
        return model_tensors(picked)[None]

    return shards


def solution(mesh):
    in_specs = (P(None, "rows", "cols", None), P(("rows", "cols"), None, None))
    out_specs = P(("rows", "cols"), None, None)
    shards = make_shards(mesh.shape["rows"], mesh.shape["cols"])
    return jax.shard_map(shards, mesh=mesh, in_specs=in_specs, out_specs=out_specs, check_vma=False)
```

```python
import numpy as np
import jax
import jax.numpy as jnp
import ml_dtypes
from jax import lax
from jax.sharding import PartitionSpec as P
from jax.experimental import pallas as pl
from jax.experimental.pallas import tpu as pltpu

first_tap = -20
last_tap = 27
sigma_sq = 256.0 / 12.0
coarse_step = 8.0
model_coeff = 1.0 / 3.0
upper_pairs = ((0, 0), (0, 1), (0, 2), (1, 1), (1, 2), (2, 2))
block_len = 1024
halo = 128


def tap_weights(offsets):
    f32 = np.float32
    every_tap = np.arange(first_tap, last_tap + 1).astype(f32)
    weight_sum = np.sum(np.exp(-(every_tap - f32(3.5)) * (every_tap - f32(3.5)) / f32(2.0 * sigma_sq)), dtype=f32)
    shifted = offsets.astype(f32) - f32(3.5)
    inside = (offsets >= first_tap) & (offsets <= last_tap)
    gauss = np.where(inside, np.exp(-shifted * shifted / f32(2.0 * sigma_sq)), f32(0.0)).astype(f32) / weight_sum
    slope = (f32(-coarse_step) * shifted / f32(sigma_sq) * gauss).astype(f32)
    bf = ml_dtypes.bfloat16
    return gauss.astype(bf).astype(f32), slope.astype(bf).astype(f32)


def line_matrices(length):
    fine_pos = np.arange(length)[:, None]
    coarse_pos = np.arange(length // 8)[None, :]
    offsets = np.mod(fine_pos - 8 * coarse_pos, length)
    offsets = np.where(offsets >= length // 2, offsets - length, offsets)
    return tap_weights(offsets)


def z_tables(length):
    coarse = np.arange(length // 8)[None, :]
    main = np.arange(length)[:, None] - 8 * coarse
    prev = np.arange(halo)[:, None] - halo - 8 * coarse
    nxt = np.arange(halo)[:, None] + length - 8 * coarse
    return [tap_weights(o) for o in (main, prev, nxt)]


def filter_kernel(block_count, coarse_block, value_rows, slope_rows):
    def body(x_ref, main_ref, halo_ref, w_ref, ov_ref, os_ref, zv_ref, zs_ref):
        per_step, rows, length = x_ref.shape
        blen = length // block_count
        for b in range(block_count):
            main = x_ref[:, :, b * blen:(b + 1) * blen].reshape(per_step * rows, blen)
            start = (b * blen - halo) % length
            tail = x_ref[:, :, start:start + halo].reshape(per_step * rows, halo)
            start = ((b + 1) * blen) % length
            head = x_ref[:, :, start:start + halo].reshape(per_step * rows, halo)
            edges = jnp.concatenate([tail, head], axis=1)
            acc = jnp.dot(main, main_ref[...], preferred_element_type=jnp.float32)
            acc = acc + jnp.dot(edges, halo_ref[...], preferred_element_type=jnp.float32)
            lanes = slice(b * coarse_block, (b + 1) * coarse_block)
            zv_ref[:, lanes] = acc[:, :coarse_block].astype(jnp.bfloat16)
            zs_ref[:, lanes] = acc[:, coarse_block:].astype(jnp.bfloat16)
        for k in range(per_step):
            zv = zv_ref[k * rows:(k + 1) * rows, :]
            zs = zs_ref[k * rows:(k + 1) * rows, :]
            pv = jnp.dot(w_ref[0, :value_rows, :], zv, preferred_element_type=jnp.float32)
            pv = pv + jnp.dot(w_ref[1, :value_rows, :], zv, preferred_element_type=jnp.float32)
            ps = jnp.dot(w_ref[0, value_rows:, :], zs, preferred_element_type=jnp.float32)
            ps = ps + jnp.dot(w_ref[1, value_rows:, :], zs, preferred_element_type=jnp.float32)
            ov_ref[k] = pv
            os_ref[k] = ps

    return body


def split_hi_lo(w):
    hi = w.astype(jnp.bfloat16)
    lo = (w - hi.astype(jnp.float32)).astype(jnp.bfloat16)
    return jnp.stack([hi, lo], axis=0)


def filtered_partials(fields3, weights):
    field_count, rows, length = fields3.shape
    blen = block_len if (length % block_len == 0 and length > block_len) else length
    block_count = length // blen
    coarse_block = blen // 8
    tables = z_tables(blen)
    joined = [np.concatenate([t[0], t[1]], axis=1) for t in tables]
    main = jnp.asarray(joined[0], jnp.bfloat16)
    halo_w = jnp.asarray(np.concatenate([joined[1], joined[2]], axis=0), jnp.bfloat16)
    w = split_hi_lo(weights)
    total_rows = w.shape[1]
    value_rows = total_rows // 3 * 2
    coarse = length // 8
    per_step = 3 if field_count % 3 == 0 else 1
    const = lambda f: (0, 0)
    return pl.pallas_call(
        filter_kernel(block_count, coarse_block, value_rows, total_rows - value_rows),
        out_shape=[
            jax.ShapeDtypeStruct((field_count, value_rows, coarse), jnp.float32),
            jax.ShapeDtypeStruct((field_count, total_rows - value_rows, coarse), jnp.float32),
        ],
        grid=(field_count // per_step,),
        in_specs=[
            pl.BlockSpec((per_step, rows, length), lambda f: (f, 0, 0)),
            pl.BlockSpec(main.shape, const),
            pl.BlockSpec(halo_w.shape, const),
            pl.BlockSpec(w.shape, lambda f: (0, 0, 0)),
        ],
        out_specs=[
            pl.BlockSpec((per_step, value_rows, coarse), lambda f: (f, 0, 0)),
            pl.BlockSpec((per_step, total_rows - value_rows, coarse), lambda f: (f, 0, 0)),
        ],
        scratch_shapes=[pltpu.VMEM((per_step * rows, coarse), jnp.bfloat16)] * 2,
    )(fields3, main, halo_w, w)


def window_tables(blocks, count, full):
    smooth, deriv = line_matrices(full)
    coarse = full // 8
    out = []
    for at in range(blocks):
        base, width = window(at, count, coarse)
        picks = (base + np.arange(width)) % coarse
        part = slice(at * count, (at + 1) * count)
        out.append(np.stack([smooth[part][:, picks].T, deriv[part][:, picks].T]))
    return np.stack(out)


def pick_kernel(group_steps, step, chunk, owner_len, pack):
    def body(idx_ref, xv_ref, xs_ref, sel_ref, o_ref, tab_ref, buf_ref):
        j = pl.program_id(0)
        fields = xv_ref.shape[0]
        lanes = xv_ref.shape[2]
        width = tab_ref.shape[2]
        per_field = 3 * pack

        @pl.when(j < group_steps)
        def _():
            for t in range(step):
                parts = []
                for k in range(pack):
                    for f in range(fields):
                        at = 2 * (pack * t + k)
                        parts.append(xv_ref[f, at:at + 2, :])
                        parts.append(xs_ref[f, pack * t + k:pack * t + k + 1, :])
                parts.append(jnp.zeros((width - fields * per_field, lanes), xv_ref.dtype))
                slab = jnp.concatenate(parts, axis=0)
                at = pl.multiple_of((j * step + t) * (lanes // 8), lanes // 8)
                tab_ref[pl.ds(at, lanes // 8), :, :] = slab.T.reshape(lanes // 8, 8, width)

        @pl.when(j == group_steps - 1)
        def _():
            tab_ref[tab_ref.shape[0] - 1] = jnp.zeros((8, width), tab_ref.dtype)

        @pl.when(j >= group_steps)
        def _():
            base = (j - group_steps) * chunk

            def eight(i, carry):
                for k in range(8):
                    code = idx_ref[base + i * 8 + k]
                    tile = lax.shift_right_logical(code, 3)
                    row = tab_ref[tile, pl.ds(code & 7, 1), :]
                    buf_ref[i, pl.ds(k, 1), :] = row
                return carry

            lax.fori_loop(0, chunk // 8, eight, 0, unroll=16)
            flipped = buf_ref[...].reshape(chunk, width).T
            sel = sel_ref[...]
            rows = fields * 3
            picked = flipped[:rows]
            for k in range(1, pack):
                picked = jnp.where(sel == k, flipped[k * rows:(k + 1) * rows], picked)
            for owner in range(chunk // owner_len):
                o_ref[owner] = picked[:, owner * owner_len:(owner + 1) * owner_len]

    return body


def pick_cells(xv, xs, flat, sel, owner_len, pack, chunk=2048):
    fields, groups, lanes = xs.shape
    rows = fields * 3
    step = 8
    group_steps = groups // (step * pack)
    entries = flat.shape[0]
    chunk = min(chunk, entries)
    width = -(-(rows * pack) // 128) * 128
    per_chunk = chunk // owner_len
    grid_spec = pltpu.PrefetchScalarGridSpec(
        num_scalar_prefetch=1,
        grid=(group_steps + entries // chunk,),
        in_specs=[
            pl.BlockSpec((fields, 2 * step * pack, lanes), lambda j, idx: (0, jnp.minimum(j, group_steps - 1), 0)),
            pl.BlockSpec((fields, step * pack, lanes), lambda j, idx: (0, jnp.minimum(j, group_steps - 1), 0)),
            pl.BlockSpec((1, chunk), lambda j, idx: (0, jnp.maximum(j - group_steps, 0))),
        ],
        out_specs=pl.BlockSpec((per_chunk, rows, owner_len), lambda j, idx: (jnp.maximum(j - group_steps, 0), 0, 0)),
        scratch_shapes=[pltpu.VMEM((groups // pack * lanes // 8 + 1, 8, width), xs.dtype), pltpu.VMEM((chunk // 8, 8, width), xs.dtype)],
    )
    return pl.pallas_call(
        pick_kernel(group_steps, step, chunk, owner_len, pack),
        out_shape=jax.ShapeDtypeStruct((entries // owner_len, rows, owner_len), xs.dtype),
        grid_spec=grid_spec,
    )(flat, xv, xs, sel)


def model_tensors(coarse):
    values = coarse.astype(jnp.float32)
    points = values.shape[-1]
    values = values.reshape(values.shape[0] // 3, 3, points)
    velocity = values[:3]
    species = values[3:]
    stress = [
        jnp.sum(velocity[first_comp] * velocity[second_comp], axis=0)
        for first_comp, second_comp in upper_pairs
    ]
    species_flux = jnp.sum(species[:, None, :, :] * velocity[None, :, :, :], axis=2)
    joined = jnp.concatenate([jnp.stack(stress, axis=0), species_flux.reshape(-1, points)], axis=0)
    return (model_coeff * joined).astype(jnp.bfloat16)


def window(at, count, coarse):
    reach = (count + 19) // 8 + 4
    if count % 8 or reach >= coarse:
        return 0, coarse
    return at * (count // 8) - 3, reach


def make_shards(row_count, col_count):
    def shards(fields, front_cells):
        field_count, local_x, local_y, z_length = fields.shape
        devices = row_count * col_count
        full_x = local_x * row_count
        full_y = local_y * col_count
        coarse_x = full_x // 8
        coarse_y = full_y // 8
        coarse_z = z_length // 8
        slab = coarse_z // devices
        slots = front_cells.shape[2]
        row = lax.axis_index("rows")
        col = lax.axis_index("cols")
        me = row * col_count + col

        copies = jnp.broadcast_to(front_cells, (devices,) + front_cells.shape[1:])
        every_cell = lax.all_to_all(copies, ("rows", "cols"), split_axis=0, concat_axis=0, tiled=True)

        x_base, x_count = window(row, local_x, coarse_x)
        y_base, y_count = window(col, local_y, coarse_y)
        wx = jnp.asarray(window_tables(row_count, local_x, full_x))[row]
        wy = jnp.asarray(window_tables(col_count, local_y, full_y))[col]
        group = x_count * y_count
        pack = 3
        padded = -(-group // (8 * pack)) * 8 * pack
        xs = jnp.stack([wx[1], wx[0], wx[0]])
        ys = jnp.stack([wy[0], wy[1], wy[0]])
        weights = xs[:, :, None, :, None] * ys[:, None, :, None, :]
        weights = weights.reshape(3, group, local_x * local_y)
        weights = jnp.pad(weights, ((0, 0), (0, padded - group), (0, 0)))
        weights = jnp.concatenate([jnp.transpose(weights[:2], (1, 0, 2)).reshape(2 * padded, -1), weights[2]], axis=0)
        fields3 = fields.reshape(field_count, local_x * local_y, z_length)
        partials = filtered_partials(fields3, weights)

        by_owner = jnp.transpose(every_cell, (1, 0, 2))
        holder = lax.broadcasted_iota(jnp.int32, by_owner.shape, 1)
        clipped = jnp.clip(by_owner, 0, coarse_x * coarse_y * slab - 1)
        cell_pq = clipped // slab
        at_z = holder * slab + clipped % slab
        at_x = (cell_pq // coarse_y - x_base) % coarse_x
        at_y = (cell_pq % coarse_y - y_base) % coarse_y
        inside = (at_x < x_count) & (at_y < y_count) & (by_owner >= 0)
        at_group = at_x * y_count + at_y
        flat = jnp.where(inside, (at_group // pack) * coarse_z + at_z, padded // pack * coarse_z)
        sel = jnp.where(inside, at_group % pack, 0).reshape(1, -1)
        owner_len = devices * slots
        value_part, slope_part = partials
        taken = pick_cells(value_part, slope_part, flat.reshape(-1), sel, owner_len, pack)
        arrived = lax.all_to_all(taken, ("rows", "cols"), split_axis=0, concat_axis=0, tiled=True)
        summed = jnp.sum(arrived, axis=0)
        rounded = lax.reduce_precision(summed, exponent_bits=8, mantissa_bits=7)
        mine = lax.dynamic_index_in_dim(by_owner, me, axis=0, keepdims=False).reshape(-1)
        picked = jnp.where(mine[None, :] >= 0, rounded, jnp.zeros_like(rounded))
        return model_tensors(picked)[None]

    return shards


def solution(mesh):
    in_specs = (P(None, "rows", "cols", None), P(("rows", "cols"), None, None))
    out_specs = P(("rows", "cols"), None, None)
    shards = make_shards(mesh.shape["rows"], mesh.shape["cols"])
    return jax.shard_map(shards, mesh=mesh, in_specs=in_specs, out_specs=out_specs, check_vma=False)
```
